512 devices in a mesh: dp: 4 (over z_lo), ctx: 128 (over x, z_hi, y, core).
Axes of the slice: x: 4, y: 4, z: 16 (z_hi: 4, z_lo: 4; z = z_hi * 4 + z_lo), core: 2. Of those that a mesh axis runs over, the one named last changes fastest.
Arguments:
- query_proj: bfloat16 [2048, 65536], P(None, ('dp', 'ctx')), may hold values from -6 to 6
- key_proj: bfloat16 [2048, 65536], P(None, ('dp', 'ctx')), may hold values from -6 to 6
- value_proj: bfloat16 [2048, 65536], P(None, ('dp', 'ctx')), may hold values from -6 to 6
- grad_out: bfloat16 [2048, 65536], P(None, ('dp', 'ctx')), may hold values from -6 to 6
- filters: bfloat16 [128, 16384], P('ctx'), may hold values from -0.046875 to 0.046875
- short_taps: float32 [3, 2048], replicated, may hold values from -3 to 3
Outputs:
- grad_query: bfloat16 [2048, 65536], P(None, ('dp', 'ctx'))
- grad_key: bfloat16 [2048, 65536], P(None, ('dp', 'ctx'))
- grad_value: bfloat16 [2048, 65536], P(None, ('dp', 'ctx'))
- grad_filters: float32 [128, 16384], P('ctx', 'dp')
The draws below stay inside these ranges and needn't reach their ends.
All inputs are finite; a program needn't handle non-finite values.
Results may differ from the reference program's by a relative error of at most 0.0076.
Values may be sent and summed in bfloat16 or wider, within the bound.
No kernel may reach another device: no remote copies, remote signals or barrier semaphores. Data moves between devices by JAX's collectives and lax.ppermute only.
A program may use at most 64 MiB of HBM per device.

```python
import math
import jax
import jax.numpy as jnp
from jax import lax

D = 2048
GSIZE = 16
SHORT = 3
LEN = 16384
SEQ_GRP = 1
GROUPS = 128
TOKENS = 65536
N_DP = 4


def shard_levels(stream_key, shape, split, low, top_value):
    def one(position, parts):
        steps = jax.random.uniform(jax.random.fold_in(jax.random.fold_in(stream_key, 6), position), (parts,), jnp.float32, low / len(split), top_value / len(split))
        return jnp.repeat(jnp.exp(steps), shape[position] // parts).reshape((-1,) + (1,) * (len(shape) - position - 1))

    loudness = one(*split[0])
    for cut in split[1:]:
        loudness = loudness * one(*cut)
    return loudness


def centred(rng, extent, width, bound, cuts=(), held_as=jnp.bfloat16):
    gain = shard_levels(rng, extent, cuts, -0.22, 0.18) if cuts else 1.0
    result = jax.random.normal(rng, extent, jnp.float32) * width * gain
    return jnp.minimum(jnp.maximum(result, -bound), bound).astype(held_as)


def setup_inputs(seed: int = 0) -> dict:
    keys = jax.random.split(jax.random.key(seed), 7)
    query_proj = centred(keys[0], (D, TOKENS), 1.0, 6.0, ((1, 512),))
    key_proj = centred(keys[1], (D, TOKENS), 1.0, 6.0, ((1, 512),))
    value_proj = centred(keys[2], (D, TOKENS), 1.0, 6.0, ((1, 512),))
    grad_out = centred(keys[3], (D, TOKENS), 1.0, 6.0, ((1, 512),))
    filters = centred(keys[4], (GROUPS, LEN), LEN ** -0.5, 0.046875, ((0, 128),))
    short_taps = centred(keys[5], (SHORT, D), 0.6, 3.0, (), jnp.float32)
    return {"query_proj": query_proj, "key_proj": key_proj, "value_proj": value_proj, "grad_out": grad_out, "filters": filters, "short_taps": short_taps}


def settle(value):
    return lax.optimization_barrier(value)

def forward_taps(source, taps):
    count = source.shape[2]
    padded = jnp.pad(source, ((0, 0), (0, 0), (2, 0)))
    return taps[0][:, None, None] * source + taps[1][:, None, None] * padded[:, :, 1:count + 1] + taps[2][:, None, None] * padded[:, :, 0:count]

def backward_taps(source, taps):
    count = source.shape[2]
    padded = jnp.pad(source, ((0, 0), (0, 0), (0, 2)))
    return taps[0][:, None, None] * source + taps[1][:, None, None] * padded[:, :, 1:count + 1] + taps[2][:, None, None] * padded[:, :, 2:count + 2]

def one_group(pieces):
    query_rows, key_rows, value_rows, grad_rows, filter_row, taps = pieces
    seq_count = query_rows.shape[1] // LEN
    shape_three = (GSIZE, seq_count, LEN)
    query_conv = forward_taps(query_rows.astype(jnp.float32).reshape(shape_three), taps).astype(jnp.bfloat16)
    key_conv = forward_taps(key_rows.astype(jnp.float32).reshape(shape_three), taps).astype(jnp.bfloat16)
    value_conv = forward_taps(value_rows.astype(jnp.float32).reshape(shape_three), taps).astype(jnp.bfloat16)
    query_conv, key_conv, value_conv = settle((query_conv, key_conv, value_conv))
    gated = settle((key_conv.astype(jnp.float32) * value_conv.astype(jnp.float32)).astype(jnp.bfloat16))
    padded_len = 2 * LEN
    filter_spec = jnp.fft.rfft(filter_row.astype(jnp.float32), n=padded_len)
    gated_spec = jnp.fft.rfft(gated.astype(jnp.float32), n=padded_len)
    mixed = jnp.fft.irfft(gated_spec * filter_spec, n=padded_len)[..., :LEN].astype(jnp.bfloat16)
    mixed = settle(mixed)
    cotangent = grad_rows.astype(jnp.float32).reshape(shape_three)
    grad_mixed = settle((cotangent * query_conv.astype(jnp.float32)).astype(jnp.bfloat16))
    grad_qconv = (cotangent * mixed.astype(jnp.float32)).astype(jnp.bfloat16)
    grad_spec = jnp.fft.rfft(grad_mixed.astype(jnp.float32), n=padded_len)
    grad_gated = jnp.fft.irfft(grad_spec * jnp.conj(filter_spec), n=padded_len)[..., :LEN].astype(jnp.bfloat16)
    grad_gated = settle(grad_gated)
    filter_sum = jnp.fft.irfft(lax.optimization_barrier(jnp.sum(grad_spec * jnp.conj(gated_spec), axis=(0, 1))), n=padded_len)[:LEN]
    grad_kconv = (grad_gated.astype(jnp.float32) * value_conv.astype(jnp.float32)).astype(jnp.bfloat16)
    grad_vconv = (grad_gated.astype(jnp.float32) * key_conv.astype(jnp.float32)).astype(jnp.bfloat16)
    grad_qconv, grad_kconv, grad_vconv = settle((grad_qconv, grad_kconv, grad_vconv))
    grad_q = backward_taps(grad_qconv.astype(jnp.float32), taps).astype(jnp.bfloat16).reshape(GSIZE, -1)
    grad_k = backward_taps(grad_kconv.astype(jnp.float32), taps).astype(jnp.bfloat16).reshape(GSIZE, -1)
    grad_v = backward_taps(grad_vconv.astype(jnp.float32), taps).astype(jnp.bfloat16).reshape(GSIZE, -1)
    return (grad_q, grad_k, grad_v, filter_sum.astype(jnp.float32))

def reference(query_proj, key_proj, value_proj, grad_out, filters, short_taps):
    group_count = D // GSIZE

    def split_rows(source):
        return source.reshape(group_count, GSIZE, source.shape[1])
    taps = short_taps.reshape(SHORT, group_count, GSIZE).transpose(1, 0, 2)
    grad_q, grad_k, grad_v, filter_sum = lax.map(one_group, (split_rows(query_proj), split_rows(key_proj), split_rows(value_proj), split_rows(grad_out), filters, taps))
    scale = 1.0 / math.sqrt(float(N_DP * SEQ_GRP * GSIZE * LEN))
    return (grad_q.reshape(D, -1), grad_k.reshape(D, -1), grad_v.reshape(D, -1), (filter_sum * scale).astype(jnp.float32))
```

```python
import math

import jax
import jax.numpy as jnp
from jax import lax
from jax.sharding import PartitionSpec as P

highest = lax.Precision.HIGHEST
triple = lax.Precision.HIGH


def shifted(array, axis, by):
    size = lax.axis_size(axis)
    pairs = [(i, i + by) for i in range(size) if 0 <= i + by < size]
    return lax.ppermute(array, axis, pairs)


def ring_scatter_sum(terms, axis):
    count = lax.axis_size(axis)
    width = terms.shape[1] // count
    me = lax.axis_index(axis)
    total = lax.dynamic_slice_in_dim(terms, me * width, width, axis=1)
    for step in range(1, count):
        target = (me + step) % count
        piece = lax.dynamic_slice_in_dim(terms, target * width, width, axis=1)
        pairs = [(i, (i + step) % count) for i in range(count)]
        total = total + lax.ppermute(piece, axis, pairs)
    return total


def angle_table(first_count, second_count, modulus):
    first_index = jnp.arange(first_count, dtype=jnp.int32)
    second_index = jnp.arange(second_count, dtype=jnp.int32)
    product = first_index[:, None] * second_index[None, :] % modulus
    angle = product.astype(jnp.float32) * (2.0 * math.pi / modulus)
    return (jnp.cos(angle), jnp.sin(angle))


def rotation_table(cos_part, sin_part):
    upper = jnp.concatenate([cos_part, -sin_part], axis=1)
    lower = jnp.concatenate([sin_part, cos_part], axis=1)
    return jnp.concatenate([upper, lower], axis=0)


def fourier_tables(length):
    inner = min(128, length)
    outer = 2 * length // inner
    outer_cos, outer_sin = angle_table(outer // 2, outer, outer)
    twist_cos, twist_sin = angle_table(outer, inner, 2 * length)
    inner_cos, inner_sin = angle_table(inner, inner, inner)
    fwd_outer = rotation_table(outer_cos, outer_sin)
    fwd_inner = rotation_table(inner_cos, inner_sin)
    inv_inner = rotation_table(inner_cos, -inner_sin)
    inv_outer = rotation_table(outer_cos.T, -outer_sin.T)
    return (fwd_outer, fwd_inner, inv_inner, inv_outer, twist_cos, twist_sin)


def forward_spectrum(real_rows, imag_rows, tables):
    fwd_outer, fwd_inner, inv_inner, inv_outer, twist_cos, twist_sin = tables
    row_count = real_rows.shape[0]
    outer = twist_cos.shape[0]
    inner = twist_cos.shape[1]
    half_outer = outer // 2
    real_blocks = real_rows.reshape(row_count, half_outer, inner)
    if imag_rows is None:
        blocks = real_blocks
        table = fwd_outer[:half_outer]
    else:
        blocks = jnp.concatenate(
            [real_blocks, imag_rows.reshape(row_count, half_outer, inner)], axis=1
        )
        table = fwd_outer
    first = jnp.einsum("man,ak->mkn", blocks, table, precision=triple)
    first_real = first[:, :outer]
    first_imag = first[:, outer:]
    turned = jnp.concatenate(
        [
            first_real * twist_cos + first_imag * twist_sin,
            first_imag * twist_cos - first_real * twist_sin,
        ],
        axis=2,
    )
    return jnp.einsum("mkn,nj->mkj", turned, fwd_inner, precision=highest)


def inverse_spectrum(spectrum, tables, both_parts):
    fwd_outer, fwd_inner, inv_inner, inv_outer, twist_cos, twist_sin = tables
    row_count = spectrum.shape[0]
    outer = twist_cos.shape[0]
    inner = twist_cos.shape[1]
    half_outer = outer // 2
    length = half_outer * inner
    first = jnp.einsum("mkj,jn->mkn", spectrum, inv_inner, precision=highest)
    first_real = first[..., :inner]
    first_imag = first[..., inner:]
    turned = jnp.concatenate(
        [
            first_real * twist_cos - first_imag * twist_sin,
            first_imag * twist_cos + first_real * twist_sin,
        ],
        axis=1,
    )
    table = inv_outer if both_parts else inv_outer[:, :half_outer]
    values = jnp.einsum("mkn,ka->man", turned, table, precision=highest) * (1.0 / (2.0 * length))
    if both_parts:
        return (
            values[:, :half_outer].reshape(row_count, length),
            values[:, half_outer:].reshape(row_count, length),
        )
    return values.reshape(row_count, length)


def taps_forward(current, earlier, short_taps):
    columns = current.shape[1]
    joined = jnp.concatenate([earlier, current], axis=1)
    return (
        short_taps[0][:, None] * current
        + short_taps[1][:, None] * joined[:, 1 : columns + 1]
        + short_taps[2][:, None] * joined[:, 0:columns]
    )


def taps_backward(current, following, short_taps):
    columns = current.shape[1]
    joined = jnp.concatenate([current, following], axis=1)
    return (
        short_taps[0][:, None] * current
        + short_taps[1][:, None] * joined[:, 1 : columns + 1]
        + short_taps[2][:, None] * joined[:, 2 : columns + 2]
    )


def per_device(query_proj, key_proj, value_proj, grad_out, filters, short_taps):
    all_chans, tok_cols = query_proj.shape
    ctx_count = lax.axis_size("ctx")
    seq_len = tok_cols * ctx_count
    seq_count = ctx_count * tok_cols // seq_len
    groups_dev = filters.shape[0]
    chan_dev = all_chans // ctx_count
    group_size = chan_dev // groups_dev
    group_rows = group_size * seq_count
    pair_rows = group_rows // 2
    position = lax.axis_index("ctx") * tok_cols
    keep_prev = jnp.where(position % seq_len == 0, 0.0, 1.0).astype(jnp.float32)
    keep_next = jnp.where((position + tok_cols) % seq_len == 0, 0.0, 1.0).astype(jnp.float32)
    tables = fourier_tables(seq_len)
    inner = tables[4].shape[1]
    earlier = shifted((query_proj[:, -2:], key_proj[:, -2:], value_proj[:, -2:]), "ctx", 1)
    query_conv = taps_forward(
        query_proj.astype(jnp.float32), earlier[0].astype(jnp.float32) * keep_prev, short_taps
    ).astype(jnp.bfloat16)
    key_conv = taps_forward(
        key_proj.astype(jnp.float32), earlier[1].astype(jnp.float32) * keep_prev, short_taps
    ).astype(jnp.bfloat16)
    value_conv = taps_forward(
        value_proj.astype(jnp.float32), earlier[2].astype(jnp.float32) * keep_prev, short_taps
    ).astype(jnp.bfloat16)
    query_conv, key_conv, value_conv = lax.optimization_barrier((query_conv, key_conv, value_conv))
    gated_tok = (key_conv.astype(jnp.float32) * value_conv.astype(jnp.float32)).astype(jnp.bfloat16)
    filter_spec = forward_spectrum(filters.astype(jnp.float32), None, tables)
    filter_real = filter_spec[:, None, :, :inner]
    filter_imag = filter_spec[:, None, :, inner:]

    def to_rows(source):
        return source.reshape(groups_dev, group_rows, seq_len)

    def to_chan(source):
        return source.reshape(chan_dev, ctx_count * tok_cols)

    def spectrum_of(rows_three):
        paired = rows_three.reshape(groups_dev, pair_rows, 2, seq_len).astype(jnp.float32)
        spec = forward_spectrum(
            paired[:, :, 0].reshape(-1, seq_len), paired[:, :, 1].reshape(-1, seq_len), tables
        )
        spec = spec.reshape((groups_dev, pair_rows) + spec.shape[1:])
        return (spec[..., :inner], spec[..., inner:])

    def back_to_rows(spec_real, spec_imag):
        joined = jnp.concatenate([spec_real, spec_imag], axis=-1)
        joined = joined.reshape((-1,) + joined.shape[2:])
        first_rows, second_rows = inverse_spectrum(joined, tables, True)
        return jnp.stack([first_rows, second_rows], axis=1).reshape(groups_dev, group_rows, seq_len)

    gated_rows = to_rows(lax.all_to_all(gated_tok, "ctx", split_axis=0, concat_axis=1, tiled=True))
    gated_spec = spectrum_of(gated_rows)
    prod_real = gated_spec[0] * filter_real - gated_spec[1] * filter_imag
    prod_imag = gated_spec[0] * filter_imag + gated_spec[1] * filter_real
    mixed_rows = back_to_rows(prod_real, prod_imag).astype(jnp.bfloat16)
    mixed_tok = lax.all_to_all(to_chan(mixed_rows), "ctx", split_axis=1, concat_axis=0, tiled=True)
    cotangent = grad_out.astype(jnp.float32)
    grad_mixed_tok = (cotangent * query_conv.astype(jnp.float32)).astype(jnp.bfloat16)
    grad_qconv = (cotangent * mixed_tok.astype(jnp.float32)).astype(jnp.bfloat16)
    grad_mixed = to_rows(
        lax.all_to_all(grad_mixed_tok, "ctx", split_axis=0, concat_axis=1, tiled=True)
    )
    grad_spec = spectrum_of(grad_mixed)
    prod_real = grad_spec[0] * filter_real + grad_spec[1] * filter_imag
    prod_imag = grad_spec[1] * filter_real - grad_spec[0] * filter_imag
    grad_gated = back_to_rows(prod_real, prod_imag).astype(jnp.bfloat16)
    grad_gated_tok = lax.all_to_all(
        to_chan(grad_gated), "ctx", split_axis=1, concat_axis=0, tiled=True
    )
    cross_real = jnp.sum(grad_spec[0] * gated_spec[0] + grad_spec[1] * gated_spec[1], axis=1)
    cross_imag = jnp.sum(grad_spec[1] * gated_spec[0] - grad_spec[0] * gated_spec[1], axis=1)
    filter_terms = inverse_spectrum(
        jnp.concatenate([cross_real, cross_imag], axis=-1), tables, False
    )
    scale = 1.0 / math.sqrt(float(lax.axis_size("dp") * seq_count * group_size * seq_len))
    grad_filters = ring_scatter_sum(filter_terms, "dp") * scale
    grad_kconv = (grad_gated_tok.astype(jnp.float32) * value_conv.astype(jnp.float32)).astype(
        jnp.bfloat16
    )
    grad_vconv = (grad_gated_tok.astype(jnp.float32) * key_conv.astype(jnp.float32)).astype(
        jnp.bfloat16
    )
    grad_qconv, grad_kconv, grad_vconv = lax.optimization_barrier(
        (grad_qconv, grad_kconv, grad_vconv)
    )
    following = shifted((grad_qconv[:, :2], grad_kconv[:, :2], grad_vconv[:, :2]), "ctx", -1)
    grad_query = taps_backward(
        grad_qconv.astype(jnp.float32), following[0].astype(jnp.float32) * keep_next, short_taps
    ).astype(jnp.bfloat16)
    grad_key = taps_backward(
        grad_kconv.astype(jnp.float32), following[1].astype(jnp.float32) * keep_next, short_taps
    ).astype(jnp.bfloat16)
    grad_value = taps_backward(
        grad_vconv.astype(jnp.float32), following[2].astype(jnp.float32) * keep_next, short_taps
    ).astype(jnp.bfloat16)
    return (grad_query, grad_key, grad_value, grad_filters)


def solution(mesh):
    in_specs = (
        P(None, ("dp", "ctx")),
        P(None, ("dp", "ctx")),
        P(None, ("dp", "ctx")),
        P(None, ("dp", "ctx")),
        P("ctx", None),
        P(),
    )
    out_specs = (
        P(None, ("dp", "ctx")),
        P(None, ("dp", "ctx")),
        P(None, ("dp", "ctx")),
        P("ctx", "dp"),
    )
    return jax.shard_map(
        per_device, mesh=mesh, in_specs=in_specs, out_specs=out_specs, check_vma=False
    )
```

```python
import math

import jax
import jax.numpy as jnp
from jax import lax
from jax.sharding import PartitionSpec as P

highest = lax.Precision.HIGHEST
triple = lax.Precision.HIGH


def shifted(array, axis, by):
    size = lax.axis_size(axis)
    pairs = [(i, i + by) for i in range(size) if 0 <= i + by < size]
    return lax.ppermute(array, axis, pairs)


def ring_scatter_sum(terms, axis):
    count = lax.axis_size(axis)
    width = terms.shape[1] // count
    me = lax.axis_index(axis)
    total = lax.dynamic_slice_in_dim(terms, me * width, width, axis=1)
    for step in range(1, count):
        target = (me + step) % count
        piece = lax.dynamic_slice_in_dim(terms, target * width, width, axis=1)
        pairs = [(i, (i + step) % count) for i in range(count)]
        total = total + lax.ppermute(piece, axis, pairs)
    return total


def angle_table(first_count, second_count, modulus):
    first_index = jnp.arange(first_count, dtype=jnp.int32)
    second_index = jnp.arange(second_count, dtype=jnp.int32)
    product = first_index[:, None] * second_index[None, :] % modulus
    angle = product.astype(jnp.float32) * (2.0 * math.pi / modulus)
    return (jnp.cos(angle), jnp.sin(angle))


def rotation_table(cos_part, sin_part):
    upper = jnp.concatenate([cos_part, -sin_part], axis=1)
    lower = jnp.concatenate([sin_part, cos_part], axis=1)
    return jnp.concatenate([upper, lower], axis=0)


def fourier_tables(length):
    inner = min(128, length)
    outer = 2 * length // inner
    outer_cos, outer_sin = angle_table(outer // 2, outer, outer)
    twist_cos, twist_sin = angle_table(outer, inner, 2 * length)
    inner_cos, inner_sin = angle_table(inner, inner, inner)
    fwd_outer = rotation_table(outer_cos, outer_sin)
    fwd_inner = rotation_table(inner_cos, inner_sin)
    inv_inner = rotation_table(inner_cos, -inner_sin)
    inv_outer = rotation_table(outer_cos.T, -outer_sin.T)
    return (fwd_outer, fwd_inner, inv_inner, inv_outer, twist_cos, twist_sin)


def forward_spectrum(real_rows, imag_rows, tables):
    fwd_outer, fwd_inner, inv_inner, inv_outer, twist_cos, twist_sin = tables
    row_count = real_rows.shape[0]
    outer = twist_cos.shape[0]
    inner = twist_cos.shape[1]
    half_outer = outer // 2
    real_blocks = real_rows.reshape(row_count, half_outer, inner)
    if imag_rows is None:
        blocks = real_blocks
        table = fwd_outer[:half_outer]
    else:
        blocks = jnp.concatenate(
            [real_blocks, imag_rows.reshape(row_count, half_outer, inner)], axis=1
        )
        table = fwd_outer
    first = jnp.einsum("man,ak->mkn", blocks, table, precision=triple)
    first_real = first[:, :outer]
    first_imag = first[:, outer:]
    turned = jnp.concatenate(
        [
            first_real * twist_cos + first_imag * twist_sin,
            first_imag * twist_cos - first_real * twist_sin,
        ],
        axis=2,
    )
    return jnp.einsum("mkn,nj->mkj", turned, fwd_inner, precision=highest)


def inverse_spectrum(spectrum, tables, both_parts):
    fwd_outer, fwd_inner, inv_inner, inv_outer, twist_cos, twist_sin = tables
    row_count = spectrum.shape[0]
    outer = twist_cos.shape[0]
    inner = twist_cos.shape[1]
    half_outer = outer // 2
    length = half_outer * inner
    first = jnp.einsum("mkj,jn->mkn", spectrum, inv_inner, precision=highest)
    first_real = first[..., :inner]
    first_imag = first[..., inner:]
    turned = jnp.concatenate(
        [
            first_real * twist_cos - first_imag * twist_sin,
            first_imag * twist_cos + first_real * twist_sin,
        ],
        axis=1,
    )
    table = inv_outer if both_parts else inv_outer[:, :half_outer]
    values = jnp.einsum("mkn,ka->man", turned, table, precision=highest) * (1.0 / (2.0 * length))
    if both_parts:
        return (
            values[:, :half_outer].reshape(row_count, length),
            values[:, half_outer:].reshape(row_count, length),
        )
    return values.reshape(row_count, length)


def taps_forward(current, earlier, short_taps):
    columns = current.shape[1]
    joined = jnp.concatenate([earlier, current], axis=1)
    return (
        short_taps[0][:, None] * current
        + short_taps[1][:, None] * joined[:, 1 : columns + 1]
        + short_taps[2][:, None] * joined[:, 0:columns]
    )


def taps_backward(current, following, short_taps):
    columns = current.shape[1]
    joined = jnp.concatenate([current, following], axis=1)
    return (
        short_taps[0][:, None] * current
        + short_taps[1][:, None] * joined[:, 1 : columns + 1]
        + short_taps[2][:, None] * joined[:, 2 : columns + 2]
    )


def per_device(query_proj, key_proj, value_proj, grad_out, filters, short_taps):
    all_chans, tok_cols = query_proj.shape
    ctx_count = lax.axis_size("ctx")
    seq_len = tok_cols * ctx_count
    seq_count = ctx_count * tok_cols // seq_len
    groups_dev = filters.shape[0]
    chan_dev = all_chans // ctx_count
    group_size = chan_dev // groups_dev
    group_rows = group_size * seq_count
    pair_rows = group_rows // 2
    position = lax.axis_index("ctx") * tok_cols
    keep_prev = jnp.where(position % seq_len == 0, 0.0, 1.0).astype(jnp.float32)
    keep_next = jnp.where((position + tok_cols) % seq_len == 0, 0.0, 1.0).astype(jnp.float32)
    tables = fourier_tables(seq_len)
    inner = tables[4].shape[1]
    tails = jnp.concatenate([query_proj[:, -2:], key_proj[:, -2:], value_proj[:, -2:]], axis=1)
    tails = shifted(tails, "ctx", 1)
    earlier = (tails[:, 0:2], tails[:, 2:4], tails[:, 4:6])
    query_conv = taps_forward(
        query_proj.astype(jnp.float32), earlier[0].astype(jnp.float32) * keep_prev, short_taps
    ).astype(jnp.bfloat16)
    key_conv = taps_forward(
        key_proj.astype(jnp.float32), earlier[1].astype(jnp.float32) * keep_prev, short_taps
    ).astype(jnp.bfloat16)
    value_conv = taps_forward(
        value_proj.astype(jnp.float32), earlier[2].astype(jnp.float32) * keep_prev, short_taps
    ).astype(jnp.bfloat16)
    query_conv, key_conv, value_conv = lax.optimization_barrier((query_conv, key_conv, value_conv))
    gated_tok = (key_conv.astype(jnp.float32) * value_conv.astype(jnp.float32)).astype(jnp.bfloat16)
    filter_spec = forward_spectrum(filters.astype(jnp.float32), None, tables)
    filter_real = filter_spec[:, None, :, :inner]
    filter_imag = filter_spec[:, None, :, inner:]

    def to_rows(source):
        return source.reshape(groups_dev, group_rows, seq_len)

    def to_chan(source):
        return source.reshape(chan_dev, ctx_count * tok_cols)

    def spectrum_of(rows_three):
        paired = rows_three.reshape(groups_dev, pair_rows, 2, seq_len).astype(jnp.float32)
        spec = forward_spectrum(
            paired[:, :, 0].reshape(-1, seq_len), paired[:, :, 1].reshape(-1, seq_len), tables
        )
        spec = spec.reshape((groups_dev, pair_rows) + spec.shape[1:])
        return (spec[..., :inner], spec[..., inner:])

    def back_to_rows(spec_real, spec_imag):
        joined = jnp.concatenate([spec_real, spec_imag], axis=-1)
        joined = joined.reshape((-1,) + joined.shape[2:])
        first_rows, second_rows = inverse_spectrum(joined, tables, True)
        return jnp.stack([first_rows, second_rows], axis=1).reshape(groups_dev, group_rows, seq_len)

    cotangent = grad_out.astype(jnp.float32)
    grad_mixed_tok = (cotangent * query_conv.astype(jnp.float32)).astype(jnp.bfloat16)
    outgoing = jnp.stack([gated_tok, grad_mixed_tok], axis=0)
    incoming = lax.all_to_all(outgoing, "ctx", split_axis=1, concat_axis=2, tiled=True)
    gated_rows = to_rows(incoming[0])
    grad_mixed = to_rows(incoming[1])
    gated_spec = spectrum_of(gated_rows)
    prod_real = gated_spec[0] * filter_real - gated_spec[1] * filter_imag
    prod_imag = gated_spec[0] * filter_imag + gated_spec[1] * filter_real
    mixed_rows = back_to_rows(prod_real, prod_imag).astype(jnp.bfloat16)
    grad_spec = spectrum_of(grad_mixed)
    prod_real = grad_spec[0] * filter_real + grad_spec[1] * filter_imag
    prod_imag = grad_spec[1] * filter_real - grad_spec[0] * filter_imag
    grad_gated = back_to_rows(prod_real, prod_imag).astype(jnp.bfloat16)
    returning = jnp.stack([to_chan(mixed_rows), to_chan(grad_gated)], axis=0)
    returned = lax.all_to_all(returning, "ctx", split_axis=2, concat_axis=1, tiled=True)
    mixed_tok = returned[0]
    grad_gated_tok = returned[1]
    grad_qconv = (cotangent * mixed_tok.astype(jnp.float32)).astype(jnp.bfloat16)
    cross_real = jnp.sum(grad_spec[0] * gated_spec[0] + grad_spec[1] * gated_spec[1], axis=1)
    cross_imag = jnp.sum(grad_spec[1] * gated_spec[0] - grad_spec[0] * gated_spec[1], axis=1)
    filter_terms = inverse_spectrum(
        jnp.concatenate([cross_real, cross_imag], axis=-1), tables, False
    )
    scale = 1.0 / math.sqrt(float(lax.axis_size("dp") * seq_count * group_size * seq_len))
    grad_filters = ring_scatter_sum(filter_terms, "dp") * scale
    grad_kconv = (grad_gated_tok.astype(jnp.float32) * value_conv.astype(jnp.float32)).astype(
        jnp.bfloat16
    )
    grad_vconv = (grad_gated_tok.astype(jnp.float32) * key_conv.astype(jnp.float32)).astype(
        jnp.bfloat16
    )
    grad_qconv, grad_kconv, grad_vconv = lax.optimization_barrier(
        (grad_qconv, grad_kconv, grad_vconv)
    )
    heads = jnp.concatenate([grad_qconv[:, :2], grad_kconv[:, :2], grad_vconv[:, :2]], axis=1)
    heads = shifted(heads, "ctx", -1)
    following = (heads[:, 0:2], heads[:, 2:4], heads[:, 4:6])
    grad_query = taps_backward(
        grad_qconv.astype(jnp.float32), following[0].astype(jnp.float32) * keep_next, short_taps
    ).astype(jnp.bfloat16)
    grad_key = taps_backward(
        grad_kconv.astype(jnp.float32), following[1].astype(jnp.float32) * keep_next, short_taps
    ).astype(jnp.bfloat16)
    grad_value = taps_backward(
        grad_vconv.astype(jnp.float32), following[2].astype(jnp.float32) * keep_next, short_taps
    ).astype(jnp.bfloat16)
    return (grad_query, grad_key, grad_value, grad_filters)


def solution(mesh):
    in_specs = (
        P(None, ("dp", "ctx")),
        P(None, ("dp", "ctx")),
        P(None, ("dp", "ctx")),
        P(None, ("dp", "ctx")),
        P("ctx", None),
        P(),
    )
    out_specs = (
        P(None, ("dp", "ctx")),
        P(None, ("dp", "ctx")),
        P(None, ("dp", "ctx")),
        P("ctx", "dp"),
    )
    return jax.shard_map(
        per_device, mesh=mesh, in_specs=in_specs, out_specs=out_specs, check_vma=False
    )
```

```python
import math

import jax
import jax.numpy as jnp
from jax import lax
from jax.sharding import PartitionSpec as P

highest = lax.Precision.HIGHEST
triple = lax.Precision.HIGH


def shifted(array, axis, by):
    size = lax.axis_size(axis)
    pairs = [(i, i + by) for i in range(size) if 0 <= i + by < size]
    return lax.ppermute(array, axis, pairs)


def ring_scatter_sum(terms, axis):
    count = lax.axis_size(axis)
    width = terms.shape[1] // count
    me = lax.axis_index(axis)
    total = lax.dynamic_slice_in_dim(terms, me * width, width, axis=1)
    for step in range(1, count):
        target = (me + step) % count
        piece = lax.dynamic_slice_in_dim(terms, target * width, width, axis=1)
        pairs = [(i, (i + step) % count) for i in range(count)]
        total = total + lax.ppermute(piece, axis, pairs)
    return total


def angle_table(first_count, second_count, modulus):
    first_index = jnp.arange(first_count, dtype=jnp.int32)
    second_index = jnp.arange(second_count, dtype=jnp.int32)
    product = first_index[:, None] * second_index[None, :] % modulus
    angle = product.astype(jnp.float32) * (2.0 * math.pi / modulus)
    return (jnp.cos(angle), jnp.sin(angle))


def rotation_table(cos_part, sin_part):
    upper = jnp.concatenate([cos_part, -sin_part], axis=1)
    lower = jnp.concatenate([sin_part, cos_part], axis=1)
    return jnp.concatenate([upper, lower], axis=0)


def fourier_tables(length):
    inner = min(128, length)
    outer = 2 * length // inner
    outer_cos, outer_sin = angle_table(outer // 2, outer, outer)
    twist_cos, twist_sin = angle_table(outer, inner, 2 * length)
    inner_cos, inner_sin = angle_table(inner, inner, inner)
    fwd_outer = rotation_table(outer_cos, outer_sin)
    fwd_inner = rotation_table(inner_cos, inner_sin)
    inv_inner = rotation_table(inner_cos, -inner_sin)
    inv_outer = rotation_table(outer_cos.T, -outer_sin.T)
    return (fwd_outer, fwd_inner, inv_inner, inv_outer, twist_cos, twist_sin)


def forward_spectrum(real_rows, imag_rows, tables):
    fwd_outer, fwd_inner, inv_inner, inv_outer, twist_cos, twist_sin = tables
    row_count = real_rows.shape[0]
    outer = twist_cos.shape[0]
    inner = twist_cos.shape[1]
    half_outer = outer // 2
    real_blocks = real_rows.reshape(row_count, half_outer, inner)
    if imag_rows is None:
        blocks = real_blocks
        table = fwd_outer[:half_outer]
    else:
        blocks = jnp.concatenate(
            [real_blocks, imag_rows.reshape(row_count, half_outer, inner)], axis=1
        )
        table = fwd_outer
    first = jnp.einsum("man,ak->mkn", blocks, table, precision=triple)
    first_real = first[:, :outer]
    first_imag = first[:, outer:]
    turned = jnp.concatenate(
        [
            first_real * twist_cos + first_imag * twist_sin,
            first_imag * twist_cos - first_real * twist_sin,
        ],
        axis=2,
    )
    return jnp.einsum("mkn,nj->mkj", turned, fwd_inner, precision=highest)


def inverse_spectrum(spectrum, tables, both_parts):
    fwd_outer, fwd_inner, inv_inner, inv_outer, twist_cos, twist_sin = tables
    row_count = spectrum.shape[0]
    outer = twist_cos.shape[0]
    inner = twist_cos.shape[1]
    half_outer = outer // 2
    length = half_outer * inner
    first = jnp.einsum("mkj,jn->mkn", spectrum, inv_inner, precision=highest)
    first_real = first[..., :inner]
    first_imag = first[..., inner:]
    turned = jnp.concatenate(
        [
            first_real * twist_cos - first_imag * twist_sin,
            first_imag * twist_cos + first_real * twist_sin,
        ],
        axis=1,
    )
    table = inv_outer if both_parts else inv_outer[:, :half_outer]
    values = jnp.einsum("mkn,ka->man", turned, table, precision=highest) * (1.0 / (2.0 * length))
    if both_parts:
        return (
            values[:, :half_outer].reshape(row_count, length),
            values[:, half_outer:].reshape(row_count, length),
        )
    return values.reshape(row_count, length)


def taps_forward(current, earlier, short_taps):
    columns = current.shape[1]
    joined = jnp.concatenate([earlier, current], axis=1)
    return (
        short_taps[0][:, None] * current
        + short_taps[1][:, None] * joined[:, 1 : columns + 1]
        + short_taps[2][:, None] * joined[:, 0:columns]
    )


def taps_backward(current, following, short_taps):
    columns = current.shape[1]
    joined = jnp.concatenate([current, following], axis=1)
    return (
        short_taps[0][:, None] * current
        + short_taps[1][:, None] * joined[:, 1 : columns + 1]
        + short_taps[2][:, None] * joined[:, 2 : columns + 2]
    )


def per_device(query_proj, key_proj, value_proj, grad_out, filters, short_taps):
    all_chans, tok_cols = query_proj.shape
    ctx_count = lax.axis_size("ctx")
    seq_len = tok_cols * ctx_count
    seq_count = ctx_count * tok_cols // seq_len
    groups_dev = filters.shape[0]
    chan_dev = all_chans // ctx_count
    group_size = chan_dev // groups_dev
    group_rows = group_size * seq_count
    pair_rows = group_rows // 2
    position = lax.axis_index("ctx") * tok_cols
    keep_prev = jnp.where(position % seq_len == 0, 0.0, 1.0).astype(jnp.float32)
    keep_next = jnp.where((position + tok_cols) % seq_len == 0, 0.0, 1.0).astype(jnp.float32)
    tables = fourier_tables(seq_len)
    inner = tables[4].shape[1]
    tails = jnp.concatenate([query_proj[:, -2:], key_proj[:, -2:], value_proj[:, -2:]], axis=1)
    tails = shifted(tails, "ctx", 1)
    earlier = (tails[:, 0:2], tails[:, 2:4], tails[:, 4:6])
    query_conv = taps_forward(
        query_proj.astype(jnp.float32), earlier[0].astype(jnp.float32) * keep_prev, short_taps
    ).astype(jnp.bfloat16)
    key_conv = taps_forward(
        key_proj.astype(jnp.float32), earlier[1].astype(jnp.float32) * keep_prev, short_taps
    ).astype(jnp.bfloat16)
    value_conv = taps_forward(
        value_proj.astype(jnp.float32), earlier[2].astype(jnp.float32) * keep_prev, short_taps
    ).astype(jnp.bfloat16)
    query_conv, key_conv, value_conv = lax.optimization_barrier((query_conv, key_conv, value_conv))
    gated_tok = (key_conv.astype(jnp.float32) * value_conv.astype(jnp.float32)).astype(jnp.bfloat16)
    filter_spec = forward_spectrum(filters.astype(jnp.float32), None, tables)
    filter_real = filter_spec[:, None, :, :inner]
    filter_imag = filter_spec[:, None, :, inner:]

    def to_rows(source):
        return source.reshape(groups_dev, group_rows, seq_len)

    def to_chan(source):
        return source.reshape(chan_dev, ctx_count * tok_cols)

    def spectrum_of(rows_three):
        paired = rows_three.reshape(groups_dev, pair_rows, 2, seq_len).astype(jnp.float32)
        spec = forward_spectrum(
            paired[:, :, 0].reshape(-1, seq_len), paired[:, :, 1].reshape(-1, seq_len), tables
        )
        spec = spec.reshape((groups_dev, pair_rows) + spec.shape[1:])
        return (spec[..., :inner], spec[..., inner:])

    def back_to_rows(spec_real, spec_imag):
        joined = jnp.concatenate([spec_real, spec_imag], axis=-1)
        joined = joined.reshape((-1,) + joined.shape[2:])
        first_rows, second_rows = inverse_spectrum(joined, tables, True)
        return jnp.stack([first_rows, second_rows], axis=1).reshape(groups_dev, group_rows, seq_len)

    cotangent = grad_out.astype(jnp.float32)
    grad_mixed_tok = (cotangent * query_conv.astype(jnp.float32)).astype(jnp.bfloat16)
    outgoing = jnp.concatenate(
        [
            gated_tok.reshape(ctx_count, chan_dev, tok_cols),
            grad_mixed_tok.reshape(ctx_count, chan_dev, tok_cols),
        ],
        axis=1,
    ).reshape(2 * all_chans, tok_cols)
    incoming = lax.all_to_all(outgoing, "ctx", split_axis=0, concat_axis=1, tiled=True)
    gated_rows = to_rows(incoming[:chan_dev])
    grad_mixed = to_rows(incoming[chan_dev:])
    gated_spec = spectrum_of(gated_rows)
    prod_real = gated_spec[0] * filter_real - gated_spec[1] * filter_imag
    prod_imag = gated_spec[0] * filter_imag + gated_spec[1] * filter_real
    mixed_rows = back_to_rows(prod_real, prod_imag).astype(jnp.bfloat16)
    grad_spec = spectrum_of(grad_mixed)
    prod_real = grad_spec[0] * filter_real + grad_spec[1] * filter_imag
    prod_imag = grad_spec[1] * filter_real - grad_spec[0] * filter_imag
    grad_gated = back_to_rows(prod_real, prod_imag).astype(jnp.bfloat16)
    returning = jnp.concatenate([to_chan(mixed_rows), to_chan(grad_gated)], axis=0)
    returned = lax.all_to_all(returning, "ctx", split_axis=1, concat_axis=0, tiled=True)
    returned = returned.reshape(ctx_count, 2 * chan_dev, tok_cols)
    mixed_tok = returned[:, :chan_dev].reshape(all_chans, tok_cols)
    grad_gated_tok = returned[:, chan_dev:].reshape(all_chans, tok_cols)
    grad_qconv = (cotangent * mixed_tok.astype(jnp.float32)).astype(jnp.bfloat16)
    cross_real = jnp.sum(grad_spec[0] * gated_spec[0] + grad_spec[1] * gated_spec[1], axis=1)
    cross_imag = jnp.sum(grad_spec[1] * gated_spec[0] - grad_spec[0] * gated_spec[1], axis=1)
    filter_terms = inverse_spectrum(
        jnp.concatenate([cross_real, cross_imag], axis=-1), tables, False
    )
    scale = 1.0 / math.sqrt(float(lax.axis_size("dp") * seq_count * group_size * seq_len))
    grad_filters = ring_scatter_sum(filter_terms, "dp") * scale
    grad_kconv = (grad_gated_tok.astype(jnp.float32) * value_conv.astype(jnp.float32)).astype(
        jnp.bfloat16
    )
    grad_vconv = (grad_gated_tok.astype(jnp.float32) * key_conv.astype(jnp.float32)).astype(
        jnp.bfloat16
    )
    grad_qconv, grad_kconv, grad_vconv = lax.optimization_barrier(
        (grad_qconv, grad_kconv, grad_vconv)
    )
    heads = jnp.concatenate([grad_qconv[:, :2], grad_kconv[:, :2], grad_vconv[:, :2]], axis=1)
    heads = shifted(heads, "ctx", -1)
    following = (heads[:, 0:2], heads[:, 2:4], heads[:, 4:6])
    grad_query = taps_backward(
        grad_qconv.astype(jnp.float32), following[0].astype(jnp.float32) * keep_next, short_taps
    ).astype(jnp.bfloat16)
    grad_key = taps_backward(
        grad_kconv.astype(jnp.float32), following[1].astype(jnp.float32) * keep_next, short_taps
    ).astype(jnp.bfloat16)
    grad_value = taps_backward(
        grad_vconv.astype(jnp.float32), following[2].astype(jnp.float32) * keep_next, short_taps
    ).astype(jnp.bfloat16)
    return (grad_query, grad_key, grad_value, grad_filters)


def solution(mesh):
    in_specs = (
        P(None, ("dp", "ctx")),
        P(None, ("dp", "ctx")),
        P(None, ("dp", "ctx")),
        P(None, ("dp", "ctx")),
        P("ctx", None),
        P(),
    )
    out_specs = (
        P(None, ("dp", "ctx")),
        P(None, ("dp", "ctx")),
        P(None, ("dp", "ctx")),
        P("ctx", "dp"),
    )
    return jax.shard_map(
        per_device, mesh=mesh, in_specs=in_specs, out_specs=out_specs, check_vma=False
    )
```

```python
import math

import jax
import jax.numpy as jnp
from jax import lax
from jax.sharding import PartitionSpec as P

highest = lax.Precision.HIGH
triple = lax.Precision.HIGH


def shifted(array, axis, by):
    size = lax.axis_size(axis)
    pairs = [(i, i + by) for i in range(size) if 0 <= i + by < size]
    return lax.ppermute(array, axis, pairs)


def ring_scatter_sum(terms, axis):
    count = lax.axis_size(axis)
    width = terms.shape[1] // count
    me = lax.axis_index(axis)
    total = lax.dynamic_slice_in_dim(terms, me * width, width, axis=1)
    for step in range(1, count):
        target = (me + step) % count
        piece = lax.dynamic_slice_in_dim(terms, target * width, width, axis=1)
        pairs = [(i, (i + step) % count) for i in range(count)]
        total = total + lax.ppermute(piece, axis, pairs)
    return total


def angle_table(first_count, second_count, modulus):
    first_index = jnp.arange(first_count, dtype=jnp.int32)
    second_index = jnp.arange(second_count, dtype=jnp.int32)
    product = first_index[:, None] * second_index[None, :] % modulus
    angle = product.astype(jnp.float32) * (2.0 * math.pi / modulus)
    return (jnp.cos(angle), jnp.sin(angle))


def rotation_table(cos_part, sin_part):
    upper = jnp.concatenate([cos_part, -sin_part], axis=1)
    lower = jnp.concatenate([sin_part, cos_part], axis=1)
    return jnp.concatenate([upper, lower], axis=0)


def fourier_tables(length):
    inner = min(128, length)
    outer = 2 * length // inner
    outer_cos, outer_sin = angle_table(outer // 2, outer, outer)
    twist_cos, twist_sin = angle_table(outer, inner, 2 * length)
    inner_cos, inner_sin = angle_table(inner, inner, inner)
    fwd_outer = rotation_table(outer_cos, outer_sin)
    fwd_inner = rotation_table(inner_cos, inner_sin)
    inv_inner = rotation_table(inner_cos, -inner_sin)
    inv_outer = rotation_table(outer_cos.T, -outer_sin.T)
    return (fwd_outer, fwd_inner, inv_inner, inv_outer, twist_cos, twist_sin)


def forward_spectrum(real_rows, imag_rows, tables):
    fwd_outer, fwd_inner, inv_inner, inv_outer, twist_cos, twist_sin = tables
    row_count = real_rows.shape[0]
    outer = twist_cos.shape[0]
    inner = twist_cos.shape[1]
    half_outer = outer // 2
    real_blocks = real_rows.reshape(row_count, half_outer, inner)
    if imag_rows is None:
        blocks = real_blocks
        table = fwd_outer[:half_outer]
    else:
        blocks = jnp.concatenate(
            [real_blocks, imag_rows.reshape(row_count, half_outer, inner)], axis=1
        )
        table = fwd_outer
    first = jnp.einsum("man,ak->mkn", blocks, table, precision=triple)
    first_real = first[:, :outer]
    first_imag = first[:, outer:]
    turned = jnp.concatenate(
        [
            first_real * twist_cos + first_imag * twist_sin,
            first_imag * twist_cos - first_real * twist_sin,
        ],
        axis=2,
    )
    return jnp.einsum("mkn,nj->mkj", turned, fwd_inner, precision=highest)


def inverse_spectrum(spectrum, tables, both_parts):
    fwd_outer, fwd_inner, inv_inner, inv_outer, twist_cos, twist_sin = tables
    row_count = spectrum.shape[0]
    outer = twist_cos.shape[0]
    inner = twist_cos.shape[1]
    half_outer = outer // 2
    length = half_outer * inner
    first = jnp.einsum("mkj,jn->mkn", spectrum, inv_inner, precision=highest)
    first_real = first[..., :inner]
    first_imag = first[..., inner:]
    turned = jnp.concatenate(
        [
            first_real * twist_cos - first_imag * twist_sin,
            first_imag * twist_cos + first_real * twist_sin,
        ],
        axis=1,
    )
    table = inv_outer if both_parts else inv_outer[:, :half_outer]
    values = jnp.einsum("mkn,ka->man", turned, table, precision=highest) * (1.0 / (2.0 * length))
    if both_parts:
        return (
            values[:, :half_outer].reshape(row_count, length),
            values[:, half_outer:].reshape(row_count, length),
        )
    return values.reshape(row_count, length)


def taps_forward(current, earlier, short_taps):
    columns = current.shape[1]
    joined = jnp.concatenate([earlier, current], axis=1)
    return (
        short_taps[0][:, None] * current
        + short_taps[1][:, None] * joined[:, 1 : columns + 1]
        + short_taps[2][:, None] * joined[:, 0:columns]
    )


def taps_backward(current, following, short_taps):
    columns = current.shape[1]
    joined = jnp.concatenate([current, following], axis=1)
    return (
        short_taps[0][:, None] * current
        + short_taps[1][:, None] * joined[:, 1 : columns + 1]
        + short_taps[2][:, None] * joined[:, 2 : columns + 2]
    )


def per_device(query_proj, key_proj, value_proj, grad_out, filters, short_taps):
    all_chans, tok_cols = query_proj.shape
    ctx_count = lax.axis_size("ctx")
    seq_len = tok_cols * ctx_count
    seq_count = ctx_count * tok_cols // seq_len
    groups_dev = filters.shape[0]
    chan_dev = all_chans // ctx_count
    group_size = chan_dev // groups_dev
    group_rows = group_size * seq_count
    pair_rows = group_rows // 2
    position = lax.axis_index("ctx") * tok_cols
    keep_prev = jnp.where(position % seq_len == 0, 0.0, 1.0).astype(jnp.float32)
    keep_next = jnp.where((position + tok_cols) % seq_len == 0, 0.0, 1.0).astype(jnp.float32)
    tables = fourier_tables(seq_len)
    inner = tables[4].shape[1]
    tails = jnp.concatenate([query_proj[:, -2:], key_proj[:, -2:], value_proj[:, -2:]], axis=1)
    tails = shifted(tails, "ctx", 1)
    earlier = (tails[:, 0:2], tails[:, 2:4], tails[:, 4:6])
    query_conv = taps_forward(
        query_proj.astype(jnp.float32), earlier[0].astype(jnp.float32) * keep_prev, short_taps
    ).astype(jnp.bfloat16)
    key_conv = taps_forward(
        key_proj.astype(jnp.float32), earlier[1].astype(jnp.float32) * keep_prev, short_taps
    ).astype(jnp.bfloat16)
    value_conv = taps_forward(
        value_proj.astype(jnp.float32), earlier[2].astype(jnp.float32) * keep_prev, short_taps
    ).astype(jnp.bfloat16)
    query_conv, key_conv, value_conv = lax.optimization_barrier((query_conv, key_conv, value_conv))
    gated_tok = (key_conv.astype(jnp.float32) * value_conv.astype(jnp.float32)).astype(jnp.bfloat16)
    filter_spec = forward_spectrum(filters.astype(jnp.float32), None, tables)
    filter_real = filter_spec[:, None, :, :inner]
    filter_imag = filter_spec[:, None, :, inner:]

    def to_rows(source):
        return source.reshape(groups_dev, group_rows, seq_len)

    def to_chan(source):
        return source.reshape(chan_dev, ctx_count * tok_cols)

    def spectrum_of(rows_three):
        paired = rows_three.reshape(groups_dev, 2, pair_rows, seq_len).astype(jnp.float32)
        spec = forward_spectrum(
            paired[:, 0].reshape(-1, seq_len), paired[:, 1].reshape(-1, seq_len), tables
        )
        spec = spec.reshape((groups_dev, pair_rows) + spec.shape[1:])
        return (spec[..., :inner], spec[..., inner:])

    def back_to_rows(spec_real, spec_imag):
        joined = jnp.concatenate([spec_real, spec_imag], axis=-1)
        joined = joined.reshape((-1,) + joined.shape[2:])
        first_rows, second_rows = inverse_spectrum(joined, tables, True)
        first_rows = first_rows.reshape(groups_dev, pair_rows, seq_len)
        second_rows = second_rows.reshape(groups_dev, pair_rows, seq_len)
        return jnp.concatenate([first_rows, second_rows], axis=1)

    cotangent = grad_out.astype(jnp.float32)
    grad_mixed_tok = (cotangent * query_conv.astype(jnp.float32)).astype(jnp.bfloat16)
    outgoing = jnp.concatenate(
        [
            gated_tok.reshape(ctx_count, chan_dev, tok_cols),
            grad_mixed_tok.reshape(ctx_count, chan_dev, tok_cols),
        ],
        axis=1,
    ).reshape(2 * all_chans, tok_cols)
    incoming = lax.all_to_all(outgoing, "ctx", split_axis=0, concat_axis=1, tiled=True)
    gated_rows = to_rows(incoming[:chan_dev])
    grad_mixed = to_rows(incoming[chan_dev:])
    gated_spec = spectrum_of(gated_rows)
    prod_real = gated_spec[0] * filter_real - gated_spec[1] * filter_imag
    prod_imag = gated_spec[0] * filter_imag + gated_spec[1] * filter_real
    mixed_rows = back_to_rows(prod_real, prod_imag).astype(jnp.bfloat16)
    grad_spec = spectrum_of(grad_mixed)
    prod_real = grad_spec[0] * filter_real + grad_spec[1] * filter_imag
    prod_imag = grad_spec[1] * filter_real - grad_spec[0] * filter_imag
    grad_gated = back_to_rows(prod_real, prod_imag).astype(jnp.bfloat16)
    returning = jnp.concatenate([to_chan(mixed_rows), to_chan(grad_gated)], axis=0)
    returned = lax.all_to_all(returning, "ctx", split_axis=1, concat_axis=0, tiled=True)
    returned = returned.reshape(ctx_count, 2 * chan_dev, tok_cols)
    mixed_tok = returned[:, :chan_dev].reshape(all_chans, tok_cols)
    grad_gated_tok = returned[:, chan_dev:].reshape(all_chans, tok_cols)
    grad_qconv = (cotangent * mixed_tok.astype(jnp.float32)).astype(jnp.bfloat16)
    cross_real = jnp.sum(grad_spec[0] * gated_spec[0] + grad_spec[1] * gated_spec[1], axis=1)
    cross_imag = jnp.sum(grad_spec[1] * gated_spec[0] - grad_spec[0] * gated_spec[1], axis=1)
    filter_terms = inverse_spectrum(
        jnp.concatenate([cross_real, cross_imag], axis=-1), tables, False
    )
    scale = 1.0 / math.sqrt(float(lax.axis_size("dp") * seq_count * group_size * seq_len))
    grad_filters = ring_scatter_sum(filter_terms, "dp") * scale
    grad_kconv = (grad_gated_tok.astype(jnp.float32) * value_conv.astype(jnp.float32)).astype(
        jnp.bfloat16
    )
    grad_vconv = (grad_gated_tok.astype(jnp.float32) * key_conv.astype(jnp.float32)).astype(
        jnp.bfloat16
    )
    grad_qconv, grad_kconv, grad_vconv = lax.optimization_barrier(
        (grad_qconv, grad_kconv, grad_vconv)
    )
    heads = jnp.concatenate([grad_qconv[:, :2], grad_kconv[:, :2], grad_vconv[:, :2]], axis=1)
    heads = shifted(heads, "ctx", -1)
    following = (heads[:, 0:2], heads[:, 2:4], heads[:, 4:6])
    grad_query = taps_backward(
        grad_qconv.astype(jnp.float32), following[0].astype(jnp.float32) * keep_next, short_taps
    ).astype(jnp.bfloat16)
    grad_key = taps_backward(
        grad_kconv.astype(jnp.float32), following[1].astype(jnp.float32) * keep_next, short_taps
    ).astype(jnp.bfloat16)
    grad_value = taps_backward(
        grad_vconv.astype(jnp.float32), following[2].astype(jnp.float32) * keep_next, short_taps
    ).astype(jnp.bfloat16)
    return (grad_query, grad_key, grad_value, grad_filters)


def solution(mesh):
    in_specs = (
        P(None, ("dp", "ctx")),
        P(None, ("dp", "ctx")),
        P(None, ("dp", "ctx")),
        P(None, ("dp", "ctx")),
        P("ctx", None),
        P(),
    )
    out_specs = (
        P(None, ("dp", "ctx")),
        P(None, ("dp", "ctx")),
        P(None, ("dp", "ctx")),
        P("ctx", "dp"),
    )
    return jax.shard_map(
        per_device, mesh=mesh, in_specs=in_specs, out_specs=out_specs, check_vma=False
    )
```

```python
import functools
import math

import jax
import jax.numpy as jnp
from jax import lax
from jax.experimental import pallas as pl
from jax.experimental.pallas import tpu as pltpu
from jax.sharding import PartitionSpec as P

highest = lax.Precision.HIGH
triple = lax.Precision.HIGH


def shifted(array, axis, by):
    size = lax.axis_size(axis)
    pairs = [(i, i + by) for i in range(size) if 0 <= i + by < size]
    return lax.ppermute(array, axis, pairs)


def ring_scatter_sum(terms, axis):
    count = lax.axis_size(axis)
    width = terms.shape[1] // count
    me = lax.axis_index(axis)
    total = lax.dynamic_slice_in_dim(terms, me * width, width, axis=1)
    for step in range(1, count):
        target = (me + step) % count
        piece = lax.dynamic_slice_in_dim(terms, target * width, width, axis=1)
        pairs = [(i, (i + step) % count) for i in range(count)]
        total = total + lax.ppermute(piece, axis, pairs)
    return total


def angle_table(first_count, second_count, modulus):
    first_index = jnp.arange(first_count, dtype=jnp.int32)
    second_index = jnp.arange(second_count, dtype=jnp.int32)
    product = first_index[:, None] * second_index[None, :] % modulus
    angle = product.astype(jnp.float32) * (2.0 * math.pi / modulus)
    return (jnp.cos(angle), jnp.sin(angle))


def rotation_table(cos_part, sin_part):
    upper = jnp.concatenate([cos_part, -sin_part], axis=1)
    lower = jnp.concatenate([sin_part, cos_part], axis=1)
    return jnp.concatenate([upper, lower], axis=0)


def fourier_tables(length):
    inner = min(128, length)
    outer = 2 * length // inner
    outer_cos, outer_sin = angle_table(outer // 2, outer, outer)
    twist_cos, twist_sin = angle_table(outer, inner, 2 * length)
    inner_cos, inner_sin = angle_table(inner, inner, inner)
    fwd_outer = rotation_table(outer_cos, outer_sin)
    fwd_inner = rotation_table(inner_cos, inner_sin)
    inv_inner = rotation_table(inner_cos, -inner_sin)
    inv_outer = rotation_table(outer_cos.T, -outer_sin.T)
    return (fwd_outer, fwd_inner, inv_inner, inv_outer, twist_cos, twist_sin)


def forward_spectrum(real_rows, imag_rows, tables):
    fwd_outer, fwd_inner, inv_inner, inv_outer, twist_cos, twist_sin = tables
    row_count = real_rows.shape[0]
    outer = twist_cos.shape[0]
    inner = twist_cos.shape[1]
    half_outer = outer // 2
    real_blocks = real_rows.reshape(row_count, half_outer, inner)
    if imag_rows is None:
        blocks = real_blocks
        table = fwd_outer[:half_outer]
    else:
        blocks = jnp.concatenate(
            [real_blocks, imag_rows.reshape(row_count, half_outer, inner)], axis=1
        )
        table = fwd_outer
    first = jnp.einsum("man,ak->mkn", blocks, table, precision=triple)
    first_real = first[:, :outer]
    first_imag = first[:, outer:]
    turned = jnp.concatenate(
        [
            first_real * twist_cos + first_imag * twist_sin,
            first_imag * twist_cos - first_real * twist_sin,
        ],
        axis=2,
    )
    return jnp.einsum("mkn,nj->mkj", turned, fwd_inner, precision=highest)


def inverse_spectrum(spectrum, tables, both_parts):
    fwd_outer, fwd_inner, inv_inner, inv_outer, twist_cos, twist_sin = tables
    row_count = spectrum.shape[0]
    outer = twist_cos.shape[0]
    inner = twist_cos.shape[1]
    half_outer = outer // 2
    length = half_outer * inner
    first = jnp.einsum("mkj,jn->mkn", spectrum, inv_inner, precision=highest)
    first_real = first[..., :inner]
    first_imag = first[..., inner:]
    turned = jnp.concatenate(
        [
            first_real * twist_cos - first_imag * twist_sin,
            first_imag * twist_cos + first_real * twist_sin,
        ],
        axis=1,
    )
    table = inv_outer if both_parts else inv_outer[:, :half_outer]
    values = jnp.einsum("mkn,ka->man", turned, table, precision=highest) * (1.0 / (2.0 * length))
    if both_parts:
        return (
            values[:, :half_outer].reshape(row_count, length),
            values[:, half_outer:].reshape(row_count, length),
        )
    return values.reshape(row_count, length)


BLOCK_ROWS = 256


def front_kernel(chan_dev, q_ref, k_ref, v_ref, g_ref, halo_ref, taps_ref, qc_ref, kc_ref, vc_ref, out_ref):
    rows, cols = q_ref.shape
    lane = lax.broadcasted_iota(jnp.int32, (rows, cols), 1)
    halo = halo_ref[...].astype(jnp.float32)
    taps = taps_ref[...]
    first, second, third = taps[:, 0:1], taps[:, 1:2], taps[:, 2:3]

    def conv(x_ref, slot):
        x = x_ref[...].astype(jnp.float32)
        older = halo[:, 2 * slot : 2 * slot + 1]
        newer = halo[:, 2 * slot + 1 : 2 * slot + 2]
        back_one = jnp.where(lane == 0, newer, pltpu.roll(x, 1, 1))
        rolled = pltpu.roll(x, 2, 1)
        back_two = jnp.where(lane == 0, older, jnp.where(lane == 1, newer, rolled))
        return (first * x + second * back_one + third * back_two).astype(jnp.bfloat16)

    qc = conv(q_ref, 0)
    kc = conv(k_ref, 1)
    vc = conv(v_ref, 2)
    qc_ref[...] = qc
    kc_ref[...] = kc
    vc_ref[...] = vc
    gated = (kc.astype(jnp.float32) * vc.astype(jnp.float32)).astype(jnp.bfloat16)
    grad_mixed = (g_ref[...].astype(jnp.float32) * qc.astype(jnp.float32)).astype(jnp.bfloat16)
    for j in range(rows // chan_dev):
        out_ref[2 * j * chan_dev : (2 * j + 1) * chan_dev, :] = gated[j * chan_dev : (j + 1) * chan_dev]
        out_ref[(2 * j + 1) * chan_dev : (2 * j + 2) * chan_dev, :] = grad_mixed[
            j * chan_dev : (j + 1) * chan_dev
        ]


def front(query_proj, key_proj, value_proj, grad_out, halo, taps_cols, chan_dev):
    all_chans, tok_cols = query_proj.shape
    block = min(BLOCK_ROWS, all_chans)
    tile = pl.BlockSpec((block, tok_cols), lambda i: (i, 0))
    return pl.pallas_call(
        functools.partial(front_kernel, chan_dev),
        grid=(all_chans // block,),
        in_specs=[tile, tile, tile, tile, pl.BlockSpec((block, 6), lambda i: (i, 0)),
                  pl.BlockSpec((block, 3), lambda i: (i, 0))],
        out_specs=[tile, tile, tile, pl.BlockSpec((2 * block, tok_cols), lambda i: (i, 0))],
        out_shape=[jax.ShapeDtypeStruct((all_chans, tok_cols), jnp.bfloat16)] * 3
        + [jax.ShapeDtypeStruct((2 * all_chans, tok_cols), jnp.bfloat16)],
        cost_estimate=pl.CostEstimate(flops=30 * all_chans * tok_cols, transcendentals=0,
                                      bytes_accessed=18 * all_chans * tok_cols),
    )(query_proj, key_proj, value_proj, grad_out, halo, taps_cols)


def taps_forward(current, earlier, short_taps):
    columns = current.shape[1]
    joined = jnp.concatenate([earlier, current], axis=1)
    return (
        short_taps[0][:, None] * current
        + short_taps[1][:, None] * joined[:, 1 : columns + 1]
        + short_taps[2][:, None] * joined[:, 0:columns]
    )


def taps_backward(current, following, short_taps):
    columns = current.shape[1]
    joined = jnp.concatenate([current, following], axis=1)
    return (
        short_taps[0][:, None] * current
        + short_taps[1][:, None] * joined[:, 1 : columns + 1]
        + short_taps[2][:, None] * joined[:, 2 : columns + 2]
    )


def per_device(query_proj, key_proj, value_proj, grad_out, filters, short_taps):
    all_chans, tok_cols = query_proj.shape
    ctx_count = lax.axis_size("ctx")
    seq_len = tok_cols * ctx_count
    seq_count = ctx_count * tok_cols // seq_len
    groups_dev = filters.shape[0]
    chan_dev = all_chans // ctx_count
    group_size = chan_dev // groups_dev
    group_rows = group_size * seq_count
    pair_rows = group_rows // 2
    position = lax.axis_index("ctx") * tok_cols
    keep_prev = jnp.where(position % seq_len == 0, 0.0, 1.0).astype(jnp.float32)
    keep_next = jnp.where((position + tok_cols) % seq_len == 0, 0.0, 1.0).astype(jnp.float32)
    tables = fourier_tables(seq_len)
    inner = tables[4].shape[1]
    tails = jnp.concatenate([query_proj[:, -2:], key_proj[:, -2:], value_proj[:, -2:]], axis=1)
    tails = shifted(tails, "ctx", 1)
    halo = jnp.where(keep_prev > 0, tails, jnp.zeros_like(tails))
    query_conv, key_conv, value_conv, outgoing = front(
        query_proj, key_proj, value_proj, grad_out, halo, short_taps.T, chan_dev
    )
    filter_spec = forward_spectrum(filters.astype(jnp.float32), None, tables)
    filter_real = filter_spec[:, None, :, :inner]
    filter_imag = filter_spec[:, None, :, inner:]

    def to_rows(source):
        return source.reshape(groups_dev, group_rows, seq_len)

    def to_chan(source):
        return source.reshape(chan_dev, ctx_count * tok_cols)

    def spectrum_of(rows_three):
        paired = rows_three.reshape(groups_dev, 2, pair_rows, seq_len).astype(jnp.float32)
        spec = forward_spectrum(
            paired[:, 0].reshape(-1, seq_len), paired[:, 1].reshape(-1, seq_len), tables
        )
        spec = spec.reshape((groups_dev, pair_rows) + spec.shape[1:])
        return (spec[..., :inner], spec[..., inner:])

    def back_to_rows(spec_real, spec_imag):
        joined = jnp.concatenate([spec_real, spec_imag], axis=-1)
        joined = joined.reshape((-1,) + joined.shape[2:])
        first_rows, second_rows = inverse_spectrum(joined, tables, True)
        first_rows = first_rows.reshape(groups_dev, pair_rows, seq_len)
        second_rows = second_rows.reshape(groups_dev, pair_rows, seq_len)
        return jnp.concatenate([first_rows, second_rows], axis=1)

    cotangent = grad_out.astype(jnp.float32)
    incoming = lax.all_to_all(outgoing, "ctx", split_axis=0, concat_axis=1, tiled=True)
    gated_rows = to_rows(incoming[:chan_dev])
    grad_mixed = to_rows(incoming[chan_dev:])
    gated_spec = spectrum_of(gated_rows)
    prod_real = gated_spec[0] * filter_real - gated_spec[1] * filter_imag
    prod_imag = gated_spec[0] * filter_imag + gated_spec[1] * filter_real
    mixed_rows = back_to_rows(prod_real, prod_imag).astype(jnp.bfloat16)
    grad_spec = spectrum_of(grad_mixed)
    prod_real = grad_spec[0] * filter_real + grad_spec[1] * filter_imag
    prod_imag = grad_spec[1] * filter_real - grad_spec[0] * filter_imag
    grad_gated = back_to_rows(prod_real, prod_imag).astype(jnp.bfloat16)
    returning = jnp.concatenate([to_chan(mixed_rows), to_chan(grad_gated)], axis=0)
    returned = lax.all_to_all(returning, "ctx", split_axis=1, concat_axis=0, tiled=True)
    returned = returned.reshape(ctx_count, 2 * chan_dev, tok_cols)
    mixed_tok = returned[:, :chan_dev].reshape(all_chans, tok_cols)
    grad_gated_tok = returned[:, chan_dev:].reshape(all_chans, tok_cols)
    grad_qconv = (cotangent * mixed_tok.astype(jnp.float32)).astype(jnp.bfloat16)
    cross_real = jnp.sum(grad_spec[0] * gated_spec[0] + grad_spec[1] * gated_spec[1], axis=1)
    cross_imag = jnp.sum(grad_spec[1] * gated_spec[0] - grad_spec[0] * gated_spec[1], axis=1)
    filter_terms = inverse_spectrum(
        jnp.concatenate([cross_real, cross_imag], axis=-1), tables, False
    )
    scale = 1.0 / math.sqrt(float(lax.axis_size("dp") * seq_count * group_size * seq_len))
    grad_filters = ring_scatter_sum(filter_terms, "dp") * scale
    grad_kconv = (grad_gated_tok.astype(jnp.float32) * value_conv.astype(jnp.float32)).astype(
        jnp.bfloat16
    )
    grad_vconv = (grad_gated_tok.astype(jnp.float32) * key_conv.astype(jnp.float32)).astype(
        jnp.bfloat16
    )
    grad_qconv, grad_kconv, grad_vconv = lax.optimization_barrier(
        (grad_qconv, grad_kconv, grad_vconv)
    )
    heads = jnp.concatenate([grad_qconv[:, :2], grad_kconv[:, :2], grad_vconv[:, :2]], axis=1)
    heads = shifted(heads, "ctx", -1)
    following = (heads[:, 0:2], heads[:, 2:4], heads[:, 4:6])
    grad_query = taps_backward(
        grad_qconv.astype(jnp.float32), following[0].astype(jnp.float32) * keep_next, short_taps
    ).astype(jnp.bfloat16)
    grad_key = taps_backward(
        grad_kconv.astype(jnp.float32), following[1].astype(jnp.float32) * keep_next, short_taps
    ).astype(jnp.bfloat16)
    grad_value = taps_backward(
        grad_vconv.astype(jnp.float32), following[2].astype(jnp.float32) * keep_next, short_taps
    ).astype(jnp.bfloat16)
    return (grad_query, grad_key, grad_value, grad_filters)


def solution(mesh):
    in_specs = (
        P(None, ("dp", "ctx")),
        P(None, ("dp", "ctx")),
        P(None, ("dp", "ctx")),
        P(None, ("dp", "ctx")),
        P("ctx", None),
        P(),
    )
    out_specs = (
        P(None, ("dp", "ctx")),
        P(None, ("dp", "ctx")),
        P(None, ("dp", "ctx")),
        P("ctx", "dp"),
    )
    return jax.shard_map(
        per_device, mesh=mesh, in_specs=in_specs, out_specs=out_specs, check_vma=False
    )
```

```python
import functools
import math

import jax
import jax.numpy as jnp
from jax import lax
from jax.experimental import pallas as pl
from jax.experimental.pallas import tpu as pltpu
from jax.sharding import PartitionSpec as P

highest = lax.Precision.HIGH
triple = lax.Precision.HIGH


def shifted(array, axis, by):
    size = lax.axis_size(axis)
    pairs = [(i, i + by) for i in range(size) if 0 <= i + by < size]
    return lax.ppermute(array, axis, pairs)


def ring_scatter_sum(terms, axis):
    count = lax.axis_size(axis)
    me = lax.axis_index(axis)
    total = terms
    span = count
    while span > 1:
        span //= 2
        width = total.shape[1] // 2
        upper = (me // span) % 2
        keep = lax.dynamic_slice_in_dim(total, upper * width, width, axis=1)
        give = lax.dynamic_slice_in_dim(total, (1 - upper) * width, width, axis=1)
        pairs = [(i, i ^ span) for i in range(count)]
        total = keep + lax.ppermute(give, axis, pairs)
    return total


def angle_table(first_count, second_count, modulus):
    first_index = jnp.arange(first_count, dtype=jnp.int32)
    second_index = jnp.arange(second_count, dtype=jnp.int32)
    product = first_index[:, None] * second_index[None, :] % modulus
    angle = product.astype(jnp.float32) * (2.0 * math.pi / modulus)
    return (jnp.cos(angle), jnp.sin(angle))


def rotation_table(cos_part, sin_part):
    upper = jnp.concatenate([cos_part, -sin_part], axis=1)
    lower = jnp.concatenate([sin_part, cos_part], axis=1)
    return jnp.concatenate([upper, lower], axis=0)


def fourier_tables(length):
    inner = min(128, length)
    outer = 2 * length // inner
    outer_cos, outer_sin = angle_table(outer // 2, outer, outer)
    twist_cos, twist_sin = angle_table(outer, inner, 2 * length)
    inner_cos, inner_sin = angle_table(inner, inner, inner)
    fwd_outer = rotation_table(outer_cos, outer_sin)
    fwd_inner = rotation_table(inner_cos, inner_sin)
    inv_inner = rotation_table(inner_cos, -inner_sin)
    inv_outer = rotation_table(outer_cos.T, -outer_sin.T)
    return (fwd_outer, fwd_inner, inv_inner, inv_outer, twist_cos, twist_sin)


def forward_spectrum(real_rows, imag_rows, tables):
    fwd_outer, fwd_inner, inv_inner, inv_outer, twist_cos, twist_sin = tables
    row_count = real_rows.shape[0]
    outer = twist_cos.shape[0]
    inner = twist_cos.shape[1]
    half_outer = outer // 2
    real_blocks = real_rows.reshape(row_count, half_outer, inner)
    if imag_rows is None:
        blocks = real_blocks
        table = fwd_outer[:half_outer]
    else:
        blocks = jnp.concatenate(
            [real_blocks, imag_rows.reshape(row_count, half_outer, inner)], axis=1
        )
        table = fwd_outer
    first = jnp.einsum("man,ak->mkn", blocks, table, precision=triple)
    first_real = first[:, :outer]
    first_imag = first[:, outer:]
    turned = jnp.concatenate(
        [
            first_real * twist_cos + first_imag * twist_sin,
            first_imag * twist_cos - first_real * twist_sin,
        ],
        axis=2,
    )
    return jnp.einsum("mkn,nj->mkj", turned, fwd_inner, precision=highest)


def inverse_spectrum(spectrum, tables, both_parts):
    fwd_outer, fwd_inner, inv_inner, inv_outer, twist_cos, twist_sin = tables
    row_count = spectrum.shape[0]
    outer = twist_cos.shape[0]
    inner = twist_cos.shape[1]
    half_outer = outer // 2
    length = half_outer * inner
    first = jnp.einsum("mkj,jn->mkn", spectrum, inv_inner, precision=highest)
    first_real = first[..., :inner]
    first_imag = first[..., inner:]
    turned = jnp.concatenate(
        [
            first_real * twist_cos - first_imag * twist_sin,
            first_imag * twist_cos + first_real * twist_sin,
        ],
        axis=1,
    )
    table = inv_outer if both_parts else inv_outer[:, :half_outer]
    values = jnp.einsum("mkn,ka->man", turned, table, precision=highest) * (1.0 / (2.0 * length))
    if both_parts:
        return (
            values[:, :half_outer].reshape(row_count, length),
            values[:, half_outer:].reshape(row_count, length),
        )
    return values.reshape(row_count, length)


BLOCK_ROWS = 1024


def front_kernel(chan_dev, q_ref, k_ref, v_ref, g_ref, halo_ref, taps_ref, qc_ref, kc_ref, vc_ref, out_ref):
    rows, cols = q_ref.shape
    lane = lax.broadcasted_iota(jnp.int32, (rows, cols), 1)
    halo = halo_ref[...].astype(jnp.float32)
    taps = taps_ref[...]
    first, second, third = taps[:, 0:1], taps[:, 1:2], taps[:, 2:3]

    def conv(x_ref, slot):
        x = x_ref[...].astype(jnp.float32)
        older = halo[:, 2 * slot : 2 * slot + 1]
        newer = halo[:, 2 * slot + 1 : 2 * slot + 2]
        back_one = jnp.where(lane == 0, newer, pltpu.roll(x, 1, 1))
        rolled = pltpu.roll(x, 2, 1)
        back_two = jnp.where(lane == 0, older, jnp.where(lane == 1, newer, rolled))
        return (first * x + second * back_one + third * back_two).astype(jnp.bfloat16)

    qc = conv(q_ref, 0)
    kc = conv(k_ref, 1)
    vc = conv(v_ref, 2)
    qc_ref[...] = qc
    kc_ref[...] = kc
    vc_ref[...] = vc
    gated = (kc.astype(jnp.float32) * vc.astype(jnp.float32)).astype(jnp.bfloat16)
    grad_mixed = (g_ref[...].astype(jnp.float32) * qc.astype(jnp.float32)).astype(jnp.bfloat16)
    for j in range(rows // chan_dev):
        out_ref[2 * j * chan_dev : (2 * j + 1) * chan_dev, :] = gated[j * chan_dev : (j + 1) * chan_dev]
        out_ref[(2 * j + 1) * chan_dev : (2 * j + 2) * chan_dev, :] = grad_mixed[
            j * chan_dev : (j + 1) * chan_dev
        ]


def front(query_proj, key_proj, value_proj, grad_out, halo, taps_cols, chan_dev):
    all_chans, tok_cols = query_proj.shape
    block = min(BLOCK_ROWS, all_chans)
    tile = pl.BlockSpec((block, tok_cols), lambda i: (i, 0))
    return pl.pallas_call(
        functools.partial(front_kernel, chan_dev),
        grid=(all_chans // block,),
        in_specs=[tile, tile, tile, tile, pl.BlockSpec((block, 6), lambda i: (i, 0)),
                  pl.BlockSpec((block, 3), lambda i: (i, 0))],
        out_specs=[tile, tile, tile, pl.BlockSpec((2 * block, tok_cols), lambda i: (i, 0))],
        out_shape=[jax.ShapeDtypeStruct((all_chans, tok_cols), jnp.bfloat16)] * 3
        + [jax.ShapeDtypeStruct((2 * all_chans, tok_cols), jnp.bfloat16)],
        cost_estimate=pl.CostEstimate(flops=30 * all_chans * tok_cols, transcendentals=0,
                                      bytes_accessed=18 * all_chans * tok_cols),
    )(query_proj, key_proj, value_proj, grad_out, halo, taps_cols)


def taps_forward(current, earlier, short_taps):
    columns = current.shape[1]
    joined = jnp.concatenate([earlier, current], axis=1)
    return (
        short_taps[0][:, None] * current
        + short_taps[1][:, None] * joined[:, 1 : columns + 1]
        + short_taps[2][:, None] * joined[:, 0:columns]
    )


def taps_backward(current, following, short_taps):
    columns = current.shape[1]
    joined = jnp.concatenate([current, following], axis=1)
    return (
        short_taps[0][:, None] * current
        + short_taps[1][:, None] * joined[:, 1 : columns + 1]
        + short_taps[2][:, None] * joined[:, 2 : columns + 2]
    )


def per_device(query_proj, key_proj, value_proj, grad_out, filters, short_taps):
    all_chans, tok_cols = query_proj.shape
    ctx_count = lax.axis_size("ctx")
    seq_len = tok_cols * ctx_count
    seq_count = ctx_count * tok_cols // seq_len
    groups_dev = filters.shape[0]
    chan_dev = all_chans // ctx_count
    group_size = chan_dev // groups_dev
    group_rows = group_size * seq_count
    pair_rows = group_rows // 2
    position = lax.axis_index("ctx") * tok_cols
    keep_prev = jnp.where(position % seq_len == 0, 0.0, 1.0).astype(jnp.float32)
    keep_next = jnp.where((position + tok_cols) % seq_len == 0, 0.0, 1.0).astype(jnp.float32)
    tables = fourier_tables(seq_len)
    inner = tables[4].shape[1]
    tails = jnp.concatenate([query_proj[:, -2:], key_proj[:, -2:], value_proj[:, -2:]], axis=1)
    tails = shifted(tails, "ctx", 1)
    halo = jnp.where(keep_prev > 0, tails, jnp.zeros_like(tails))
    query_conv, key_conv, value_conv, outgoing = front(
        query_proj, key_proj, value_proj, grad_out, halo, short_taps.T, chan_dev
    )
    filter_spec = forward_spectrum(filters.astype(jnp.float32), None, tables)
    filter_real = filter_spec[:, None, :, :inner]
    filter_imag = filter_spec[:, None, :, inner:]

    def to_rows(source):
        return source.reshape(groups_dev, group_rows, seq_len)

    def to_chan(source):
        return source.reshape(chan_dev, ctx_count * tok_cols)

    def spectrum_of(rows_three):
        paired = rows_three.reshape(groups_dev, 2, pair_rows, seq_len).astype(jnp.float32)
        spec = forward_spectrum(
            paired[:, 0].reshape(-1, seq_len), paired[:, 1].reshape(-1, seq_len), tables
        )
        spec = spec.reshape((groups_dev, pair_rows) + spec.shape[1:])
        return (spec[..., :inner], spec[..., inner:])

    def back_to_rows(spec_real, spec_imag):
        joined = jnp.concatenate([spec_real, spec_imag], axis=-1)
        joined = joined.reshape((-1,) + joined.shape[2:])
        first_rows, second_rows = inverse_spectrum(joined, tables, True)
        first_rows = first_rows.reshape(groups_dev, pair_rows, seq_len)
        second_rows = second_rows.reshape(groups_dev, pair_rows, seq_len)
        return jnp.concatenate([first_rows, second_rows], axis=1)

    cotangent = grad_out.astype(jnp.float32)
    incoming = lax.all_to_all(outgoing, "ctx", split_axis=0, concat_axis=1, tiled=True)
    gated_rows = to_rows(incoming[:chan_dev])
    grad_mixed = to_rows(incoming[chan_dev:])
    gated_spec = spectrum_of(gated_rows)
    prod_real = gated_spec[0] * filter_real - gated_spec[1] * filter_imag
    prod_imag = gated_spec[0] * filter_imag + gated_spec[1] * filter_real
    mixed_rows = back_to_rows(prod_real, prod_imag).astype(jnp.bfloat16)
    grad_spec = spectrum_of(grad_mixed)
    prod_real = grad_spec[0] * filter_real + grad_spec[1] * filter_imag
    prod_imag = grad_spec[1] * filter_real - grad_spec[0] * filter_imag
    grad_gated = back_to_rows(prod_real, prod_imag).astype(jnp.bfloat16)
    returning = jnp.concatenate([to_chan(mixed_rows), to_chan(grad_gated)], axis=0)
    returned = lax.all_to_all(returning, "ctx", split_axis=1, concat_axis=0, tiled=True)
    returned = returned.reshape(ctx_count, 2 * chan_dev, tok_cols)
    mixed_tok = returned[:, :chan_dev].reshape(all_chans, tok_cols)
    grad_gated_tok = returned[:, chan_dev:].reshape(all_chans, tok_cols)
    grad_qconv = (cotangent * mixed_tok.astype(jnp.float32)).astype(jnp.bfloat16)
    cross_real = jnp.sum(grad_spec[0] * gated_spec[0] + grad_spec[1] * gated_spec[1], axis=1)
    cross_imag = jnp.sum(grad_spec[1] * gated_spec[0] - grad_spec[0] * gated_spec[1], axis=1)
    filter_terms = inverse_spectrum(
        jnp.concatenate([cross_real, cross_imag], axis=-1), tables, False
    )
    scale = 1.0 / math.sqrt(float(lax.axis_size("dp") * seq_count * group_size * seq_len))
    grad_filters = ring_scatter_sum(filter_terms, "dp") * scale
    grad_kconv = (grad_gated_tok.astype(jnp.float32) * value_conv.astype(jnp.float32)).astype(
        jnp.bfloat16
    )
    grad_vconv = (grad_gated_tok.astype(jnp.float32) * key_conv.astype(jnp.float32)).astype(
        jnp.bfloat16
    )
    grad_qconv, grad_kconv, grad_vconv = lax.optimization_barrier(
        (grad_qconv, grad_kconv, grad_vconv)
    )
    heads = jnp.concatenate([grad_qconv[:, :2], grad_kconv[:, :2], grad_vconv[:, :2]], axis=1)
    heads = shifted(heads, "ctx", -1)
    following = (heads[:, 0:2], heads[:, 2:4], heads[:, 4:6])
    grad_query = taps_backward(
        grad_qconv.astype(jnp.float32), following[0].astype(jnp.float32) * keep_next, short_taps
    ).astype(jnp.bfloat16)
    grad_key = taps_backward(
        grad_kconv.astype(jnp.float32), following[1].astype(jnp.float32) * keep_next, short_taps
    ).astype(jnp.bfloat16)
    grad_value = taps_backward(
        grad_vconv.astype(jnp.float32), following[2].astype(jnp.float32) * keep_next, short_taps
    ).astype(jnp.bfloat16)
    return (grad_query, grad_key, grad_value, grad_filters)


def solution(mesh):
    in_specs = (
        P(None, ("dp", "ctx")),
        P(None, ("dp", "ctx")),
        P(None, ("dp", "ctx")),
        P(None, ("dp", "ctx")),
        P("ctx", None),
        P(),
    )
    out_specs = (
        P(None, ("dp", "ctx")),
        P(None, ("dp", "ctx")),
        P(None, ("dp", "ctx")),
        P("ctx", "dp"),
    )
    return jax.shard_map(
        per_device, mesh=mesh, in_specs=in_specs, out_specs=out_specs, check_vma=False
    )
```

```python
import functools
import math

import jax
import jax.numpy as jnp
from jax import lax
from jax.experimental import pallas as pl
from jax.experimental.pallas import tpu as pltpu
from jax.sharding import PartitionSpec as P

highest = lax.Precision.HIGH
triple = lax.Precision.HIGH


def shifted(array, axis, by):
    size = lax.axis_size(axis)
    pairs = [(i, i + by) for i in range(size) if 0 <= i + by < size]
    return lax.ppermute(array, axis, pairs)


def ring_scatter_sum(terms, axis):
    count = lax.axis_size(axis)
    width = terms.shape[1] // count
    me = lax.axis_index(axis)
    total = lax.dynamic_slice_in_dim(terms, me * width, width, axis=1)
    for step in range(1, count):
        target = (me + step) % count
        piece = lax.dynamic_slice_in_dim(terms, target * width, width, axis=1)
        pairs = [(i, (i + step) % count) for i in range(count)]
        total = total + lax.ppermute(piece, axis, pairs)
    return total


def angle_table(first_count, second_count, modulus):
    first_index = jnp.arange(first_count, dtype=jnp.int32)
    second_index = jnp.arange(second_count, dtype=jnp.int32)
    product = first_index[:, None] * second_index[None, :] % modulus
    angle = product.astype(jnp.float32) * (2.0 * math.pi / modulus)
    return (jnp.cos(angle), jnp.sin(angle))


def rotation_table(cos_part, sin_part):
    upper = jnp.concatenate([cos_part, -sin_part], axis=1)
    lower = jnp.concatenate([sin_part, cos_part], axis=1)
    return jnp.concatenate([upper, lower], axis=0)


def fourier_tables(length):
    inner = min(128, length)
    outer = 2 * length // inner
    outer_cos, outer_sin = angle_table(outer // 2, outer, outer)
    twist_cos, twist_sin = angle_table(outer, inner, 2 * length)
    inner_cos, inner_sin = angle_table(inner, inner, inner)
    fwd_outer = rotation_table(outer_cos, outer_sin)
    fwd_inner = rotation_table(inner_cos, inner_sin)
    inv_inner = rotation_table(inner_cos, -inner_sin)
    inv_outer = rotation_table(outer_cos.T, -outer_sin.T)
    return (fwd_outer, fwd_inner, inv_inner, inv_outer, twist_cos, twist_sin)


def forward_spectrum(real_rows, imag_rows, tables):
    fwd_outer, fwd_inner, inv_inner, inv_outer, twist_cos, twist_sin = tables
    row_count = real_rows.shape[0]
    outer = twist_cos.shape[0]
    inner = twist_cos.shape[1]
    half_outer = outer // 2
    real_blocks = real_rows.reshape(row_count, half_outer, inner)
    if imag_rows is None:
        blocks = real_blocks
        table = fwd_outer[:half_outer]
    else:
        blocks = jnp.concatenate(
            [real_blocks, imag_rows.reshape(row_count, half_outer, inner)], axis=1
        )
        table = fwd_outer
    first = jnp.einsum("man,ak->mkn", blocks, table, precision=triple)
    first_real = first[:, :outer]
    first_imag = first[:, outer:]
    turned = jnp.concatenate(
        [
            first_real * twist_cos + first_imag * twist_sin,
            first_imag * twist_cos - first_real * twist_sin,
        ],
        axis=2,
    )
    return jnp.einsum("mkn,nj->mkj", turned, fwd_inner, precision=highest)


def inverse_spectrum(spectrum, tables, both_parts):
    fwd_outer, fwd_inner, inv_inner, inv_outer, twist_cos, twist_sin = tables
    row_count = spectrum.shape[0]
    outer = twist_cos.shape[0]
    inner = twist_cos.shape[1]
    half_outer = outer // 2
    length = half_outer * inner
    first = jnp.einsum("mkj,jn->mkn", spectrum, inv_inner, precision=highest)
    first_real = first[..., :inner]
    first_imag = first[..., inner:]
    turned = jnp.concatenate(
        [
            first_real * twist_cos - first_imag * twist_sin,
            first_imag * twist_cos + first_real * twist_sin,
        ],
        axis=1,
    )
    table = inv_outer if both_parts else inv_outer[:, :half_outer]
    values = jnp.einsum("mkn,ka->man", turned, table, precision=highest) * (1.0 / (2.0 * length))
    if both_parts:
        return (
            values[:, :half_outer].reshape(row_count, length),
            values[:, half_outer:].reshape(row_count, length),
        )
    return values.reshape(row_count, length)


BLOCK_ROWS = 1024
SUB_ROWS = 128


def front_kernel(chan_dev, q_ref, k_ref, v_ref, g_ref, halo_ref, taps_ref, qc_ref, kc_ref, vc_ref, out_ref):
    rows, cols = q_ref.shape
    chunk = min(SUB_ROWS, rows)
    per_chunk = chunk // chan_dev
    lane = lax.broadcasted_iota(jnp.int32, (chunk, cols), 1)

    def body(step, carry):
        span = pl.ds(pl.multiple_of(step * chunk, chunk), chunk)
        halo = halo_ref[span, :].astype(jnp.float32)
        taps = taps_ref[span, :]
        first, second, third = taps[:, 0:1], taps[:, 1:2], taps[:, 2:3]

        def conv(x_ref, slot):
            x = x_ref[span, :].astype(jnp.float32)
            older = halo[:, 2 * slot : 2 * slot + 1]
            newer = halo[:, 2 * slot + 1 : 2 * slot + 2]
            back_one = jnp.where(lane == 0, newer, pltpu.roll(x, 1, 1))
            rolled = pltpu.roll(x, 2, 1)
            back_two = jnp.where(lane == 0, older, jnp.where(lane == 1, newer, rolled))
            return (first * x + second * back_one + third * back_two).astype(jnp.bfloat16)

        qc = conv(q_ref, 0)
        kc = conv(k_ref, 1)
        vc = conv(v_ref, 2)
        qc_ref[span, :] = qc
        kc_ref[span, :] = kc
        vc_ref[span, :] = vc
        gated = (kc.astype(jnp.float32) * vc.astype(jnp.float32)).astype(jnp.bfloat16)
        grad_mixed = (g_ref[span, :].astype(jnp.float32) * qc.astype(jnp.float32)).astype(jnp.bfloat16)
        dest = pl.ds(pl.multiple_of(step * per_chunk, per_chunk), per_chunk)
        out_ref[dest, :chan_dev, :] = gated.reshape(per_chunk, chan_dev, cols)
        out_ref[dest, chan_dev:, :] = grad_mixed.reshape(per_chunk, chan_dev, cols)
        return carry

    lax.fori_loop(0, rows // chunk, body, 0)


def front(query_proj, key_proj, value_proj, grad_out, halo, taps_cols, chan_dev):
    all_chans, tok_cols = query_proj.shape
    block = min(BLOCK_ROWS, all_chans)
    tile = pl.BlockSpec((block, tok_cols), lambda i: (i, 0))
    return pl.pallas_call(
        functools.partial(front_kernel, chan_dev),
        grid=(all_chans // block,),
        in_specs=[tile, tile, tile, tile, pl.BlockSpec((block, 6), lambda i: (i, 0)),
                  pl.BlockSpec((block, 3), lambda i: (i, 0))],
        out_specs=[tile, tile, tile,
                   pl.BlockSpec((block // chan_dev, 2 * chan_dev, tok_cols), lambda i: (i, 0, 0))],
        out_shape=[jax.ShapeDtypeStruct((all_chans, tok_cols), jnp.bfloat16)] * 3
        + [jax.ShapeDtypeStruct((all_chans // chan_dev, 2 * chan_dev, tok_cols), jnp.bfloat16)],
        cost_estimate=pl.CostEstimate(flops=30 * all_chans * tok_cols, transcendentals=0,
                                      bytes_accessed=18 * all_chans * tok_cols),
    )(query_proj, key_proj, value_proj, grad_out, halo, taps_cols)


def taps_forward(current, earlier, short_taps):
    columns = current.shape[1]
    joined = jnp.concatenate([earlier, current], axis=1)
    return (
        short_taps[0][:, None] * current
        + short_taps[1][:, None] * joined[:, 1 : columns + 1]
        + short_taps[2][:, None] * joined[:, 0:columns]
    )


def taps_backward(current, following, short_taps):
    columns = current.shape[1]
    joined = jnp.concatenate([current, following], axis=1)
    return (
        short_taps[0][:, None] * current
        + short_taps[1][:, None] * joined[:, 1 : columns + 1]
        + short_taps[2][:, None] * joined[:, 2 : columns + 2]
    )


def per_device(query_proj, key_proj, value_proj, grad_out, filters, short_taps):
    all_chans, tok_cols = query_proj.shape
    ctx_count = lax.axis_size("ctx")
    seq_len = tok_cols * ctx_count
    seq_count = ctx_count * tok_cols // seq_len
    groups_dev = filters.shape[0]
    chan_dev = all_chans // ctx_count
    group_size = chan_dev // groups_dev
    group_rows = group_size * seq_count
    pair_rows = group_rows // 2
    position = lax.axis_index("ctx") * tok_cols
    keep_prev = jnp.where(position % seq_len == 0, 0.0, 1.0).astype(jnp.float32)
    keep_next = jnp.where((position + tok_cols) % seq_len == 0, 0.0, 1.0).astype(jnp.float32)
    tables = fourier_tables(seq_len)
    inner = tables[4].shape[1]
    tails = jnp.concatenate([query_proj[:, -2:], key_proj[:, -2:], value_proj[:, -2:]], axis=1)
    tails = shifted(tails, "ctx", 1)
    halo = jnp.where(keep_prev > 0, tails, jnp.zeros_like(tails))
    query_conv, key_conv, value_conv, outgoing = front(
        query_proj, key_proj, value_proj, grad_out, halo, short_taps.T, chan_dev
    )
    outgoing = outgoing.reshape(2 * all_chans, tok_cols)
    filter_spec = forward_spectrum(filters.astype(jnp.float32), None, tables)
    filter_real = filter_spec[:, None, :, :inner]
    filter_imag = filter_spec[:, None, :, inner:]

    def to_rows(source):
        return source.reshape(groups_dev, group_rows, seq_len)

    def to_chan(source):
        return source.reshape(chan_dev, ctx_count * tok_cols)

    def spectrum_of(rows_three):
        paired = rows_three.reshape(groups_dev, 2, pair_rows, seq_len).astype(jnp.float32)
        spec = forward_spectrum(
            paired[:, 0].reshape(-1, seq_len), paired[:, 1].reshape(-1, seq_len), tables
        )
        spec = spec.reshape((groups_dev, pair_rows) + spec.shape[1:])
        return (spec[..., :inner], spec[..., inner:])

    def back_to_rows(spec_real, spec_imag):
        joined = jnp.concatenate([spec_real, spec_imag], axis=-1)
        joined = joined.reshape((-1,) + joined.shape[2:])
        first_rows, second_rows = inverse_spectrum(joined, tables, True)
        first_rows = first_rows.reshape(groups_dev, pair_rows, seq_len)
        second_rows = second_rows.reshape(groups_dev, pair_rows, seq_len)
        return jnp.concatenate([first_rows, second_rows], axis=1)

    cotangent = grad_out.astype(jnp.float32)
    incoming = lax.all_to_all(outgoing, "ctx", split_axis=0, concat_axis=1, tiled=True)
    gated_rows = to_rows(incoming[:chan_dev])
    grad_mixed = to_rows(incoming[chan_dev:])
    gated_spec = spectrum_of(gated_rows)
    prod_real = gated_spec[0] * filter_real - gated_spec[1] * filter_imag
    prod_imag = gated_spec[0] * filter_imag + gated_spec[1] * filter_real
    mixed_rows = back_to_rows(prod_real, prod_imag).astype(jnp.bfloat16)
    grad_spec = spectrum_of(grad_mixed)
    prod_real = grad_spec[0] * filter_real + grad_spec[1] * filter_imag
    prod_imag = grad_spec[1] * filter_real - grad_spec[0] * filter_imag
    grad_gated = back_to_rows(prod_real, prod_imag).astype(jnp.bfloat16)
    returning = jnp.concatenate([to_chan(mixed_rows), to_chan(grad_gated)], axis=0)
    returned = lax.all_to_all(returning, "ctx", split_axis=1, concat_axis=0, tiled=True)
    returned = returned.reshape(ctx_count, 2 * chan_dev, tok_cols)
    mixed_tok = returned[:, :chan_dev].reshape(all_chans, tok_cols)
    grad_gated_tok = returned[:, chan_dev:].reshape(all_chans, tok_cols)
    grad_qconv = (cotangent * mixed_tok.astype(jnp.float32)).astype(jnp.bfloat16)
    cross_real = jnp.sum(grad_spec[0] * gated_spec[0] + grad_spec[1] * gated_spec[1], axis=1)
    cross_imag = jnp.sum(grad_spec[1] * gated_spec[0] - grad_spec[0] * gated_spec[1], axis=1)
    filter_terms = inverse_spectrum(
        jnp.concatenate([cross_real, cross_imag], axis=-1), tables, False
    )
    scale = 1.0 / math.sqrt(float(lax.axis_size("dp") * seq_count * group_size * seq_len))
    grad_filters = ring_scatter_sum(filter_terms, "dp") * scale
    grad_kconv = (grad_gated_tok.astype(jnp.float32) * value_conv.astype(jnp.float32)).astype(
        jnp.bfloat16
    )
    grad_vconv = (grad_gated_tok.astype(jnp.float32) * key_conv.astype(jnp.float32)).astype(
        jnp.bfloat16
    )
    grad_qconv, grad_kconv, grad_vconv = lax.optimization_barrier(
        (grad_qconv, grad_kconv, grad_vconv)
    )
    zero_tail = jnp.zeros((all_chans, 2), jnp.float32)
    interior = lax.optimization_barrier(
        tuple(
            taps_backward(part.astype(jnp.float32), zero_tail, short_taps).astype(jnp.bfloat16)
            for part in (grad_qconv, grad_kconv, grad_vconv)
        )
    )
    heads = jnp.concatenate([grad_qconv[:, :2], grad_kconv[:, :2], grad_vconv[:, :2]], axis=1)
    heads = shifted(heads, "ctx", -1).astype(jnp.float32) * keep_next

    def patched(whole, part, slot):
        edge = taps_backward(
            part[:, -2:].astype(jnp.float32), heads[:, 2 * slot : 2 * slot + 2], short_taps
        ).astype(jnp.bfloat16)
        return lax.dynamic_update_slice(whole, edge, (0, tok_cols - 2))

    grad_query = patched(interior[0], grad_qconv, 0)
    grad_key = patched(interior[1], grad_kconv, 1)
    grad_value = patched(interior[2], grad_vconv, 2)
    return (grad_query, grad_key, grad_value, grad_filters)


def solution(mesh):
    in_specs = (
        P(None, ("dp", "ctx")),
        P(None, ("dp", "ctx")),
        P(None, ("dp", "ctx")),
        P(None, ("dp", "ctx")),
        P("ctx", None),
        P(),
    )
    out_specs = (
        P(None, ("dp", "ctx")),
        P(None, ("dp", "ctx")),
        P(None, ("dp", "ctx")),
        P("ctx", "dp"),
    )
    return jax.shard_map(
        per_device, mesh=mesh, in_specs=in_specs, out_specs=out_specs, check_vma=False
    )
```

```python
import functools
import math

import jax
import jax.numpy as jnp
from jax import lax
from jax.experimental import pallas as pl
from jax.experimental.pallas import tpu as pltpu
from jax.sharding import PartitionSpec as P

highest = lax.Precision.HIGH
triple = lax.Precision.HIGH


def shifted(array, axis, by):
    size = lax.axis_size(axis)
    pairs = [(i, i + by) for i in range(size) if 0 <= i + by < size]
    return lax.ppermute(array, axis, pairs)


def ring_scatter_sum(terms, axis):
    count = lax.axis_size(axis)
    width = terms.shape[1] // count
    me = lax.axis_index(axis)
    total = lax.dynamic_slice_in_dim(terms, me * width, width, axis=1)
    for step in range(1, count):
        target = (me + step) % count
        piece = lax.dynamic_slice_in_dim(terms, target * width, width, axis=1)
        pairs = [(i, (i + step) % count) for i in range(count)]
        total = total + lax.ppermute(piece, axis, pairs)
    return total


def angle_table(first_count, second_count, modulus):
    first_index = jnp.arange(first_count, dtype=jnp.int32)
    second_index = jnp.arange(second_count, dtype=jnp.int32)
    product = first_index[:, None] * second_index[None, :] % modulus
    angle = product.astype(jnp.float32) * (2.0 * math.pi / modulus)
    return (jnp.cos(angle), jnp.sin(angle))


def rotation_table(cos_part, sin_part):
    upper = jnp.concatenate([cos_part, -sin_part], axis=1)
    lower = jnp.concatenate([sin_part, cos_part], axis=1)
    return jnp.concatenate([upper, lower], axis=0)


def fourier_tables(length):
    inner = min(128, length)
    outer = 2 * length // inner
    outer_cos, outer_sin = angle_table(outer // 2, outer, outer)
    twist_cos, twist_sin = angle_table(outer, inner, 2 * length)
    inner_cos, inner_sin = angle_table(inner, inner, inner)
    fwd_outer = rotation_table(outer_cos, outer_sin)
    fwd_inner = rotation_table(inner_cos, inner_sin)
    inv_inner = rotation_table(inner_cos, -inner_sin)
    inv_outer = rotation_table(outer_cos.T, -outer_sin.T)
    return (fwd_outer, fwd_inner, inv_inner, inv_outer, twist_cos, twist_sin)


def forward_spectrum(real_rows, imag_rows, tables):
    fwd_outer, fwd_inner, inv_inner, inv_outer, twist_cos, twist_sin = tables
    row_count = real_rows.shape[0]
    outer = twist_cos.shape[0]
    inner = twist_cos.shape[1]
    half_outer = outer // 2
    real_blocks = real_rows.reshape(row_count, half_outer, inner)
    if imag_rows is None:
        blocks = real_blocks
        table = fwd_outer[:half_outer]
    else:
        blocks = jnp.concatenate(
            [real_blocks, imag_rows.reshape(row_count, half_outer, inner)], axis=1
        )
        table = fwd_outer
    first = jnp.einsum("man,ak->mkn", blocks, table, precision=triple)
    first_real = first[:, :outer]
    first_imag = first[:, outer:]
    turned = jnp.concatenate(
        [
            first_real * twist_cos + first_imag * twist_sin,
            first_imag * twist_cos - first_real * twist_sin,
        ],
        axis=2,
    )
    return jnp.einsum("mkn,nj->mkj", turned, fwd_inner, precision=highest)


def inverse_spectrum(spectrum, tables, both_parts):
    fwd_outer, fwd_inner, inv_inner, inv_outer, twist_cos, twist_sin = tables
    row_count = spectrum.shape[0]
    outer = twist_cos.shape[0]
    inner = twist_cos.shape[1]
    half_outer = outer // 2
    length = half_outer * inner
    first = jnp.einsum("mkj,jn->mkn", spectrum, inv_inner, precision=highest)
    first_real = first[..., :inner]
    first_imag = first[..., inner:]
    turned = jnp.concatenate(
        [
            first_real * twist_cos - first_imag * twist_sin,
            first_imag * twist_cos + first_real * twist_sin,
        ],
        axis=1,
    )
    table = inv_outer if both_parts else inv_outer[:, :half_outer]
    values = jnp.einsum("mkn,ka->man", turned, table, precision=highest) * (1.0 / (2.0 * length))
    if both_parts:
        return (
            values[:, :half_outer].reshape(row_count, length),
            values[:, half_outer:].reshape(row_count, length),
        )
    return values.reshape(row_count, length)


BLOCK_ROWS = 1024
SUB_ROWS = 128


def front_kernel(chan_dev, q_ref, k_ref, v_ref, g_ref, halo_ref, taps_ref, qc_ref, kc_ref, vc_ref, out_ref):
    rows, cols = q_ref.shape
    chunk = min(SUB_ROWS, rows)
    per_chunk = chunk // chan_dev
    lane = lax.broadcasted_iota(jnp.int32, (chunk, cols), 1)

    def body(step, carry):
        span = pl.ds(pl.multiple_of(step * chunk, chunk), chunk)
        halo = halo_ref[span, :].astype(jnp.float32)
        taps = taps_ref[span, :]
        first, second, third = taps[:, 0:1], taps[:, 1:2], taps[:, 2:3]

        def conv(x_ref, slot):
            x = x_ref[span, :].astype(jnp.float32)
            older = halo[:, 2 * slot : 2 * slot + 1]
            newer = halo[:, 2 * slot + 1 : 2 * slot + 2]
            back_one = jnp.where(lane == 0, newer, pltpu.roll(x, 1, 1))
            rolled = pltpu.roll(x, 2, 1)
            back_two = jnp.where(lane == 0, older, jnp.where(lane == 1, newer, rolled))
            return (first * x + second * back_one + third * back_two).astype(jnp.bfloat16)

        qc = conv(q_ref, 0)
        kc = conv(k_ref, 1)
        vc = conv(v_ref, 2)
        qc_ref[span, :] = qc
        kc_ref[span, :] = kc
        vc_ref[span, :] = vc
        gated = (kc.astype(jnp.float32) * vc.astype(jnp.float32)).astype(jnp.bfloat16)
        grad_mixed = (g_ref[span, :].astype(jnp.float32) * qc.astype(jnp.float32)).astype(jnp.bfloat16)
        dest = pl.ds(pl.multiple_of(step * per_chunk, per_chunk), per_chunk)
        out_ref[dest, :chan_dev, :] = gated.reshape(per_chunk, chan_dev, cols)
        out_ref[dest, chan_dev:, :] = grad_mixed.reshape(per_chunk, chan_dev, cols)
        return carry

    lax.fori_loop(0, rows // chunk, body, 0)


def front(query_proj, key_proj, value_proj, grad_out, halo, taps_cols, chan_dev):
    all_chans, tok_cols = query_proj.shape
    block = min(BLOCK_ROWS, all_chans)
    tile = pl.BlockSpec((block, tok_cols), lambda i: (i, 0))
    return pl.pallas_call(
        functools.partial(front_kernel, chan_dev),
        grid=(all_chans // block,),
        in_specs=[tile, tile, tile, tile, pl.BlockSpec((block, 6), lambda i: (i, 0)),
                  pl.BlockSpec((block, 3), lambda i: (i, 0))],
        out_specs=[tile, tile, tile,
                   pl.BlockSpec((block // chan_dev, 2 * chan_dev, tok_cols), lambda i: (i, 0, 0))],
        out_shape=[jax.ShapeDtypeStruct((all_chans, tok_cols), jnp.bfloat16)] * 3
        + [jax.ShapeDtypeStruct((all_chans // chan_dev, 2 * chan_dev, tok_cols), jnp.bfloat16)],
        cost_estimate=pl.CostEstimate(flops=30 * all_chans * tok_cols, transcendentals=0,
                                      bytes_accessed=18 * all_chans * tok_cols),
    )(query_proj, key_proj, value_proj, grad_out, halo, taps_cols)


def taps_forward(current, earlier, short_taps):
    columns = current.shape[1]
    joined = jnp.concatenate([earlier, current], axis=1)
    return (
        short_taps[0][:, None] * current
        + short_taps[1][:, None] * joined[:, 1 : columns + 1]
        + short_taps[2][:, None] * joined[:, 0:columns]
    )


def taps_backward(current, following, short_taps):
    columns = current.shape[1]
    joined = jnp.concatenate([current, following], axis=1)
    return (
        short_taps[0][:, None] * current
        + short_taps[1][:, None] * joined[:, 1 : columns + 1]
        + short_taps[2][:, None] * joined[:, 2 : columns + 2]
    )


def per_device(query_proj, key_proj, value_proj, grad_out, filters, short_taps):
    all_chans, tok_cols = query_proj.shape
    ctx_count = lax.axis_size("ctx")
    seq_len = tok_cols * ctx_count
    seq_count = ctx_count * tok_cols // seq_len
    groups_dev = filters.shape[0]
    chan_dev = all_chans // ctx_count
    group_size = chan_dev // groups_dev
    group_rows = group_size * seq_count
    pair_rows = group_rows // 2
    position = lax.axis_index("ctx") * tok_cols
    keep_prev = jnp.where(position % seq_len == 0, 0.0, 1.0).astype(jnp.float32)
    keep_next = jnp.where((position + tok_cols) % seq_len == 0, 0.0, 1.0).astype(jnp.float32)
    tables = fourier_tables(seq_len)
    inner = tables[4].shape[1]
    tails = jnp.concatenate([query_proj[:, -2:], key_proj[:, -2:], value_proj[:, -2:]], axis=1)
    tails = shifted(tails, "ctx", 1)
    halo = jnp.where(keep_prev > 0, tails, jnp.zeros_like(tails))
    query_conv, key_conv, value_conv, outgoing = front(
        query_proj, key_proj, value_proj, grad_out, halo, short_taps.T, chan_dev
    )
    outgoing = outgoing.reshape(2 * all_chans, tok_cols)
    filter_spec = forward_spectrum(filters.astype(jnp.float32), None, tables)
    filter_real = filter_spec[:, None, :, :inner]
    filter_imag = filter_spec[:, None, :, inner:]

    def to_rows(source):
        return source.reshape(groups_dev, group_rows, seq_len)

    def to_chan(source):
        return source.reshape(chan_dev, ctx_count * tok_cols)

    def spectrum_of(rows_three):
        paired = rows_three.reshape(groups_dev, 2, pair_rows, seq_len).astype(jnp.float32)
        spec = forward_spectrum(
            paired[:, 0].reshape(-1, seq_len), paired[:, 1].reshape(-1, seq_len), tables
        )
        spec = spec.reshape((groups_dev, pair_rows) + spec.shape[1:])
        return (spec[..., :inner], spec[..., inner:])

    def back_to_rows(spec_real, spec_imag):
        joined = jnp.concatenate([spec_real, spec_imag], axis=-1)
        joined = joined.reshape((-1,) + joined.shape[2:])
        first_rows, second_rows = inverse_spectrum(joined, tables, True)
        first_rows = first_rows.reshape(groups_dev, pair_rows, seq_len)
        second_rows = second_rows.reshape(groups_dev, pair_rows, seq_len)
        return jnp.concatenate([first_rows, second_rows], axis=1)

    cotangent = grad_out.astype(jnp.float32)
    incoming = lax.all_to_all(outgoing, "ctx", split_axis=0, concat_axis=1, tiled=True)
    gated_rows = to_rows(incoming[:chan_dev])
    grad_mixed = to_rows(incoming[chan_dev:])
    gated_spec = spectrum_of(gated_rows)
    prod_real = gated_spec[0] * filter_real - gated_spec[1] * filter_imag
    prod_imag = gated_spec[0] * filter_imag + gated_spec[1] * filter_real
    mixed_rows = back_to_rows(prod_real, prod_imag).astype(jnp.bfloat16)
    grad_spec = spectrum_of(grad_mixed)
    prod_real = grad_spec[0] * filter_real + grad_spec[1] * filter_imag
    prod_imag = grad_spec[1] * filter_real - grad_spec[0] * filter_imag
    grad_gated = back_to_rows(prod_real, prod_imag).astype(jnp.bfloat16)
    returning = jnp.concatenate([to_chan(mixed_rows), to_chan(grad_gated)], axis=0)
    returned = lax.all_to_all(returning, "ctx", split_axis=1, concat_axis=0, tiled=True)
    returned = returned.reshape(ctx_count, 2 * chan_dev, tok_cols)
    mixed_tok = returned[:, :chan_dev].reshape(all_chans, tok_cols)
    grad_gated_tok = returned[:, chan_dev:].reshape(all_chans, tok_cols)
    grad_qconv = (cotangent * mixed_tok.astype(jnp.float32)).astype(jnp.bfloat16)
    cross_real = jnp.sum(grad_spec[0] * gated_spec[0] + grad_spec[1] * gated_spec[1], axis=1)
    cross_imag = jnp.sum(grad_spec[1] * gated_spec[0] - grad_spec[0] * gated_spec[1], axis=1)
    filter_terms = inverse_spectrum(
        jnp.concatenate([cross_real, cross_imag], axis=-1), tables, False
    )
    scale = 1.0 / math.sqrt(float(lax.axis_size("dp") * seq_count * group_size * seq_len))
    grad_filters = ring_scatter_sum(filter_terms, "dp") * scale
    grad_kconv = (grad_gated_tok.astype(jnp.float32) * value_conv.astype(jnp.float32)).astype(
        jnp.bfloat16
    )
    grad_vconv = (grad_gated_tok.astype(jnp.float32) * key_conv.astype(jnp.float32)).astype(
        jnp.bfloat16
    )
    grad_qconv, grad_kconv, grad_vconv = lax.optimization_barrier(
        (grad_qconv, grad_kconv, grad_vconv)
    )
    zero_tail = jnp.zeros((all_chans, 2), jnp.float32)
    interior = lax.optimization_barrier(
        tuple(
            taps_backward(part.astype(jnp.float32), zero_tail, short_taps).astype(jnp.bfloat16)
            for part in (grad_qconv, grad_kconv, grad_vconv)
        )
    )
    heads = jnp.concatenate([grad_qconv[:, :2], grad_kconv[:, :2], grad_vconv[:, :2]], axis=1)
    heads = shifted(heads, "ctx", -1).astype(jnp.float32) * keep_next

    lane = lax.broadcasted_iota(jnp.int32, (all_chans, tok_cols), 1)

    def patched(whole, part, slot):
        edge = taps_backward(
            part[:, -2:].astype(jnp.float32), heads[:, 2 * slot : 2 * slot + 2], short_taps
        ).astype(jnp.bfloat16)
        edge = jnp.pad(edge, ((0, 0), (tok_cols - 2, 0)))
        return jnp.where(lane >= tok_cols - 2, edge, whole)

    grad_query = patched(interior[0], grad_qconv, 0)
    grad_key = patched(interior[1], grad_kconv, 1)
    grad_value = patched(interior[2], grad_vconv, 2)
    return (grad_query, grad_key, grad_value, grad_filters)


def solution(mesh):
    in_specs = (
        P(None, ("dp", "ctx")),
        P(None, ("dp", "ctx")),
        P(None, ("dp", "ctx")),
        P(None, ("dp", "ctx")),
        P("ctx", None),
        P(),
    )
    out_specs = (
        P(None, ("dp", "ctx")),
        P(None, ("dp", "ctx")),
        P(None, ("dp", "ctx")),
        P("ctx", "dp"),
    )
    return jax.shard_map(
        per_device, mesh=mesh, in_specs=in_specs, out_specs=out_specs, check_vma=False
    )
```

```python
import functools
import math

import jax
import jax.numpy as jnp
from jax import lax
from jax.experimental import pallas as pl
from jax.experimental.pallas import tpu as pltpu
from jax.sharding import PartitionSpec as P

highest = lax.Precision.HIGH
triple = lax.Precision.HIGH


def shifted(array, axis, by):
    size = lax.axis_size(axis)
    pairs = [(i, i + by) for i in range(size) if 0 <= i + by < size]
    return lax.ppermute(array, axis, pairs)


def ring_scatter_sum(terms, axis):
    count = lax.axis_size(axis)
    width = terms.shape[1] // count
    me = lax.axis_index(axis)
    total = lax.dynamic_slice_in_dim(terms, me * width, width, axis=1)
    for step in range(1, count):
        target = (me + step) % count
        piece = lax.dynamic_slice_in_dim(terms, target * width, width, axis=1)
        pairs = [(i, (i + step) % count) for i in range(count)]
        total = total + lax.ppermute(piece, axis, pairs)
    return total


def angle_table(first_count, second_count, modulus):
    first_index = jnp.arange(first_count, dtype=jnp.int32)
    second_index = jnp.arange(second_count, dtype=jnp.int32)
    product = first_index[:, None] * second_index[None, :] % modulus
    angle = product.astype(jnp.float32) * (2.0 * math.pi / modulus)
    return (jnp.cos(angle), jnp.sin(angle))


def rotation_table(cos_part, sin_part):
    upper = jnp.concatenate([cos_part, -sin_part], axis=1)
    lower = jnp.concatenate([sin_part, cos_part], axis=1)
    return jnp.concatenate([upper, lower], axis=0)


def fourier_tables(length):
    inner = min(128, length)
    outer = 2 * length // inner
    outer_cos, outer_sin = angle_table(outer // 2, outer, outer)
    twist_cos, twist_sin = angle_table(outer, inner, 2 * length)
    inner_cos, inner_sin = angle_table(inner, inner, inner)
    fwd_outer = rotation_table(outer_cos, outer_sin)
    fwd_inner = rotation_table(inner_cos, inner_sin)
    inv_inner = rotation_table(inner_cos, -inner_sin)
    inv_outer = rotation_table(outer_cos.T, -outer_sin.T)
    return (fwd_outer, fwd_inner, inv_inner, inv_outer, twist_cos, twist_sin)


def forward_spectrum(real_rows, imag_rows, tables):
    fwd_outer, fwd_inner, inv_inner, inv_outer, twist_cos, twist_sin = tables
    row_count = real_rows.shape[0]
    outer = twist_cos.shape[0]
    inner = twist_cos.shape[1]
    half_outer = outer // 2
    real_blocks = real_rows.reshape(row_count, half_outer, inner)
    if imag_rows is None:
        blocks = real_blocks
        table = fwd_outer[:half_outer]
    else:
        blocks = jnp.concatenate(
            [real_blocks, imag_rows.reshape(row_count, half_outer, inner)], axis=1
        )
        table = fwd_outer
    first = jnp.einsum("man,ak->mkn", blocks, table, precision=triple)
    first_real = first[:, :outer]
    first_imag = first[:, outer:]
    turned = jnp.concatenate(
        [
            first_real * twist_cos + first_imag * twist_sin,
            first_imag * twist_cos - first_real * twist_sin,
        ],
        axis=2,
    )
    return jnp.einsum("mkn,nj->mkj", turned, fwd_inner, precision=highest)


def inverse_spectrum(spectrum, tables, both_parts):
    fwd_outer, fwd_inner, inv_inner, inv_outer, twist_cos, twist_sin = tables
    row_count = spectrum.shape[0]
    outer = twist_cos.shape[0]
    inner = twist_cos.shape[1]
    half_outer = outer // 2
    length = half_outer * inner
    first = jnp.einsum("mkj,jn->mkn", spectrum, inv_inner, precision=highest)
    first_real = first[..., :inner]
    first_imag = first[..., inner:]
    turned = jnp.concatenate(
        [
            first_real * twist_cos - first_imag * twist_sin,
            first_imag * twist_cos + first_real * twist_sin,
        ],
        axis=1,
    )
    table = inv_outer if both_parts else inv_outer[:, :half_outer]
    values = jnp.einsum("mkn,ka->man", turned, table, precision=highest) * (1.0 / (2.0 * length))
    if both_parts:
        return (
            values[:, :half_outer].reshape(row_count, length),
            values[:, half_outer:].reshape(row_count, length),
        )
    return values.reshape(row_count, length)


BLOCK_ROWS = 1024


def front_kernel(chan_dev, q_ref, k_ref, v_ref, g_ref, halo_ref, taps_ref, qc_ref, kc_ref, vc_ref, out_ref):
    rows, cols = q_ref.shape
    lane = lax.broadcasted_iota(jnp.int32, (rows, cols), 1)
    halo = halo_ref[...].astype(jnp.float32)
    taps = taps_ref[...]
    first, second, third = taps[:, 0:1], taps[:, 1:2], taps[:, 2:3]

    def conv(x_ref, slot):
        x = x_ref[...].astype(jnp.float32)
        older = halo[:, 2 * slot : 2 * slot + 1]
        newer = halo[:, 2 * slot + 1 : 2 * slot + 2]
        back_one = jnp.where(lane == 0, newer, pltpu.roll(x, 1, 1))
        rolled = pltpu.roll(x, 2, 1)
        back_two = jnp.where(lane == 0, older, jnp.where(lane == 1, newer, rolled))
        return (first * x + second * back_one + third * back_two).astype(jnp.bfloat16)

    qc = conv(q_ref, 0)
    kc = conv(k_ref, 1)
    vc = conv(v_ref, 2)
    qc_ref[...] = qc
    kc_ref[...] = kc
    vc_ref[...] = vc
    gated = (kc.astype(jnp.float32) * vc.astype(jnp.float32)).astype(jnp.bfloat16)
    grad_mixed = (g_ref[...].astype(jnp.float32) * qc.astype(jnp.float32)).astype(jnp.bfloat16)
    for j in range(rows // chan_dev):
        out_ref[2 * j * chan_dev : (2 * j + 1) * chan_dev, :] = gated[j * chan_dev : (j + 1) * chan_dev]
        out_ref[(2 * j + 1) * chan_dev : (2 * j + 2) * chan_dev, :] = grad_mixed[
            j * chan_dev : (j + 1) * chan_dev
        ]


def front(query_proj, key_proj, value_proj, grad_out, halo, taps_cols, chan_dev):
    all_chans, tok_cols = query_proj.shape
    block = min(BLOCK_ROWS, all_chans)
    tile = pl.BlockSpec((block, tok_cols), lambda i: (i, 0))
    return pl.pallas_call(
        functools.partial(front_kernel, chan_dev),
        grid=(all_chans // block,),
        in_specs=[tile, tile, tile, tile, pl.BlockSpec((block, 6), lambda i: (i, 0)),
                  pl.BlockSpec((block, 3), lambda i: (i, 0))],
        out_specs=[tile, tile, tile, pl.BlockSpec((2 * block, tok_cols), lambda i: (i, 0))],
        out_shape=[jax.ShapeDtypeStruct((all_chans, tok_cols), jnp.bfloat16)] * 3
        + [jax.ShapeDtypeStruct((2 * all_chans, tok_cols), jnp.bfloat16)],
        cost_estimate=pl.CostEstimate(flops=30 * all_chans * tok_cols, transcendentals=0,
                                      bytes_accessed=18 * all_chans * tok_cols),
    )(query_proj, key_proj, value_proj, grad_out, halo, taps_cols)


def taps_forward(current, earlier, short_taps):
    columns = current.shape[1]
    joined = jnp.concatenate([earlier, current], axis=1)
    return (
        short_taps[0][:, None] * current
        + short_taps[1][:, None] * joined[:, 1 : columns + 1]
        + short_taps[2][:, None] * joined[:, 0:columns]
    )


def taps_backward(current, following, short_taps):
    columns = current.shape[1]
    joined = jnp.concatenate([current, following], axis=1)
    return (
        short_taps[0][:, None] * current
        + short_taps[1][:, None] * joined[:, 1 : columns + 1]
        + short_taps[2][:, None] * joined[:, 2 : columns + 2]
    )


def per_device(query_proj, key_proj, value_proj, grad_out, filters, short_taps):
    all_chans, tok_cols = query_proj.shape
    ctx_count = lax.axis_size("ctx")
    seq_len = tok_cols * ctx_count
    seq_count = ctx_count * tok_cols // seq_len
    groups_dev = filters.shape[0]
    chan_dev = all_chans // ctx_count
    group_size = chan_dev // groups_dev
    group_rows = group_size * seq_count
    pair_rows = group_rows // 2
    position = lax.axis_index("ctx") * tok_cols
    keep_prev = jnp.where(position % seq_len == 0, 0.0, 1.0).astype(jnp.float32)
    keep_next = jnp.where((position + tok_cols) % seq_len == 0, 0.0, 1.0).astype(jnp.float32)
    tables = fourier_tables(seq_len)
    inner = tables[4].shape[1]
    tails = jnp.concatenate([query_proj[:, -2:], key_proj[:, -2:], value_proj[:, -2:]], axis=1)
    tails = shifted(tails, "ctx", 1)
    halo = jnp.where(keep_prev > 0, tails, jnp.zeros_like(tails))
    query_conv, key_conv, value_conv, outgoing = front(
        query_proj, key_proj, value_proj, grad_out, halo, short_taps.T, chan_dev
    )
    filter_spec = forward_spectrum(filters.astype(jnp.float32), None, tables)
    filter_real = filter_spec[:, None, :, :inner]
    filter_imag = filter_spec[:, None, :, inner:]

    def to_rows(source):
        return source.reshape(groups_dev, group_rows, seq_len)

    def to_chan(source):
        return source.reshape(chan_dev, ctx_count * tok_cols)

    def spectrum_of(rows_three):
        paired = rows_three.reshape(groups_dev, 2, pair_rows, seq_len).astype(jnp.float32)
        spec = forward_spectrum(
            paired[:, 0].reshape(-1, seq_len), paired[:, 1].reshape(-1, seq_len), tables
        )
        spec = spec.reshape((groups_dev, pair_rows) + spec.shape[1:])
        return (spec[..., :inner], spec[..., inner:])

    def back_to_rows(spec_real, spec_imag):
        joined = jnp.concatenate([spec_real, spec_imag], axis=-1)
        joined = joined.reshape((-1,) + joined.shape[2:])
        first_rows, second_rows = inverse_spectrum(joined, tables, True)
        first_rows = first_rows.reshape(groups_dev, pair_rows, seq_len)
        second_rows = second_rows.reshape(groups_dev, pair_rows, seq_len)
        return jnp.concatenate([first_rows, second_rows], axis=1)

    cotangent = grad_out.astype(jnp.float32)
    incoming = lax.all_to_all(outgoing, "ctx", split_axis=0, concat_axis=1, tiled=True)
    gated_rows = to_rows(incoming[:chan_dev])
    grad_mixed = to_rows(incoming[chan_dev:])
    gated_spec = spectrum_of(gated_rows)
    prod_real = gated_spec[0] * filter_real - gated_spec[1] * filter_imag
    prod_imag = gated_spec[0] * filter_imag + gated_spec[1] * filter_real
    mixed_rows = back_to_rows(prod_real, prod_imag).astype(jnp.bfloat16)
    grad_spec = spectrum_of(grad_mixed)
    prod_real = grad_spec[0] * filter_real + grad_spec[1] * filter_imag
    prod_imag = grad_spec[1] * filter_real - grad_spec[0] * filter_imag
    grad_gated = back_to_rows(prod_real, prod_imag).astype(jnp.bfloat16)
    returning = jnp.concatenate([to_chan(mixed_rows), to_chan(grad_gated)], axis=0)
    returned = lax.all_to_all(returning, "ctx", split_axis=1, concat_axis=0, tiled=True)
    returned = returned.reshape(ctx_count, 2 * chan_dev, tok_cols)
    mixed_tok = returned[:, :chan_dev].reshape(all_chans, tok_cols)
    grad_gated_tok = returned[:, chan_dev:].reshape(all_chans, tok_cols)
    grad_qconv = (cotangent * mixed_tok.astype(jnp.float32)).astype(jnp.bfloat16)
    cross_real = jnp.sum(grad_spec[0] * gated_spec[0] + grad_spec[1] * gated_spec[1], axis=1)
    cross_imag = jnp.sum(grad_spec[1] * gated_spec[0] - grad_spec[0] * gated_spec[1], axis=1)
    filter_terms = inverse_spectrum(
        jnp.concatenate([cross_real, cross_imag], axis=-1), tables, False
    )
    scale = 1.0 / math.sqrt(float(lax.axis_size("dp") * seq_count * group_size * seq_len))
    grad_filters = ring_scatter_sum(filter_terms, "dp") * scale
    grad_kconv = (grad_gated_tok.astype(jnp.float32) * value_conv.astype(jnp.float32)).astype(
        jnp.bfloat16
    )
    grad_vconv = (grad_gated_tok.astype(jnp.float32) * key_conv.astype(jnp.float32)).astype(
        jnp.bfloat16
    )
    grad_qconv, grad_kconv, grad_vconv = lax.optimization_barrier(
        (grad_qconv, grad_kconv, grad_vconv)
    )
    heads = jnp.concatenate([grad_qconv[:, :2], grad_kconv[:, :2], grad_vconv[:, :2]], axis=1)
    heads = shifted(heads, "ctx", -1)
    following = (heads[:, 0:2], heads[:, 2:4], heads[:, 4:6])
    grad_query = taps_backward(
        grad_qconv.astype(jnp.float32), following[0].astype(jnp.float32) * keep_next, short_taps
    ).astype(jnp.bfloat16)
    grad_key = taps_backward(
        grad_kconv.astype(jnp.float32), following[1].astype(jnp.float32) * keep_next, short_taps
    ).astype(jnp.bfloat16)
    grad_value = taps_backward(
        grad_vconv.astype(jnp.float32), following[2].astype(jnp.float32) * keep_next, short_taps
    ).astype(jnp.bfloat16)
    return (grad_query, grad_key, grad_value, grad_filters)


def solution(mesh):
    in_specs = (
        P(None, ("dp", "ctx")),
        P(None, ("dp", "ctx")),
        P(None, ("dp", "ctx")),
        P(None, ("dp", "ctx")),
        P("ctx", None),
        P(),
    )
    out_specs = (
        P(None, ("dp", "ctx")),
        P(None, ("dp", "ctx")),
        P(None, ("dp", "ctx")),
        P("ctx", "dp"),
    )
    return jax.shard_map(
        per_device, mesh=mesh, in_specs=in_specs, out_specs=out_specs, check_vma=False
    )
```

```python
import functools
import math

import jax
import jax.numpy as jnp
from jax import lax
from jax.experimental import pallas as pl
from jax.experimental.pallas import tpu as pltpu
from jax.sharding import PartitionSpec as P

highest = lax.Precision.HIGH
triple = lax.Precision.HIGH


def shifted(array, axis, by):
    size = lax.axis_size(axis)
    pairs = [(i, i + by) for i in range(size) if 0 <= i + by < size]
    return lax.ppermute(array, axis, pairs)


def ring_scatter_sum(terms, axis):
    count = lax.axis_size(axis)
    width = terms.shape[1] // count
    me = lax.axis_index(axis)
    total = lax.dynamic_slice_in_dim(terms, me * width, width, axis=1)
    for step in range(1, count):
        target = (me + step) % count
        piece = lax.dynamic_slice_in_dim(terms, target * width, width, axis=1)
        pairs = [(i, (i + step) % count) for i in range(count)]
        total = total + lax.ppermute(piece, axis, pairs)
    return total


def angle_table(first_count, second_count, modulus):
    first_index = jnp.arange(first_count, dtype=jnp.int32)
    second_index = jnp.arange(second_count, dtype=jnp.int32)
    product = first_index[:, None] * second_index[None, :] % modulus
    angle = product.astype(jnp.float32) * (2.0 * math.pi / modulus)
    return (jnp.cos(angle), jnp.sin(angle))


def rotation_table(cos_part, sin_part):
    upper = jnp.concatenate([cos_part, -sin_part], axis=1)
    lower = jnp.concatenate([sin_part, cos_part], axis=1)
    return jnp.concatenate([upper, lower], axis=0)


def fourier_tables(length):
    inner = min(128, length)
    outer = 2 * length // inner
    outer_cos, outer_sin = angle_table(outer // 2, outer, outer)
    twist_cos, twist_sin = angle_table(outer, inner, 2 * length)
    inner_cos, inner_sin = angle_table(inner, inner, inner)
    fwd_outer = rotation_table(outer_cos, outer_sin)
    fwd_inner = rotation_table(inner_cos, inner_sin)
    inv_inner = rotation_table(inner_cos, -inner_sin)
    inv_outer = rotation_table(outer_cos.T, -outer_sin.T)
    return (fwd_outer, fwd_inner, inv_inner, inv_outer, twist_cos, twist_sin)


def forward_spectrum(real_rows, imag_rows, tables):
    fwd_outer, fwd_inner, inv_inner, inv_outer, twist_cos, twist_sin = tables
    row_count = real_rows.shape[0]
    outer = twist_cos.shape[0]
    inner = twist_cos.shape[1]
    half_outer = outer // 2
    real_blocks = real_rows.reshape(row_count, half_outer, inner)
    if imag_rows is None:
        blocks = real_blocks
        table = fwd_outer[:half_outer]
    else:
        blocks = jnp.concatenate(
            [real_blocks, imag_rows.reshape(row_count, half_outer, inner)], axis=1
        )
        table = fwd_outer
    first = jnp.einsum("man,ak->mkn", blocks, table, precision=triple)
    first_real = first[:, :outer]
    first_imag = first[:, outer:]
    turned = jnp.concatenate(
        [
            first_real * twist_cos + first_imag * twist_sin,
            first_imag * twist_cos - first_real * twist_sin,
        ],
        axis=2,
    )
    return jnp.einsum("mkn,nj->mkj", turned, fwd_inner, precision=highest)


def inverse_spectrum(spectrum, tables, both_parts):
    fwd_outer, fwd_inner, inv_inner, inv_outer, twist_cos, twist_sin = tables
    row_count = spectrum.shape[0]
    outer = twist_cos.shape[0]
    inner = twist_cos.shape[1]
    half_outer = outer // 2
    length = half_outer * inner
    first = jnp.einsum("mkj,jn->mkn", spectrum, inv_inner, precision=highest)
    first_real = first[..., :inner]
    first_imag = first[..., inner:]
    turned = jnp.concatenate(
        [
            first_real * twist_cos - first_imag * twist_sin,
            first_imag * twist_cos + first_real * twist_sin,
        ],
        axis=1,
    )
    table = inv_outer if both_parts else inv_outer[:, :half_outer]
    values = jnp.einsum("mkn,ka->man", turned, table, precision=highest) * (1.0 / (2.0 * length))
    if both_parts:
        return (
            values[:, :half_outer].reshape(row_count, length),
            values[:, half_outer:].reshape(row_count, length),
        )
    return values.reshape(row_count, length)


BLOCK_ROWS = 1024


def front_kernel(chan_dev, q_ref, k_ref, v_ref, g_ref, halo_ref, taps_ref, qc_ref, kc_ref, vc_ref, out_ref):
    rows, cols = q_ref.shape
    lane = lax.broadcasted_iota(jnp.int32, (rows, cols), 1)
    halo = halo_ref[...].astype(jnp.float32)
    taps = taps_ref[...]
    first, second, third = taps[:, 0:1], taps[:, 1:2], taps[:, 2:3]

    def conv(x_ref, slot):
        x = x_ref[...].astype(jnp.float32)
        older = halo[:, 2 * slot : 2 * slot + 1]
        newer = halo[:, 2 * slot + 1 : 2 * slot + 2]
        back_one = jnp.where(lane == 0, newer, pltpu.roll(x, 1, 1))
        rolled = pltpu.roll(x, 2, 1)
        back_two = jnp.where(lane == 0, older, jnp.where(lane == 1, newer, rolled))
        return (first * x + second * back_one + third * back_two).astype(jnp.bfloat16)

    qc = conv(q_ref, 0)
    kc = conv(k_ref, 1)
    vc = conv(v_ref, 2)
    qc_ref[...] = qc
    kc_ref[...] = kc
    vc_ref[...] = vc
    gated = (kc.astype(jnp.float32) * vc.astype(jnp.float32)).astype(jnp.bfloat16)
    grad_mixed = (g_ref[...].astype(jnp.float32) * qc.astype(jnp.float32)).astype(jnp.bfloat16)
    for j in range(rows // chan_dev):
        out_ref[2 * j * chan_dev : (2 * j + 1) * chan_dev, :] = gated[j * chan_dev : (j + 1) * chan_dev]
        out_ref[(2 * j + 1) * chan_dev : (2 * j + 2) * chan_dev, :] = grad_mixed[
            j * chan_dev : (j + 1) * chan_dev
        ]


def front(query_proj, key_proj, value_proj, grad_out, halo, taps_cols, chan_dev):
    all_chans, tok_cols = query_proj.shape
    block = min(BLOCK_ROWS, all_chans)
    tile = pl.BlockSpec((block, tok_cols), lambda i: (i, 0))
    return pl.pallas_call(
        functools.partial(front_kernel, chan_dev),
        grid=(all_chans // block,),
        in_specs=[tile, tile, tile, tile, pl.BlockSpec((block, 6), lambda i: (i, 0)),
                  pl.BlockSpec((block, 3), lambda i: (i, 0))],
        out_specs=[tile, tile, tile, pl.BlockSpec((2 * block, tok_cols), lambda i: (i, 0))],
        out_shape=[jax.ShapeDtypeStruct((all_chans, tok_cols), jnp.bfloat16)] * 3
        + [jax.ShapeDtypeStruct((2 * all_chans, tok_cols), jnp.bfloat16)],
        cost_estimate=pl.CostEstimate(flops=30 * all_chans * tok_cols, transcendentals=0,
                                      bytes_accessed=18 * all_chans * tok_cols),
    )(query_proj, key_proj, value_proj, grad_out, halo, taps_cols)


def taps_forward(current, earlier, short_taps):
    columns = current.shape[1]
    joined = jnp.concatenate([earlier, current], axis=1)
    return (
        short_taps[0][:, None] * current
        + short_taps[1][:, None] * joined[:, 1 : columns + 1]
        + short_taps[2][:, None] * joined[:, 0:columns]
    )


def taps_backward(current, following, short_taps):
    columns = current.shape[1]
    joined = jnp.concatenate([current, following], axis=1)
    return (
        short_taps[0][:, None] * current
        + short_taps[1][:, None] * joined[:, 1 : columns + 1]
        + short_taps[2][:, None] * joined[:, 2 : columns + 2]
    )


def per_device(query_proj, key_proj, value_proj, grad_out, filters, short_taps):
    all_chans, tok_cols = query_proj.shape
    ctx_count = lax.axis_size("ctx")
    seq_len = tok_cols * ctx_count
    seq_count = ctx_count * tok_cols // seq_len
    groups_dev = filters.shape[0]
    chan_dev = all_chans // ctx_count
    group_size = chan_dev // groups_dev
    group_rows = group_size * seq_count
    pair_rows = group_rows // 2
    position = lax.axis_index("ctx") * tok_cols
    keep_prev = jnp.where(position % seq_len == 0, 0.0, 1.0).astype(jnp.float32)
    keep_next = jnp.where((position + tok_cols) % seq_len == 0, 0.0, 1.0).astype(jnp.float32)
    tables = fourier_tables(seq_len)
    inner = tables[4].shape[1]
    tails = jnp.concatenate([query_proj[:, -2:], key_proj[:, -2:], value_proj[:, -2:]], axis=1)
    tails = jnp.where(keep_next > 0, tails, jnp.zeros_like(tails))
    halo = shifted(tails, "ctx", 1)
    query_conv, key_conv, value_conv, outgoing = front(
        query_proj, key_proj, value_proj, grad_out, halo, short_taps.T, chan_dev
    )
    filter_spec = forward_spectrum(filters.astype(jnp.float32), None, tables)
    filter_real = filter_spec[:, None, :, :inner]
    filter_imag = filter_spec[:, None, :, inner:]

    def to_rows(source):
        return source.reshape(groups_dev, group_rows, seq_len)

    def to_chan(source):
        return source.reshape(chan_dev, ctx_count * tok_cols)

    def spectrum_of(rows_three):
        paired = rows_three.reshape(groups_dev, 2, pair_rows, seq_len).astype(jnp.float32)
        spec = forward_spectrum(
            paired[:, 0].reshape(-1, seq_len), paired[:, 1].reshape(-1, seq_len), tables
        )
        spec = spec.reshape((groups_dev, pair_rows) + spec.shape[1:])
        return (spec[..., :inner], spec[..., inner:])

    def back_to_rows(spec_real, spec_imag):
        joined = jnp.concatenate([spec_real, spec_imag], axis=-1)
        joined = joined.reshape((-1,) + joined.shape[2:])
        first_rows, second_rows = inverse_spectrum(joined, tables, True)
        first_rows = first_rows.reshape(groups_dev, pair_rows, seq_len)
        second_rows = second_rows.reshape(groups_dev, pair_rows, seq_len)
        return jnp.concatenate([first_rows, second_rows], axis=1)

    cotangent = grad_out.astype(jnp.float32)
    incoming = lax.all_to_all(outgoing, "ctx", split_axis=0, concat_axis=1, tiled=True)
    gated_rows = to_rows(incoming[:chan_dev])
    grad_mixed = to_rows(incoming[chan_dev:])
    gated_spec = spectrum_of(gated_rows)
    prod_real = gated_spec[0] * filter_real - gated_spec[1] * filter_imag
    prod_imag = gated_spec[0] * filter_imag + gated_spec[1] * filter_real
    mixed_rows = back_to_rows(prod_real, prod_imag).astype(jnp.bfloat16)
    grad_spec = spectrum_of(grad_mixed)
    prod_real = grad_spec[0] * filter_real + grad_spec[1] * filter_imag
    prod_imag = grad_spec[1] * filter_real - grad_spec[0] * filter_imag
    grad_gated = back_to_rows(prod_real, prod_imag).astype(jnp.bfloat16)
    returning = jnp.concatenate([to_chan(mixed_rows), to_chan(grad_gated)], axis=0)
    returned = lax.all_to_all(returning, "ctx", split_axis=1, concat_axis=0, tiled=True)
    returned = returned.reshape(ctx_count, 2 * chan_dev, tok_cols)
    mixed_tok = returned[:, :chan_dev].reshape(all_chans, tok_cols)
    grad_gated_tok = returned[:, chan_dev:].reshape(all_chans, tok_cols)
    grad_qconv = (cotangent * mixed_tok.astype(jnp.float32)).astype(jnp.bfloat16)
    cross_real = jnp.sum(grad_spec[0] * gated_spec[0] + grad_spec[1] * gated_spec[1], axis=1)
    cross_imag = jnp.sum(grad_spec[1] * gated_spec[0] - grad_spec[0] * gated_spec[1], axis=1)
    filter_terms = inverse_spectrum(
        jnp.concatenate([cross_real, cross_imag], axis=-1), tables, False
    )
    scale = 1.0 / math.sqrt(float(lax.axis_size("dp") * seq_count * group_size * seq_len))
    grad_filters = ring_scatter_sum(filter_terms, "dp") * scale
    grad_kconv = (grad_gated_tok.astype(jnp.float32) * value_conv.astype(jnp.float32)).astype(
        jnp.bfloat16
    )
    grad_vconv = (grad_gated_tok.astype(jnp.float32) * key_conv.astype(jnp.float32)).astype(
        jnp.bfloat16
    )
    grad_qconv, grad_kconv, grad_vconv = lax.optimization_barrier(
        (grad_qconv, grad_kconv, grad_vconv)
    )
    heads = jnp.concatenate([grad_qconv[:, :2], grad_kconv[:, :2], grad_vconv[:, :2]], axis=1)
    heads = jnp.where(keep_prev > 0, heads, jnp.zeros_like(heads))
    heads = shifted(heads, "ctx", -1)
    following = (heads[:, 0:2], heads[:, 2:4], heads[:, 4:6])
    grad_query = taps_backward(
        grad_qconv.astype(jnp.float32), following[0].astype(jnp.float32), short_taps
    ).astype(jnp.bfloat16)
    grad_key = taps_backward(
        grad_kconv.astype(jnp.float32), following[1].astype(jnp.float32), short_taps
    ).astype(jnp.bfloat16)
    grad_value = taps_backward(
        grad_vconv.astype(jnp.float32), following[2].astype(jnp.float32), short_taps
    ).astype(jnp.bfloat16)
    return (grad_query, grad_key, grad_value, grad_filters)


def solution(mesh):
    in_specs = (
        P(None, ("dp", "ctx")),
        P(None, ("dp", "ctx")),
        P(None, ("dp", "ctx")),
        P(None, ("dp", "ctx")),
        P("ctx", None),
        P(),
    )
    out_specs = (
        P(None, ("dp", "ctx")),
        P(None, ("dp", "ctx")),
        P(None, ("dp", "ctx")),
        P("ctx", "dp"),
    )
    return jax.shard_map(
        per_device, mesh=mesh, in_specs=in_specs, out_specs=out_specs, check_vma=False
    )
```

```python
import functools
import math

import jax
import jax.numpy as jnp
from jax import lax
from jax.experimental import pallas as pl
from jax.experimental.pallas import tpu as pltpu
from jax.sharding import PartitionSpec as P

highest = lax.Precision.HIGH
triple = lax.Precision.HIGH


def shifted(array, axis, by):
    size = lax.axis_size(axis)
    pairs = [(i, i + by) for i in range(size) if 0 <= i + by < size]
    return lax.ppermute(array, axis, pairs)


def ring_scatter_sum(terms, axis):
    count = lax.axis_size(axis)
    width = terms.shape[1] // count
    me = lax.axis_index(axis)
    total = lax.dynamic_slice_in_dim(terms, me * width, width, axis=1)
    for step in range(1, count):
        target = (me + step) % count
        piece = lax.dynamic_slice_in_dim(terms, target * width, width, axis=1)
        pairs = [(i, (i + step) % count) for i in range(count)]
        total = total + lax.ppermute(piece, axis, pairs)
    return total


def angle_table(first_count, second_count, modulus):
    first_index = jnp.arange(first_count, dtype=jnp.int32)
    second_index = jnp.arange(second_count, dtype=jnp.int32)
    product = first_index[:, None] * second_index[None, :] % modulus
    angle = product.astype(jnp.float32) * (2.0 * math.pi / modulus)
    return (jnp.cos(angle), jnp.sin(angle))


def rotation_table(cos_part, sin_part):
    upper = jnp.concatenate([cos_part, -sin_part], axis=1)
    lower = jnp.concatenate([sin_part, cos_part], axis=1)
    return jnp.concatenate([upper, lower], axis=0)


def fourier_tables(length):
    inner = min(128, length)
    outer = 2 * length // inner
    outer_cos, outer_sin = angle_table(outer // 2, outer, outer)
    twist_cos, twist_sin = angle_table(outer, inner, 2 * length)
    inner_cos, inner_sin = angle_table(inner, inner, inner)
    fwd_outer = rotation_table(outer_cos, outer_sin)
    fwd_inner = rotation_table(inner_cos, inner_sin)
    inv_inner = rotation_table(inner_cos, -inner_sin)
    inv_outer = rotation_table(outer_cos.T, -outer_sin.T)
    return (fwd_outer, fwd_inner, inv_inner, inv_outer, twist_cos, twist_sin)


def forward_spectrum(real_rows, imag_rows, tables):
    fwd_outer, fwd_inner, inv_inner, inv_outer, twist_cos, twist_sin = tables
    row_count = real_rows.shape[0]
    outer = twist_cos.shape[0]
    inner = twist_cos.shape[1]
    half_outer = outer // 2
    real_blocks = real_rows.reshape(row_count, half_outer, inner)
    if imag_rows is None:
        blocks = real_blocks
        table = fwd_outer[:half_outer]
    else:
        blocks = jnp.concatenate(
            [real_blocks, imag_rows.reshape(row_count, half_outer, inner)], axis=1
        )
        table = fwd_outer
    first = jnp.einsum("man,ak->mkn", blocks, table, precision=triple)
    first_real = first[:, :outer]
    first_imag = first[:, outer:]
    turned = jnp.concatenate(
        [
            first_real * twist_cos + first_imag * twist_sin,
            first_imag * twist_cos - first_real * twist_sin,
        ],
        axis=2,
    )
    return jnp.einsum("mkn,nj->mkj", turned, fwd_inner, precision=highest)


def inverse_spectrum(spectrum, tables, both_parts):
    fwd_outer, fwd_inner, inv_inner, inv_outer, twist_cos, twist_sin = tables
    row_count = spectrum.shape[0]
    outer = twist_cos.shape[0]
    inner = twist_cos.shape[1]
    half_outer = outer // 2
    length = half_outer * inner
    first = jnp.einsum("mkj,jn->mkn", spectrum, inv_inner, precision=highest)
    first_real = first[..., :inner]
    first_imag = first[..., inner:]
    turned = jnp.concatenate(
        [
            first_real * twist_cos - first_imag * twist_sin,
            first_imag * twist_cos + first_real * twist_sin,
        ],
        axis=1,
    )
    table = inv_outer if both_parts else inv_outer[:, :half_outer]
    values = jnp.einsum("mkn,ka->man", turned, table, precision=highest) * (1.0 / (2.0 * length))
    if both_parts:
        return (
            values[:, :half_outer].reshape(row_count, length),
            values[:, half_outer:].reshape(row_count, length),
        )
    return values.reshape(row_count, length)


BLOCK_ROWS = 1024


def front_kernel(chan_dev, q_ref, k_ref, v_ref, g_ref, halo_ref, taps_ref, qc_ref, kc_ref, vc_ref, out_ref):
    rows, cols = q_ref.shape
    lane = lax.broadcasted_iota(jnp.int32, (rows, cols), 1)
    halo = halo_ref[...].astype(jnp.float32)
    taps = taps_ref[...]
    first, second, third = taps[:, 0:1], taps[:, 1:2], taps[:, 2:3]

    def conv(x_ref, slot):
        x = x_ref[...].astype(jnp.float32)
        older = halo[:, 2 * slot : 2 * slot + 1]
        newer = halo[:, 2 * slot + 1 : 2 * slot + 2]
        back_one = jnp.where(lane == 0, newer, pltpu.roll(x, 1, 1))
        rolled = pltpu.roll(x, 2, 1)
        back_two = jnp.where(lane == 0, older, jnp.where(lane == 1, newer, rolled))
        return (first * x + second * back_one + third * back_two).astype(jnp.bfloat16)

    qc = conv(q_ref, 0)
    kc = conv(k_ref, 1)
    vc = conv(v_ref, 2)
    qc_ref[...] = qc
    kc_ref[...] = kc
    vc_ref[...] = vc
    gated = (kc.astype(jnp.float32) * vc.astype(jnp.float32)).astype(jnp.bfloat16)
    grad_mixed = (g_ref[...].astype(jnp.float32) * qc.astype(jnp.float32)).astype(jnp.bfloat16)
    for j in range(rows // chan_dev):
        out_ref[2 * j * chan_dev : (2 * j + 1) * chan_dev, :] = gated[j * chan_dev : (j + 1) * chan_dev]
        out_ref[(2 * j + 1) * chan_dev : (2 * j + 2) * chan_dev, :] = grad_mixed[
            j * chan_dev : (j + 1) * chan_dev
        ]


def front(query_proj, key_proj, value_proj, grad_out, halo, taps_cols, chan_dev):
    all_chans, tok_cols = query_proj.shape
    block = min(BLOCK_ROWS, all_chans)
    tile = pl.BlockSpec((block, tok_cols), lambda i: (i, 0))
    return pl.pallas_call(
        functools.partial(front_kernel, chan_dev),
        grid=(all_chans // block,),
        in_specs=[tile, tile, tile, tile, pl.BlockSpec((block, 6), lambda i: (i, 0)),
                  pl.BlockSpec((block, 3), lambda i: (i, 0))],
        out_specs=[tile, tile, tile, pl.BlockSpec((2 * block, tok_cols), lambda i: (i, 0))],
        out_shape=[jax.ShapeDtypeStruct((all_chans, tok_cols), jnp.bfloat16)] * 3
        + [jax.ShapeDtypeStruct((2 * all_chans, tok_cols), jnp.bfloat16)],
        cost_estimate=pl.CostEstimate(flops=30 * all_chans * tok_cols, transcendentals=0,
                                      bytes_accessed=18 * all_chans * tok_cols),
    )(query_proj, key_proj, value_proj, grad_out, halo, taps_cols)


def tails_kernel(keep_ref, q_ref, k_ref, v_ref, out_ref):
    cols = q_ref.shape[1]
    keep = keep_ref[0, 0]
    for slot, ref in enumerate((q_ref, k_ref, v_ref)):
        part = ref[:, cols - 2 : cols].astype(jnp.float32) * keep
        out_ref[:, 2 * slot : 2 * slot + 2] = part.astype(out_ref.dtype)


def tails_of(query_proj, key_proj, value_proj, keep):
    all_chans, tok_cols = query_proj.shape
    block = min(BLOCK_ROWS, all_chans)
    tile = pl.BlockSpec((block, tok_cols), lambda i: (i, 0))
    return pl.pallas_call(
        tails_kernel,
        grid=(all_chans // block,),
        in_specs=[pl.BlockSpec(memory_space=pltpu.SMEM), tile, tile, tile],
        out_specs=pl.BlockSpec((block, 6), lambda i: (i, 0)),
        out_shape=jax.ShapeDtypeStruct((all_chans, 6), query_proj.dtype),
        cost_estimate=pl.CostEstimate(flops=6 * all_chans, transcendentals=0,
                                      bytes_accessed=6 * all_chans * tok_cols),
    )(keep.reshape(1, 1), query_proj, key_proj, value_proj)


def taps_forward(current, earlier, short_taps):
    columns = current.shape[1]
    joined = jnp.concatenate([earlier, current], axis=1)
    return (
        short_taps[0][:, None] * current
        + short_taps[1][:, None] * joined[:, 1 : columns + 1]
        + short_taps[2][:, None] * joined[:, 0:columns]
    )


def taps_backward(current, following, short_taps):
    columns = current.shape[1]
    joined = jnp.concatenate([current, following], axis=1)
    return (
        short_taps[0][:, None] * current
        + short_taps[1][:, None] * joined[:, 1 : columns + 1]
        + short_taps[2][:, None] * joined[:, 2 : columns + 2]
    )


def per_device(query_proj, key_proj, value_proj, grad_out, filters, short_taps):
    all_chans, tok_cols = query_proj.shape
    ctx_count = lax.axis_size("ctx")
    seq_len = tok_cols * ctx_count
    seq_count = ctx_count * tok_cols // seq_len
    groups_dev = filters.shape[0]
    chan_dev = all_chans // ctx_count
    group_size = chan_dev // groups_dev
    group_rows = group_size * seq_count
    pair_rows = group_rows // 2
    position = lax.axis_index("ctx") * tok_cols
    keep_prev = jnp.where(position % seq_len == 0, 0.0, 1.0).astype(jnp.float32)
    keep_next = jnp.where((position + tok_cols) % seq_len == 0, 0.0, 1.0).astype(jnp.float32)
    tables = fourier_tables(seq_len)
    inner = tables[4].shape[1]
    tails = tails_of(query_proj, key_proj, value_proj, keep_next)
    halo = shifted(tails, "ctx", 1)
    query_conv, key_conv, value_conv, outgoing = front(
        query_proj, key_proj, value_proj, grad_out, halo, short_taps.T, chan_dev
    )
    filter_spec = forward_spectrum(filters.astype(jnp.float32), None, tables)
    filter_real = filter_spec[:, None, :, :inner]
    filter_imag = filter_spec[:, None, :, inner:]

    def to_rows(source):
        return source.reshape(groups_dev, group_rows, seq_len)

    def to_chan(source):
        return source.reshape(chan_dev, ctx_count * tok_cols)

    def spectrum_of(rows_three):
        paired = rows_three.reshape(groups_dev, 2, pair_rows, seq_len).astype(jnp.float32)
        spec = forward_spectrum(
            paired[:, 0].reshape(-1, seq_len), paired[:, 1].reshape(-1, seq_len), tables
        )
        spec = spec.reshape((groups_dev, pair_rows) + spec.shape[1:])
        return (spec[..., :inner], spec[..., inner:])

    def back_to_rows(spec_real, spec_imag):
        joined = jnp.concatenate([spec_real, spec_imag], axis=-1)
        joined = joined.reshape((-1,) + joined.shape[2:])
        first_rows, second_rows = inverse_spectrum(joined, tables, True)
        first_rows = first_rows.reshape(groups_dev, pair_rows, seq_len)
        second_rows = second_rows.reshape(groups_dev, pair_rows, seq_len)
        return jnp.concatenate([first_rows, second_rows], axis=1)

    cotangent = grad_out.astype(jnp.float32)
    incoming = lax.all_to_all(outgoing, "ctx", split_axis=0, concat_axis=1, tiled=True)
    gated_rows = to_rows(incoming[:chan_dev])
    grad_mixed = to_rows(incoming[chan_dev:])
    gated_spec = spectrum_of(gated_rows)
    prod_real = gated_spec[0] * filter_real - gated_spec[1] * filter_imag
    prod_imag = gated_spec[0] * filter_imag + gated_spec[1] * filter_real
    mixed_rows = back_to_rows(prod_real, prod_imag).astype(jnp.bfloat16)
    grad_spec = spectrum_of(grad_mixed)
    prod_real = grad_spec[0] * filter_real + grad_spec[1] * filter_imag
    prod_imag = grad_spec[1] * filter_real - grad_spec[0] * filter_imag
    grad_gated = back_to_rows(prod_real, prod_imag).astype(jnp.bfloat16)
    returning = jnp.concatenate([to_chan(mixed_rows), to_chan(grad_gated)], axis=0)
    returned = lax.all_to_all(returning, "ctx", split_axis=1, concat_axis=0, tiled=True)
    returned = returned.reshape(ctx_count, 2 * chan_dev, tok_cols)
    mixed_tok = returned[:, :chan_dev].reshape(all_chans, tok_cols)
    grad_gated_tok = returned[:, chan_dev:].reshape(all_chans, tok_cols)
    grad_qconv = (cotangent * mixed_tok.astype(jnp.float32)).astype(jnp.bfloat16)
    cross_real = jnp.sum(grad_spec[0] * gated_spec[0] + grad_spec[1] * gated_spec[1], axis=1)
    cross_imag = jnp.sum(grad_spec[1] * gated_spec[0] - grad_spec[0] * gated_spec[1], axis=1)
    filter_terms = inverse_spectrum(
        jnp.concatenate([cross_real, cross_imag], axis=-1), tables, False
    )
    scale = 1.0 / math.sqrt(float(lax.axis_size("dp") * seq_count * group_size * seq_len))
    grad_filters = ring_scatter_sum(filter_terms, "dp") * scale
    grad_kconv = (grad_gated_tok.astype(jnp.float32) * value_conv.astype(jnp.float32)).astype(
        jnp.bfloat16
    )
    grad_vconv = (grad_gated_tok.astype(jnp.float32) * key_conv.astype(jnp.float32)).astype(
        jnp.bfloat16
    )
    grad_qconv, grad_kconv, grad_vconv = lax.optimization_barrier(
        (grad_qconv, grad_kconv, grad_vconv)
    )
    heads = jnp.concatenate([grad_qconv[:, :2], grad_kconv[:, :2], grad_vconv[:, :2]], axis=1)
    heads = jnp.where(keep_prev > 0, heads, jnp.zeros_like(heads))
    heads = shifted(heads, "ctx", -1)
    following = (heads[:, 0:2], heads[:, 2:4], heads[:, 4:6])
    grad_query = taps_backward(
        grad_qconv.astype(jnp.float32), following[0].astype(jnp.float32), short_taps
    ).astype(jnp.bfloat16)
    grad_key = taps_backward(
        grad_kconv.astype(jnp.float32), following[1].astype(jnp.float32), short_taps
    ).astype(jnp.bfloat16)
    grad_value = taps_backward(
        grad_vconv.astype(jnp.float32), following[2].astype(jnp.float32), short_taps
    ).astype(jnp.bfloat16)
    return (grad_query, grad_key, grad_value, grad_filters)


def solution(mesh):
    in_specs = (
        P(None, ("dp", "ctx")),
        P(None, ("dp", "ctx")),
        P(None, ("dp", "ctx")),
        P(None, ("dp", "ctx")),
        P("ctx", None),
        P(),
    )
    out_specs = (
        P(None, ("dp", "ctx")),
        P(None, ("dp", "ctx")),
        P(None, ("dp", "ctx")),
        P("ctx", "dp"),
    )
    return jax.shard_map(
        per_device, mesh=mesh, in_specs=in_specs, out_specs=out_specs, check_vma=False
    )
```

```python
import functools
import math

import jax
import jax.numpy as jnp
from jax import lax
from jax.experimental import pallas as pl
from jax.experimental.pallas import tpu as pltpu
from jax.sharding import PartitionSpec as P

highest = lax.Precision.HIGH
triple = lax.Precision.HIGH


def shifted(array, axis, by):
    size = lax.axis_size(axis)
    pairs = [(i, i + by) for i in range(size) if 0 <= i + by < size]
    return lax.ppermute(array, axis, pairs)


def ring_scatter_sum(terms, axis):
    count = lax.axis_size(axis)
    width = terms.shape[1] // count
    me = lax.axis_index(axis)
    total = lax.dynamic_slice_in_dim(terms, me * width, width, axis=1)
    for step in range(1, count):
        target = (me + step) % count
        piece = lax.dynamic_slice_in_dim(terms, target * width, width, axis=1)
        pairs = [(i, (i + step) % count) for i in range(count)]
        total = total + lax.ppermute(piece, axis, pairs)
    return total


def angle_table(first_count, second_count, modulus):
    first_index = jnp.arange(first_count, dtype=jnp.int32)
    second_index = jnp.arange(second_count, dtype=jnp.int32)
    product = first_index[:, None] * second_index[None, :] % modulus
    angle = product.astype(jnp.float32) * (2.0 * math.pi / modulus)
    return (jnp.cos(angle), jnp.sin(angle))


def rotation_table(cos_part, sin_part):
    upper = jnp.concatenate([cos_part, -sin_part], axis=1)
    lower = jnp.concatenate([sin_part, cos_part], axis=1)
    return jnp.concatenate([upper, lower], axis=0)


def fourier_tables(length):
    inner = min(128, length)
    outer = 2 * length // inner
    outer_cos, outer_sin = angle_table(outer // 2, outer, outer)
    twist_cos, twist_sin = angle_table(outer, inner, 2 * length)
    inner_cos, inner_sin = angle_table(inner, inner, inner)
    fwd_outer = rotation_table(outer_cos, outer_sin)
    fwd_inner = rotation_table(inner_cos, inner_sin)
    inv_inner = rotation_table(inner_cos, -inner_sin)
    inv_outer = rotation_table(outer_cos.T, -outer_sin.T)
    return (fwd_outer, fwd_inner, inv_inner, inv_outer, twist_cos, twist_sin)


def forward_spectrum(real_rows, imag_rows, tables):
    fwd_outer, fwd_inner, inv_inner, inv_outer, twist_cos, twist_sin = tables
    row_count = real_rows.shape[0]
    outer = twist_cos.shape[0]
    inner = twist_cos.shape[1]
    half_outer = outer // 2
    real_blocks = real_rows.reshape(row_count, half_outer, inner)
    if imag_rows is None:
        blocks = real_blocks
        table = fwd_outer[:half_outer]
    else:
        blocks = jnp.concatenate(
            [real_blocks, imag_rows.reshape(row_count, half_outer, inner)], axis=1
        )
        table = fwd_outer
    if blocks.dtype == jnp.bfloat16:
        table_hi = table.astype(jnp.bfloat16)
        table_lo = (table - table_hi.astype(jnp.float32)).astype(jnp.bfloat16)
        first = jnp.einsum(
            "man,ak->mkn", blocks, table_hi, preferred_element_type=jnp.float32
        ) + jnp.einsum("man,ak->mkn", blocks, table_lo, preferred_element_type=jnp.float32)
    else:
        first = jnp.einsum("man,ak->mkn", blocks, table, precision=triple)
    first_real = first[:, :outer]
    first_imag = first[:, outer:]
    turned = jnp.concatenate(
        [
            first_real * twist_cos + first_imag * twist_sin,
            first_imag * twist_cos - first_real * twist_sin,
        ],
        axis=2,
    )
    return jnp.einsum("mkn,nj->mkj", turned, fwd_inner, precision=highest)


def inverse_spectrum(spectrum, tables, both_parts):
    fwd_outer, fwd_inner, inv_inner, inv_outer, twist_cos, twist_sin = tables
    row_count = spectrum.shape[0]
    outer = twist_cos.shape[0]
    inner = twist_cos.shape[1]
    half_outer = outer // 2
    length = half_outer * inner
    first = jnp.einsum("mkj,jn->mkn", spectrum, inv_inner, precision=highest)
    first_real = first[..., :inner]
    first_imag = first[..., inner:]
    turned = jnp.concatenate(
        [
            first_real * twist_cos - first_imag * twist_sin,
            first_imag * twist_cos + first_real * twist_sin,
        ],
        axis=1,
    )
    table = inv_outer if both_parts else inv_outer[:, :half_outer]
    values = jnp.einsum("mkn,ka->man", turned, table, precision=highest) * (1.0 / (2.0 * length))
    if both_parts:
        return (
            values[:, :half_outer].reshape(row_count, length),
            values[:, half_outer:].reshape(row_count, length),
        )
    return values.reshape(row_count, length)


BLOCK_ROWS = 1024


def front_kernel(chan_dev, q_ref, k_ref, v_ref, g_ref, halo_ref, taps_ref, qc_ref, kc_ref, vc_ref, out_ref):
    rows, cols = q_ref.shape
    lane = lax.broadcasted_iota(jnp.int32, (rows, cols), 1)
    halo = halo_ref[...].astype(jnp.float32)
    taps = taps_ref[...]
    first, second, third = taps[:, 0:1], taps[:, 1:2], taps[:, 2:3]

    def conv(x_ref, slot):
        x = x_ref[...].astype(jnp.float32)
        older = halo[:, 2 * slot : 2 * slot + 1]
        newer = halo[:, 2 * slot + 1 : 2 * slot + 2]
        back_one = jnp.where(lane == 0, newer, pltpu.roll(x, 1, 1))
        rolled = pltpu.roll(x, 2, 1)
        back_two = jnp.where(lane == 0, older, jnp.where(lane == 1, newer, rolled))
        return (first * x + second * back_one + third * back_two).astype(jnp.bfloat16)

    qc = conv(q_ref, 0)
    kc = conv(k_ref, 1)
    vc = conv(v_ref, 2)
    qc_ref[...] = qc
    kc_ref[...] = kc
    vc_ref[...] = vc
    gated = (kc.astype(jnp.float32) * vc.astype(jnp.float32)).astype(jnp.bfloat16)
    grad_mixed = (g_ref[...].astype(jnp.float32) * qc.astype(jnp.float32)).astype(jnp.bfloat16)
    for j in range(rows // chan_dev):
        out_ref[2 * j * chan_dev : (2 * j + 1) * chan_dev, :] = gated[j * chan_dev : (j + 1) * chan_dev]
        out_ref[(2 * j + 1) * chan_dev : (2 * j + 2) * chan_dev, :] = grad_mixed[
            j * chan_dev : (j + 1) * chan_dev
        ]


def front(query_proj, key_proj, value_proj, grad_out, halo, taps_cols, chan_dev):
    all_chans, tok_cols = query_proj.shape
    block = min(BLOCK_ROWS, all_chans)
    tile = pl.BlockSpec((block, tok_cols), lambda i: (i, 0))
    return pl.pallas_call(
        functools.partial(front_kernel, chan_dev),
        grid=(all_chans // block,),
        in_specs=[tile, tile, tile, tile, pl.BlockSpec((block, 6), lambda i: (i, 0)),
                  pl.BlockSpec((block, 3), lambda i: (i, 0))],
        out_specs=[tile, tile, tile, pl.BlockSpec((2 * block, tok_cols), lambda i: (i, 0))],
        out_shape=[jax.ShapeDtypeStruct((all_chans, tok_cols), jnp.bfloat16)] * 3
        + [jax.ShapeDtypeStruct((2 * all_chans, tok_cols), jnp.bfloat16)],
        cost_estimate=pl.CostEstimate(flops=30 * all_chans * tok_cols, transcendentals=0,
                                      bytes_accessed=18 * all_chans * tok_cols),
    )(query_proj, key_proj, value_proj, grad_out, halo, taps_cols)


def taps_forward(current, earlier, short_taps):
    columns = current.shape[1]
    joined = jnp.concatenate([earlier, current], axis=1)
    return (
        short_taps[0][:, None] * current
        + short_taps[1][:, None] * joined[:, 1 : columns + 1]
        + short_taps[2][:, None] * joined[:, 0:columns]
    )


def taps_backward(current, following, short_taps):
    columns = current.shape[1]
    joined = jnp.concatenate([current, following], axis=1)
    return (
        short_taps[0][:, None] * current
        + short_taps[1][:, None] * joined[:, 1 : columns + 1]
        + short_taps[2][:, None] * joined[:, 2 : columns + 2]
    )


def per_device(query_proj, key_proj, value_proj, grad_out, filters, short_taps):
    all_chans, tok_cols = query_proj.shape
    ctx_count = lax.axis_size("ctx")
    seq_len = tok_cols * ctx_count
    seq_count = ctx_count * tok_cols // seq_len
    groups_dev = filters.shape[0]
    chan_dev = all_chans // ctx_count
    group_size = chan_dev // groups_dev
    group_rows = group_size * seq_count
    pair_rows = group_rows // 2
    position = lax.axis_index("ctx") * tok_cols
    keep_prev = jnp.where(position % seq_len == 0, 0.0, 1.0).astype(jnp.float32)
    keep_next = jnp.where((position + tok_cols) % seq_len == 0, 0.0, 1.0).astype(jnp.float32)
    tables = fourier_tables(seq_len)
    inner = tables[4].shape[1]
    tails = jnp.concatenate([query_proj[:, -2:], key_proj[:, -2:], value_proj[:, -2:]], axis=1)
    tails = shifted(tails, "ctx", 1)
    halo = jnp.where(keep_prev > 0, tails, jnp.zeros_like(tails))
    query_conv, key_conv, value_conv, outgoing = front(
        query_proj, key_proj, value_proj, grad_out, halo, short_taps.T, chan_dev
    )
    filter_spec = forward_spectrum(filters, None, tables)
    filter_real = filter_spec[:, None, :, :inner]
    filter_imag = filter_spec[:, None, :, inner:]

    def to_rows(source):
        return source.reshape(groups_dev, group_rows, seq_len)

    def to_chan(source):
        return source.reshape(chan_dev, ctx_count * tok_cols)

    def spectrum_of(rows_three):
        paired = rows_three.reshape(groups_dev, 2, pair_rows, seq_len)
        spec = forward_spectrum(
            paired[:, 0].reshape(-1, seq_len), paired[:, 1].reshape(-1, seq_len), tables
        )
        spec = spec.reshape((groups_dev, pair_rows) + spec.shape[1:])
        return (spec[..., :inner], spec[..., inner:])

    def back_to_rows(spec_real, spec_imag):
        joined = jnp.concatenate([spec_real, spec_imag], axis=-1)
        joined = joined.reshape((-1,) + joined.shape[2:])
        first_rows, second_rows = inverse_spectrum(joined, tables, True)
        first_rows = first_rows.reshape(groups_dev, pair_rows, seq_len)
        second_rows = second_rows.reshape(groups_dev, pair_rows, seq_len)
        return jnp.concatenate([first_rows, second_rows], axis=1)

    cotangent = grad_out.astype(jnp.float32)
    incoming = lax.all_to_all(outgoing, "ctx", split_axis=0, concat_axis=1, tiled=True)
    gated_rows = to_rows(incoming[:chan_dev])
    grad_mixed = to_rows(incoming[chan_dev:])
    gated_spec = spectrum_of(gated_rows)
    prod_real = gated_spec[0] * filter_real - gated_spec[1] * filter_imag
    prod_imag = gated_spec[0] * filter_imag + gated_spec[1] * filter_real
    mixed_rows = back_to_rows(prod_real, prod_imag).astype(jnp.bfloat16)
    grad_spec = spectrum_of(grad_mixed)
    prod_real = grad_spec[0] * filter_real + grad_spec[1] * filter_imag
    prod_imag = grad_spec[1] * filter_real - grad_spec[0] * filter_imag
    grad_gated = back_to_rows(prod_real, prod_imag).astype(jnp.bfloat16)
    returning = jnp.concatenate([to_chan(mixed_rows), to_chan(grad_gated)], axis=0)
    returned = lax.all_to_all(returning, "ctx", split_axis=1, concat_axis=0, tiled=True)
    returned = returned.reshape(ctx_count, 2 * chan_dev, tok_cols)
    mixed_tok = returned[:, :chan_dev].reshape(all_chans, tok_cols)
    grad_gated_tok = returned[:, chan_dev:].reshape(all_chans, tok_cols)
    grad_qconv = (cotangent * mixed_tok.astype(jnp.float32)).astype(jnp.bfloat16)
    cross_real = jnp.sum(grad_spec[0] * gated_spec[0] + grad_spec[1] * gated_spec[1], axis=1)
    cross_imag = jnp.sum(grad_spec[1] * gated_spec[0] - grad_spec[0] * gated_spec[1], axis=1)
    filter_terms = inverse_spectrum(
        jnp.concatenate([cross_real, cross_imag], axis=-1), tables, False
    )
    scale = 1.0 / math.sqrt(float(lax.axis_size("dp") * seq_count * group_size * seq_len))
    grad_filters = ring_scatter_sum(filter_terms, "dp") * scale
    grad_kconv = (grad_gated_tok.astype(jnp.float32) * value_conv.astype(jnp.float32)).astype(
        jnp.bfloat16
    )
    grad_vconv = (grad_gated_tok.astype(jnp.float32) * key_conv.astype(jnp.float32)).astype(
        jnp.bfloat16
    )
    grad_qconv, grad_kconv, grad_vconv = lax.optimization_barrier(
        (grad_qconv, grad_kconv, grad_vconv)
    )
    heads = jnp.concatenate([grad_qconv[:, :2], grad_kconv[:, :2], grad_vconv[:, :2]], axis=1)
    heads = shifted(heads, "ctx", -1)
    following = (heads[:, 0:2], heads[:, 2:4], heads[:, 4:6])
    grad_query = taps_backward(
        grad_qconv.astype(jnp.float32), following[0].astype(jnp.float32) * keep_next, short_taps
    ).astype(jnp.bfloat16)
    grad_key = taps_backward(
        grad_kconv.astype(jnp.float32), following[1].astype(jnp.float32) * keep_next, short_taps
    ).astype(jnp.bfloat16)
    grad_value = taps_backward(
        grad_vconv.astype(jnp.float32), following[2].astype(jnp.float32) * keep_next, short_taps
    ).astype(jnp.bfloat16)
    return (grad_query, grad_key, grad_value, grad_filters)


def solution(mesh):
    in_specs = (
        P(None, ("dp", "ctx")),
        P(None, ("dp", "ctx")),
        P(None, ("dp", "ctx")),
        P(None, ("dp", "ctx")),
        P("ctx", None),
        P(),
    )
    out_specs = (
        P(None, ("dp", "ctx")),
        P(None, ("dp", "ctx")),
        P(None, ("dp", "ctx")),
        P("ctx", "dp"),
    )
    return jax.shard_map(
        per_device, mesh=mesh, in_specs=in_specs, out_specs=out_specs, check_vma=False
    )
```

```python
import functools
import math

import jax
import jax.numpy as jnp
from jax import lax
from jax.experimental import pallas as pl
from jax.experimental.pallas import tpu as pltpu
from jax.sharding import PartitionSpec as P

highest = lax.Precision.HIGH
triple = lax.Precision.HIGH


def shifted(array, axis, by):
    size = lax.axis_size(axis)
    pairs = [(i, i + by) for i in range(size) if 0 <= i + by < size]
    return lax.ppermute(array, axis, pairs)


def ring_scatter_sum(terms, axis):
    count = lax.axis_size(axis)
    width = terms.shape[1] // count
    me = lax.axis_index(axis)
    total = lax.dynamic_slice_in_dim(terms, me * width, width, axis=1)
    for step in range(1, count):
        target = (me + step) % count
        piece = lax.dynamic_slice_in_dim(terms, target * width, width, axis=1)
        pairs = [(i, (i + step) % count) for i in range(count)]
        total = total + lax.ppermute(piece, axis, pairs)
    return total


def angle_table(first_count, second_count, modulus):
    first_index = jnp.arange(first_count, dtype=jnp.int32)
    second_index = jnp.arange(second_count, dtype=jnp.int32)
    product = first_index[:, None] * second_index[None, :] % modulus
    angle = product.astype(jnp.float32) * (2.0 * math.pi / modulus)
    return (jnp.cos(angle), jnp.sin(angle))


def rotation_table(cos_part, sin_part):
    upper = jnp.concatenate([cos_part, -sin_part], axis=1)
    lower = jnp.concatenate([sin_part, cos_part], axis=1)
    return jnp.concatenate([upper, lower], axis=0)


def fourier_tables(length):
    inner = min(128, length)
    outer = 2 * length // inner
    outer_cos, outer_sin = angle_table(outer // 2, outer, outer)
    twist_cos, twist_sin = angle_table(outer, inner, 2 * length)
    inner_cos, inner_sin = angle_table(inner, inner, inner)
    fwd_outer = rotation_table(outer_cos, outer_sin)
    fwd_inner = rotation_table(inner_cos, inner_sin)
    inv_inner = rotation_table(inner_cos, -inner_sin)
    inv_outer = rotation_table(outer_cos.T, -outer_sin.T)
    return (fwd_outer, fwd_inner, inv_inner, inv_outer, twist_cos, twist_sin)


def forward_spectrum(real_rows, imag_rows, tables):
    fwd_outer, fwd_inner, inv_inner, inv_outer, twist_cos, twist_sin = tables
    row_count = real_rows.shape[0]
    outer = twist_cos.shape[0]
    inner = twist_cos.shape[1]
    half_outer = outer // 2
    real_blocks = real_rows.reshape(row_count, half_outer, inner)
    if imag_rows is None:
        blocks = real_blocks
        table = fwd_outer[:half_outer]
    else:
        blocks = jnp.concatenate(
            [real_blocks, imag_rows.reshape(row_count, half_outer, inner)], axis=1
        )
        table = fwd_outer
    first = jnp.einsum("man,ak->mkn", blocks, table, precision=triple)
    first_real = first[:, :outer]
    first_imag = first[:, outer:]
    turned = jnp.concatenate(
        [
            first_real * twist_cos + first_imag * twist_sin,
            first_imag * twist_cos - first_real * twist_sin,
        ],
        axis=2,
    )
    return jnp.einsum("mkn,nj->mkj", turned, fwd_inner, precision=highest)


def inverse_spectrum(spectrum, tables, both_parts):
    fwd_outer, fwd_inner, inv_inner, inv_outer, twist_cos, twist_sin = tables
    row_count = spectrum.shape[0]
    outer = twist_cos.shape[0]
    inner = twist_cos.shape[1]
    half_outer = outer // 2
    length = half_outer * inner
    first = jnp.einsum("mkj,jn->mkn", spectrum, inv_inner, precision=highest)
    first_real = first[..., :inner]
    first_imag = first[..., inner:]
    turned = jnp.concatenate(
        [
            first_real * twist_cos - first_imag * twist_sin,
            first_imag * twist_cos + first_real * twist_sin,
        ],
        axis=1,
    )
    table = inv_outer if both_parts else inv_outer[:, :half_outer]
    values = jnp.einsum("mkn,ka->man", turned, table, precision=highest) * (1.0 / (2.0 * length))
    if both_parts:
        return (
            values[:, :half_outer].reshape(row_count, length),
            values[:, half_outer:].reshape(row_count, length),
        )
    return values.reshape(row_count, length)


BLOCK_ROWS = 1024


def front_kernel(chan_dev, q_ref, k_ref, v_ref, g_ref, halo_ref, taps_ref, qc_ref, kc_ref, vc_ref, out_ref):
    rows, cols = q_ref.shape
    lane = lax.broadcasted_iota(jnp.int32, (rows, cols), 1)
    halo = halo_ref[...].astype(jnp.float32)
    taps = taps_ref[...]
    first, second, third = taps[:, 0:1], taps[:, 1:2], taps[:, 2:3]

    def conv(x_ref, slot):
        x = x_ref[...].astype(jnp.float32)
        older = halo[:, 2 * slot : 2 * slot + 1]
        newer = halo[:, 2 * slot + 1 : 2 * slot + 2]
        back_one = jnp.where(lane == 0, newer, pltpu.roll(x, 1, 1))
        rolled = pltpu.roll(x, 2, 1)
        back_two = jnp.where(lane == 0, older, jnp.where(lane == 1, newer, rolled))
        return (first * x + second * back_one + third * back_two).astype(jnp.bfloat16)

    qc = conv(q_ref, 0)
    kc = conv(k_ref, 1)
    vc = conv(v_ref, 2)
    qc_ref[...] = qc
    kc_ref[...] = kc
    vc_ref[...] = vc
    gated = (kc.astype(jnp.float32) * vc.astype(jnp.float32)).astype(jnp.bfloat16)
    grad_mixed = (g_ref[...].astype(jnp.float32) * qc.astype(jnp.float32)).astype(jnp.bfloat16)
    for j in range(rows // chan_dev):
        out_ref[2 * j * chan_dev : (2 * j + 1) * chan_dev, :] = gated[j * chan_dev : (j + 1) * chan_dev]
        out_ref[(2 * j + 1) * chan_dev : (2 * j + 2) * chan_dev, :] = grad_mixed[
            j * chan_dev : (j + 1) * chan_dev
        ]


def front(query_proj, key_proj, value_proj, grad_out, halo, taps_cols, chan_dev):
    all_chans, tok_cols = query_proj.shape
    block = min(BLOCK_ROWS, all_chans)
    tile = pl.BlockSpec((block, tok_cols), lambda i: (i, 0))
    return pl.pallas_call(
        functools.partial(front_kernel, chan_dev),
        grid=(all_chans // block,),
        in_specs=[tile, tile, tile, tile, pl.BlockSpec((block, 6), lambda i: (i, 0)),
                  pl.BlockSpec((block, 3), lambda i: (i, 0))],
        out_specs=[tile, tile, tile, pl.BlockSpec((2 * block, tok_cols), lambda i: (i, 0))],
        out_shape=[jax.ShapeDtypeStruct((all_chans, tok_cols), jnp.bfloat16)] * 3
        + [jax.ShapeDtypeStruct((2 * all_chans, tok_cols), jnp.bfloat16)],
        cost_estimate=pl.CostEstimate(flops=30 * all_chans * tok_cols, transcendentals=0,
                                      bytes_accessed=18 * all_chans * tok_cols),
    )(query_proj, key_proj, value_proj, grad_out, halo, taps_cols)


def taps_forward(current, earlier, short_taps):
    columns = current.shape[1]
    joined = jnp.concatenate([earlier, current], axis=1)
    return (
        short_taps[0][:, None] * current
        + short_taps[1][:, None] * joined[:, 1 : columns + 1]
        + short_taps[2][:, None] * joined[:, 0:columns]
    )


def taps_backward(current, following, short_taps):
    columns = current.shape[1]
    joined = jnp.concatenate([current, following], axis=1)
    return (
        short_taps[0][:, None] * current
        + short_taps[1][:, None] * joined[:, 1 : columns + 1]
        + short_taps[2][:, None] * joined[:, 2 : columns + 2]
    )


def per_device(query_proj, key_proj, value_proj, grad_out, filters, short_taps):
    all_chans, tok_cols = query_proj.shape
    ctx_count = lax.axis_size("ctx")
    seq_len = tok_cols * ctx_count
    seq_count = ctx_count * tok_cols // seq_len
    groups_dev = filters.shape[0]
    chan_dev = all_chans // ctx_count
    group_size = chan_dev // groups_dev
    group_rows = group_size * seq_count
    pair_rows = group_rows // 2
    position = lax.axis_index("ctx") * tok_cols
    keep_prev = jnp.where(position % seq_len == 0, 0.0, 1.0).astype(jnp.float32)
    keep_next = jnp.where((position + tok_cols) % seq_len == 0, 0.0, 1.0).astype(jnp.float32)
    tables = fourier_tables(seq_len)
    inner = tables[4].shape[1]
    tails = jnp.concatenate([query_proj[:, -2:], key_proj[:, -2:], value_proj[:, -2:]], axis=1)
    tails = shifted(tails, "ctx", 1)
    halo = jnp.where(keep_prev > 0, tails, jnp.zeros_like(tails))
    query_conv, key_conv, value_conv, outgoing = front(
        query_proj, key_proj, value_proj, grad_out, halo, short_taps.T, chan_dev
    )
    filter_spec = forward_spectrum(filters.astype(jnp.float32), None, tables)
    filter_real = filter_spec[:, None, :, :inner]
    filter_imag = filter_spec[:, None, :, inner:]

    def to_rows(source):
        return source.reshape(groups_dev, group_rows, seq_len)

    def to_chan(source):
        return source.reshape(chan_dev, ctx_count * tok_cols)

    def spectrum_of(rows_three):
        paired = rows_three.reshape(groups_dev, 2, pair_rows, seq_len).astype(jnp.float32)
        spec = forward_spectrum(
            paired[:, 0].reshape(-1, seq_len), paired[:, 1].reshape(-1, seq_len), tables
        )
        spec = spec.reshape((groups_dev, pair_rows) + spec.shape[1:])
        return (spec[..., :inner], spec[..., inner:])

    def back_to_rows(spec_real, spec_imag):
        joined = jnp.concatenate([spec_real, spec_imag], axis=-1)
        joined = joined.reshape((-1,) + joined.shape[2:])
        first_rows, second_rows = inverse_spectrum(joined, tables, True)
        first_rows = first_rows.reshape(groups_dev, pair_rows, seq_len)
        second_rows = second_rows.reshape(groups_dev, pair_rows, seq_len)
        return jnp.concatenate([first_rows, second_rows], axis=1)

    cotangent = grad_out.astype(jnp.float32)
    incoming = lax.all_to_all(outgoing, "ctx", split_axis=0, concat_axis=1, tiled=True)
    gated_rows = to_rows(incoming[:chan_dev])
    grad_mixed = to_rows(incoming[chan_dev:])
    gated_spec = spectrum_of(gated_rows)
    prod_real = gated_spec[0] * filter_real - gated_spec[1] * filter_imag
    prod_imag = gated_spec[0] * filter_imag + gated_spec[1] * filter_real
    mixed_rows = back_to_rows(prod_real, prod_imag).astype(jnp.bfloat16)
    grad_spec = spectrum_of(grad_mixed)
    prod_real = grad_spec[0] * filter_real + grad_spec[1] * filter_imag
    prod_imag = grad_spec[1] * filter_real - grad_spec[0] * filter_imag
    grad_gated = back_to_rows(prod_real, prod_imag).astype(jnp.bfloat16)
    returning = jnp.concatenate([to_chan(mixed_rows), to_chan(grad_gated)], axis=0)
    returned = lax.all_to_all(returning, "ctx", split_axis=1, concat_axis=0, tiled=True)
    returned = returned.reshape(ctx_count, 2 * chan_dev, tok_cols)
    mixed_tok = returned[:, :chan_dev].reshape(all_chans, tok_cols)
    grad_gated_tok = returned[:, chan_dev:].reshape(all_chans, tok_cols)
    grad_qconv = (cotangent * mixed_tok.astype(jnp.float32)).astype(jnp.bfloat16)
    cross_real = jnp.sum(grad_spec[0] * gated_spec[0] + grad_spec[1] * gated_spec[1], axis=1)
    cross_imag = jnp.sum(grad_spec[1] * gated_spec[0] - grad_spec[0] * gated_spec[1], axis=1)
    filter_terms = inverse_spectrum(
        jnp.concatenate([cross_real, cross_imag], axis=-1), tables, False
    )
    scale = 1.0 / math.sqrt(float(lax.axis_size("dp") * seq_count * group_size * seq_len))
    grad_filters = ring_scatter_sum(filter_terms, "dp") * scale
    grad_kconv = (grad_gated_tok.astype(jnp.float32) * value_conv.astype(jnp.float32)).astype(
        jnp.bfloat16
    )
    grad_vconv = (grad_gated_tok.astype(jnp.float32) * key_conv.astype(jnp.float32)).astype(
        jnp.bfloat16
    )
    heads = jnp.concatenate([grad_qconv[:, :2], grad_kconv[:, :2], grad_vconv[:, :2]], axis=1)
    heads = shifted(heads, "ctx", -1)
    following = (heads[:, 0:2], heads[:, 2:4], heads[:, 4:6])
    grad_query = taps_backward(
        grad_qconv.astype(jnp.float32), following[0].astype(jnp.float32) * keep_next, short_taps
    ).astype(jnp.bfloat16)
    grad_key = taps_backward(
        grad_kconv.astype(jnp.float32), following[1].astype(jnp.float32) * keep_next, short_taps
    ).astype(jnp.bfloat16)
    grad_value = taps_backward(
        grad_vconv.astype(jnp.float32), following[2].astype(jnp.float32) * keep_next, short_taps
    ).astype(jnp.bfloat16)
    return (grad_query, grad_key, grad_value, grad_filters)


def solution(mesh):
    in_specs = (
        P(None, ("dp", "ctx")),
        P(None, ("dp", "ctx")),
        P(None, ("dp", "ctx")),
        P(None, ("dp", "ctx")),
        P("ctx", None),
        P(),
    )
    out_specs = (
        P(None, ("dp", "ctx")),
        P(None, ("dp", "ctx")),
        P(None, ("dp", "ctx")),
        P("ctx", "dp"),
    )
    return jax.shard_map(
        per_device, mesh=mesh, in_specs=in_specs, out_specs=out_specs, check_vma=False
    )
```

```python
import functools
import math

import jax
import jax.numpy as jnp
from jax import lax
from jax.experimental import pallas as pl
from jax.experimental.pallas import tpu as pltpu
from jax.sharding import PartitionSpec as P

highest = lax.Precision.HIGH
triple = lax.Precision.HIGH


def shifted(array, axis, by):
    size = lax.axis_size(axis)
    pairs = [(i, i + by) for i in range(size) if 0 <= i + by < size]
    return lax.ppermute(array, axis, pairs)


def ring_scatter_sum(terms, axis):
    count = lax.axis_size(axis)
    width = terms.shape[1] // count
    me = lax.axis_index(axis)
    total = lax.dynamic_slice_in_dim(terms, me * width, width, axis=1)
    for step in range(1, count):
        target = (me + step) % count
        piece = lax.dynamic_slice_in_dim(terms, target * width, width, axis=1)
        pairs = [(i, (i + step) % count) for i in range(count)]
        total = total + lax.ppermute(piece, axis, pairs)
    return total


def angle_table(first_count, second_count, modulus):
    first_index = jnp.arange(first_count, dtype=jnp.int32)
    second_index = jnp.arange(second_count, dtype=jnp.int32)
    product = first_index[:, None] * second_index[None, :] % modulus
    angle = product.astype(jnp.float32) * (2.0 * math.pi / modulus)
    return (jnp.cos(angle), jnp.sin(angle))


def rotation_table(cos_part, sin_part):
    upper = jnp.concatenate([cos_part, -sin_part], axis=1)
    lower = jnp.concatenate([sin_part, cos_part], axis=1)
    return jnp.concatenate([upper, lower], axis=0)


def fourier_tables(length):
    inner = min(128, length)
    outer = 2 * length // inner
    outer_cos, outer_sin = angle_table(outer // 2, outer, outer)
    twist_cos, twist_sin = angle_table(outer, inner, 2 * length)
    inner_cos, inner_sin = angle_table(inner, inner, inner)
    fwd_outer = rotation_table(outer_cos, outer_sin)
    fwd_inner = rotation_table(inner_cos, inner_sin)
    inv_inner = rotation_table(inner_cos, -inner_sin)
    inv_outer = rotation_table(outer_cos.T, -outer_sin.T)
    return (fwd_outer, fwd_inner, inv_inner, inv_outer, twist_cos, twist_sin)


def forward_spectrum(real_rows, imag_rows, tables):
    fwd_outer, fwd_inner, inv_inner, inv_outer, twist_cos, twist_sin = tables
    row_count = real_rows.shape[0]
    outer = twist_cos.shape[0]
    inner = twist_cos.shape[1]
    half_outer = outer // 2
    real_blocks = real_rows.reshape(row_count, half_outer, inner)
    if imag_rows is None:
        blocks = real_blocks
        table = fwd_outer[:half_outer]
    else:
        blocks = jnp.concatenate(
            [real_blocks, imag_rows.reshape(row_count, half_outer, inner)], axis=1
        )
        table = fwd_outer
    first = jnp.einsum("man,ak->mkn", blocks, table, precision=triple)
    first_real = first[:, :outer]
    first_imag = first[:, outer:]
    turned = jnp.concatenate(
        [
            first_real * twist_cos + first_imag * twist_sin,
            first_imag * twist_cos - first_real * twist_sin,
        ],
        axis=2,
    )
    return jnp.einsum("mkn,nj->mkj", turned, fwd_inner, precision=highest)


def inverse_spectrum(spectrum, tables, both_parts):
    fwd_outer, fwd_inner, inv_inner, inv_outer, twist_cos, twist_sin = tables
    row_count = spectrum.shape[0]
    outer = twist_cos.shape[0]
    inner = twist_cos.shape[1]
    half_outer = outer // 2
    length = half_outer * inner
    first = jnp.einsum("mkj,jn->mkn", spectrum, inv_inner, precision=highest)
    first_real = first[..., :inner]
    first_imag = first[..., inner:]
    turned = jnp.concatenate(
        [
            first_real * twist_cos - first_imag * twist_sin,
            first_imag * twist_cos + first_real * twist_sin,
        ],
        axis=1,
    )
    table = inv_outer if both_parts else inv_outer[:, :half_outer]
    values = jnp.einsum("mkn,ka->man", turned, table, precision=highest) * (1.0 / (2.0 * length))
    if both_parts:
        return (
            values[:, :half_outer].reshape(row_count, length),
            values[:, half_outer:].reshape(row_count, length),
        )
    return values.reshape(row_count, length)


BLOCK_ROWS = 1024


def front_kernel(chan_dev, keep_ref, q_ref, k_ref, v_ref, g_ref, halo_ref, taps_ref, qc_ref, kc_ref, vc_ref, out_ref):
    rows, cols = q_ref.shape
    lane = lax.broadcasted_iota(jnp.int32, (rows, cols), 1)
    halo = halo_ref[...].astype(jnp.float32) * keep_ref[0, 0]
    taps = taps_ref[...]
    first, second, third = taps[:, 0:1], taps[:, 1:2], taps[:, 2:3]

    def conv(x_ref, slot):
        x = x_ref[...].astype(jnp.float32)
        older = halo[:, 2 * slot : 2 * slot + 1]
        newer = halo[:, 2 * slot + 1 : 2 * slot + 2]
        back_one = jnp.where(lane == 0, newer, pltpu.roll(x, 1, 1))
        rolled = pltpu.roll(x, 2, 1)
        back_two = jnp.where(lane == 0, older, jnp.where(lane == 1, newer, rolled))
        return (first * x + second * back_one + third * back_two).astype(jnp.bfloat16)

    qc = conv(q_ref, 0)
    kc = conv(k_ref, 1)
    vc = conv(v_ref, 2)
    qc_ref[...] = qc
    kc_ref[...] = kc
    vc_ref[...] = vc
    gated = (kc.astype(jnp.float32) * vc.astype(jnp.float32)).astype(jnp.bfloat16)
    grad_mixed = (g_ref[...].astype(jnp.float32) * qc.astype(jnp.float32)).astype(jnp.bfloat16)
    for j in range(rows // chan_dev):
        out_ref[2 * j * chan_dev : (2 * j + 1) * chan_dev, :] = gated[j * chan_dev : (j + 1) * chan_dev]
        out_ref[(2 * j + 1) * chan_dev : (2 * j + 2) * chan_dev, :] = grad_mixed[
            j * chan_dev : (j + 1) * chan_dev
        ]


def front(query_proj, key_proj, value_proj, grad_out, halo, taps_cols, chan_dev, keep):
    all_chans, tok_cols = query_proj.shape
    block = min(BLOCK_ROWS, all_chans)
    tile = pl.BlockSpec((block, tok_cols), lambda i: (i, 0))
    return pl.pallas_call(
        functools.partial(front_kernel, chan_dev),
        grid=(all_chans // block,),
        in_specs=[pl.BlockSpec(memory_space=pltpu.SMEM), tile, tile, tile, tile,
                  pl.BlockSpec((block, 6), lambda i: (i, 0)),
                  pl.BlockSpec((block, 3), lambda i: (i, 0))],
        out_specs=[tile, tile, tile, pl.BlockSpec((2 * block, tok_cols), lambda i: (i, 0))],
        out_shape=[jax.ShapeDtypeStruct((all_chans, tok_cols), jnp.bfloat16)] * 3
        + [jax.ShapeDtypeStruct((2 * all_chans, tok_cols), jnp.bfloat16)],
        cost_estimate=pl.CostEstimate(flops=30 * all_chans * tok_cols, transcendentals=0,
                                      bytes_accessed=18 * all_chans * tok_cols),
    )(keep.reshape(1, 1), query_proj, key_proj, value_proj, grad_out, halo, taps_cols)


def taps_forward(current, earlier, short_taps):
    columns = current.shape[1]
    joined = jnp.concatenate([earlier, current], axis=1)
    return (
        short_taps[0][:, None] * current
        + short_taps[1][:, None] * joined[:, 1 : columns + 1]
        + short_taps[2][:, None] * joined[:, 0:columns]
    )


def taps_backward(current, following, short_taps):
    columns = current.shape[1]
    joined = jnp.concatenate([current, following], axis=1)
    return (
        short_taps[0][:, None] * current
        + short_taps[1][:, None] * joined[:, 1 : columns + 1]
        + short_taps[2][:, None] * joined[:, 2 : columns + 2]
    )


def per_device(query_proj, key_proj, value_proj, grad_out, filters, short_taps):
    all_chans, tok_cols = query_proj.shape
    ctx_count = lax.axis_size("ctx")
    seq_len = tok_cols * ctx_count
    seq_count = ctx_count * tok_cols // seq_len
    groups_dev = filters.shape[0]
    chan_dev = all_chans // ctx_count
    group_size = chan_dev // groups_dev
    group_rows = group_size * seq_count
    pair_rows = group_rows // 2
    position = lax.axis_index("ctx") * tok_cols
    keep_prev = jnp.where(position % seq_len == 0, 0.0, 1.0).astype(jnp.float32)
    keep_next = jnp.where((position + tok_cols) % seq_len == 0, 0.0, 1.0).astype(jnp.float32)
    tables = fourier_tables(seq_len)
    inner = tables[4].shape[1]
    tails = jnp.concatenate([query_proj[:, -2:], key_proj[:, -2:], value_proj[:, -2:]], axis=1)
    tails = shifted(tails, "ctx", 1)
    query_conv, key_conv, value_conv, outgoing = front(
        query_proj, key_proj, value_proj, grad_out, tails, short_taps.T, chan_dev, keep_prev
    )
    filter_spec = forward_spectrum(filters.astype(jnp.float32), None, tables)
    filter_real = filter_spec[:, None, :, :inner]
    filter_imag = filter_spec[:, None, :, inner:]

    def to_rows(source):
        return source.reshape(groups_dev, group_rows, seq_len)

    def to_chan(source):
        return source.reshape(chan_dev, ctx_count * tok_cols)

    def spectrum_of(rows_three):
        paired = rows_three.reshape(groups_dev, 2, pair_rows, seq_len).astype(jnp.float32)
        spec = forward_spectrum(
            paired[:, 0].reshape(-1, seq_len), paired[:, 1].reshape(-1, seq_len), tables
        )
        spec = spec.reshape((groups_dev, pair_rows) + spec.shape[1:])
        return (spec[..., :inner], spec[..., inner:])

    def back_to_rows(spec_real, spec_imag):
        joined = jnp.concatenate([spec_real, spec_imag], axis=-1)
        joined = joined.reshape((-1,) + joined.shape[2:])
        first_rows, second_rows = inverse_spectrum(joined, tables, True)
        first_rows = first_rows.reshape(groups_dev, pair_rows, seq_len)
        second_rows = second_rows.reshape(groups_dev, pair_rows, seq_len)
        return jnp.concatenate([first_rows, second_rows], axis=1)

    cotangent = grad_out.astype(jnp.float32)
    incoming = lax.all_to_all(outgoing, "ctx", split_axis=0, concat_axis=1, tiled=True)
    gated_rows = to_rows(incoming[:chan_dev])
    grad_mixed = to_rows(incoming[chan_dev:])
    gated_spec = spectrum_of(gated_rows)
    prod_real = gated_spec[0] * filter_real - gated_spec[1] * filter_imag
    prod_imag = gated_spec[0] * filter_imag + gated_spec[1] * filter_real
    mixed_rows = back_to_rows(prod_real, prod_imag).astype(jnp.bfloat16)
    grad_spec = spectrum_of(grad_mixed)
    prod_real = grad_spec[0] * filter_real + grad_spec[1] * filter_imag
    prod_imag = grad_spec[1] * filter_real - grad_spec[0] * filter_imag
    grad_gated = back_to_rows(prod_real, prod_imag).astype(jnp.bfloat16)
    returning = jnp.concatenate([to_chan(mixed_rows), to_chan(grad_gated)], axis=0)
    returned = lax.all_to_all(returning, "ctx", split_axis=1, concat_axis=0, tiled=True)
    returned = returned.reshape(ctx_count, 2 * chan_dev, tok_cols)
    mixed_tok = returned[:, :chan_dev].reshape(all_chans, tok_cols)
    grad_gated_tok = returned[:, chan_dev:].reshape(all_chans, tok_cols)
    grad_qconv = (cotangent * mixed_tok.astype(jnp.float32)).astype(jnp.bfloat16)
    cross_real = jnp.sum(grad_spec[0] * gated_spec[0] + grad_spec[1] * gated_spec[1], axis=1)
    cross_imag = jnp.sum(grad_spec[1] * gated_spec[0] - grad_spec[0] * gated_spec[1], axis=1)
    filter_terms = inverse_spectrum(
        jnp.concatenate([cross_real, cross_imag], axis=-1), tables, False
    )
    scale = 1.0 / math.sqrt(float(lax.axis_size("dp") * seq_count * group_size * seq_len))
    grad_filters = ring_scatter_sum(filter_terms, "dp") * scale
    grad_kconv = (grad_gated_tok.astype(jnp.float32) * value_conv.astype(jnp.float32)).astype(
        jnp.bfloat16
    )
    grad_vconv = (grad_gated_tok.astype(jnp.float32) * key_conv.astype(jnp.float32)).astype(
        jnp.bfloat16
    )
    grad_qconv, grad_kconv, grad_vconv = lax.optimization_barrier(
        (grad_qconv, grad_kconv, grad_vconv)
    )
    heads = jnp.concatenate([grad_qconv[:, :2], grad_kconv[:, :2], grad_vconv[:, :2]], axis=1)
    heads = shifted(heads, "ctx", -1)
    following = (heads[:, 0:2], heads[:, 2:4], heads[:, 4:6])
    grad_query = taps_backward(
        grad_qconv.astype(jnp.float32), following[0].astype(jnp.float32) * keep_next, short_taps
    ).astype(jnp.bfloat16)
    grad_key = taps_backward(
        grad_kconv.astype(jnp.float32), following[1].astype(jnp.float32) * keep_next, short_taps
    ).astype(jnp.bfloat16)
    grad_value = taps_backward(
        grad_vconv.astype(jnp.float32), following[2].astype(jnp.float32) * keep_next, short_taps
    ).astype(jnp.bfloat16)
    return (grad_query, grad_key, grad_value, grad_filters)


def solution(mesh):
    in_specs = (
        P(None, ("dp", "ctx")),
        P(None, ("dp", "ctx")),
        P(None, ("dp", "ctx")),
        P(None, ("dp", "ctx")),
        P("ctx", None),
        P(),
    )
    out_specs = (
        P(None, ("dp", "ctx")),
        P(None, ("dp", "ctx")),
        P(None, ("dp", "ctx")),
        P("ctx", "dp"),
    )
    return jax.shard_map(
        per_device, mesh=mesh, in_specs=in_specs, out_specs=out_specs, check_vma=False
    )
```
